512 devices in a mesh: net: 64 (over z, y), tm: 8 (over x, core).
Axes of the slice: x: 4, y: 8, z: 8, core: 2. Of those that a mesh axis runs over, the one named last changes fastest.
Arguments:
- warm_mag: float32 [24, 16, 16384], P('tm', None, 'net'), may hold values from 0.94 to 1.06
- warm_angle: float32 [24, 16, 16384], P('tm', None, 'net'), may hold values from -0.6 to 0.6
- load_real: float32 [24, 16, 16384], P('tm', None, 'net'), may hold values from 0 to 1.2
- load_react: float32 [24, 16, 16384], P('tm', None, 'net'), may hold values from -0.3 to 0.5
- start_real: float32 [24, 16, 2048], P('tm', None, 'net'), may hold values from 0 to 2
- start_react: float32 [24, 16, 2048], P('tm', None, 'net'), may hold values from -3 to 3
- gen_bus: int32 [2048], P('net'), may hold values from 0 to 255
- gen_linear: float32 [2048], P('net'), may hold values from 0.2 to 2
- gen_quad: float32 [2048], P('net'), may hold values from 0.05 to 1
- gen_ramp: float32 [2048], P('net'), may hold values from 0.2 to 5
- gen_cap_real: float32 [2048], P('net'), may hold values from 0.5 to 3
- gen_cap_react: float32 [2048], P('net'), may hold values from 0.1 to 1
- branch_from: int32 [16384], P('net'), may hold values from 0 to 255
- branch_to: int32 [16384], P('net'), may hold values from 0 to 255
- branch_cond: float32 [16384], P('net'), may hold values from 0.2 to 2
- branch_susc: float32 [16384], P('net'), may hold values from -6 to -1.5
- branch_limit: float32 [16384], P('net'), may hold values from 0.5 to 4
- branch_steps: int32 [16384], P('net'), may hold values from 1 to 4
- cut_near: int32 [4096], P('net'), may hold values from 0 to 255
- cut_peer: int32 [4096, 1], P('net'), may hold values from 0 to 63; in each aligned block of 64 rows (0 to 63, 64 to 127, ...) at most 2 rows name the same one
- cut_bus: int32 [4096], P('net'), may hold values from 0 to 255
- cut_cond: float32 [4096], P('net'), may hold values from 0.2 to 2
- cut_susc: float32 [4096], P('net'), may hold values from -6 to -1.5
- cut_limit: float32 [4096], P('net'), may hold values from 0.5 to 4
- cut_steps: int32 [4096], P('net'), may hold values from 1 to 4
Outputs:
- bus_mag: float32 [24, 16, 16384], P('tm', None, 'net')
- bus_angle: float32 [24, 16, 16384], P('tm', None, 'net')
- bus_price: float32 [24, 16, 16384], P('tm', None, 'net')
- gen_real: float32 [24, 16, 2048], P('tm', None, 'net')
- gen_react: float32 [24, 16, 2048], P('tm', None, 'net')
The draws below stay inside these ranges and needn't reach their ends.
Inputs may be any that keep to these rules, and one draw needn't show every extreme that they name: `cut_peer`: among the 64 cut branches of one partition no partition is named more than 2 times, a bound that some block reaches.
All inputs are finite; a program needn't handle non-finite values.
Results may differ from the reference program's by a relative error of at most 0.0003.
Values sent between devices are 32-bit elements; how exact they have to be, the bound alone decides.
No kernel may reach another device: no remote copies, remote signals or barrier semaphores. Data moves between devices by JAX's collectives and lax.ppermute only.
A program may use at most 64 MiB of HBM per device.

```python
import math
import jax
import jax.numpy as jnp
import numpy as np
from jax import lax

B_DEV = 256
SCEN = 16
INNER = 4
ITERS = 2
BR_DEV = 256
CUT_DEV = 64
G_DEV = 32
CAP = 2
NB = 16384
NBR = 16384
NCUT = 4096
NGEN = 2048
HORIZON = 24
N_NET = 64


def plant(result, key, low, largest):
    dims = result.shape
    index_at = [jax.random.randint(jax.random.fold_in(key, axis), (), 0, dims[axis]) for axis in range(len(dims))]
    result = result.at[tuple(index_at)].set(low)
    longest = dims.index(max(dims))
    index_at[longest] = (index_at[longest] + 1) % dims[longest]
    return result.at[tuple(index_at)].set(largest)


def shard_levels(own_key, dims, split, low, high):
    loudness = 1.0
    for position, parts in split:
        draws = jax.random.uniform(jax.random.fold_in(jax.random.fold_in(own_key, 6), position), (parts,), jnp.float32, low / len(split), high / len(split))
        loudness = loudness * jnp.repeat(jnp.exp(draws), dims[position] // parts).reshape((-1,) + (1,) * (len(dims) - 1 - position))
    return loudness


def assign_block(own_key, own, number, rows, number_of, top, limit, slope):
    order = jax.random.permutation(own_key, number_of)
    packed, ordinary = load_shares(number_of, rows * top, limit, slope, True), load_shares(number_of, rows * top, limit, slope, False)
    places = jnp.arange(number_of)

    def named(tallies, offset_by):
        used = int((tallies > 0).sum())
        fixed = max(1, used // 4)
        shifted = fixed + (places - fixed + offset_by * (used - fixed)) % max(1, number_of - fixed)
        return jnp.zeros((number_of,), jnp.int32).at[order[jnp.where(places < fixed, places, shifted)]].set(jnp.asarray(tallies, jnp.int32))

    tallies = jnp.where(number % 4 == 0, named(packed, number // 4), named(ordinary, number - number // 4 - 1))
    mixed = jax.random.permutation(jax.random.fold_in(own, 3), number_of)
    source_of, sink = mixed[0:number_of // 2 * 2:2], mixed[1:number_of // 2 * 2:2]
    slack = jnp.minimum(tallies[source_of] - 1, limit - tallies[sink]) // 2
    slack = jnp.where((source_of == order[0]) | (sink == order[0]) | (tallies[sink] == 0), 0, jnp.maximum(slack, 0))
    shifted = jax.random.randint(jax.random.fold_in(own, 4), (number_of // 2,), 0, 1 << 20) % (slack + 1)
    tallies = tallies.at[source_of].add(-shifted).at[sink].add(shifted)
    members = jnp.searchsorted(jnp.cumsum(tallies), jnp.arange(rows * top), side="right").astype(jnp.int32)
    table = members.reshape(top, rows).T
    table = table[jax.random.permutation(jax.random.fold_in(own, 1), rows)]
    offset_by = jax.random.randint(jax.random.fold_in(own, 2), (rows, 1), 0, top)
    return jnp.take_along_axis(table, (jnp.arange(top)[None, :] + offset_by) % top, axis=1)


def load_shares(number_of, total, reach, lean, full):
    loads = [(1 << 20) // math.isqrt(grade ** lean) + 1 for grade in range(1, number_of + 1)]
    largest = reach if full else min(reach, max(-(-total // number_of), total * loads[0] // sum(loads)))
    least = 1 if total - largest >= number_of - 1 else 0
    given, spare = [largest] + [least] * (number_of - 1), total - largest - least * (number_of - 1)
    while spare > 0:
        movable = [i for i in range(1, number_of) if given[i] < largest] or [i for i in range(1, number_of) if given[i] < reach]
        whole, remaining = sum([loads[i] for i in movable]), spare
        for i in movable:
            more = min(reach - given[i], max(1, remaining * loads[i] // whole), spare)
            given[i] = given[i] + more
            spare = spare - more
    return np.array(given)


def bell_draw(rng, shape, spread, reach, shards=(), kind=jnp.bfloat16):
    result = jax.random.normal(rng, shape, jnp.float32) * spread
    if len(shards) > 0:
        result = shard_levels(rng, shape, shards, -0.22, 0.18) * result
    return jnp.clip(result, min=-reach, max=reach).astype(kind)


def setup_inputs(seed: int = 0) -> dict:
    key_list = jax.random.split(jax.random.key(seed), 26)
    warm_mag = jnp.clip(0.94 + 0.119999945 * jax.random.uniform(key_list[0], (HORIZON, SCEN, NB), jnp.float32) ** shard_levels(key_list[0], (HORIZON, SCEN, NB), ((0, 8), (2, 64)), -0.2, 0.2), 0.94, 1.06)
    warm_angle = bell_draw(key_list[1], (HORIZON, SCEN, NB), 0.15, 0.6, ((0, 8), (2, 64)), jnp.float32)
    load_real = jnp.clip(1.2 * jax.random.uniform(key_list[2], (HORIZON, SCEN, NB), jnp.float32) ** shard_levels(key_list[2], (HORIZON, SCEN, NB), ((0, 8), (2, 64)), -0.2, 0.2), 0.0, 1.2)
    load_react = jnp.clip(-0.3 + 0.8 * jax.random.uniform(key_list[3], (HORIZON, SCEN, NB), jnp.float32) ** shard_levels(key_list[3], (HORIZON, SCEN, NB), ((0, 8), (2, 64)), -0.2, 0.2), -0.3, 0.5)
    start_real = jnp.clip(2.0 * jax.random.uniform(key_list[4], (HORIZON, SCEN, NGEN), jnp.float32) ** shard_levels(key_list[4], (HORIZON, SCEN, NGEN), ((0, 8), (2, 64)), -0.2, 0.2), 0.0, 2.0)
    start_react = bell_draw(key_list[5], (HORIZON, SCEN, NGEN), 0.5, 3.0, ((0, 8), (2, 64)), jnp.float32)
    gen_bus = plant(jax.random.randint(key_list[6], (NGEN,), 0, B_DEV), jax.random.fold_in(key_list[6], 1), 0, B_DEV - 1).astype(jnp.int32)
    gen_linear = jnp.clip(0.2 + 1.8 * jax.random.uniform(key_list[7], (NGEN,), jnp.float32) ** shard_levels(key_list[7], (NGEN,), ((0, 64),), -0.2, 0.2), 0.2, 2.0)
    gen_quad = jnp.clip(jnp.exp(math.log(1.0) - 2.9957323 * jax.random.uniform(key_list[8], (NGEN,), jnp.float32) ** shard_levels(key_list[8], (NGEN,), ((0, 64),), -0.2, 0.2)), 0.05, 1.0)
    gen_ramp = jnp.clip(jnp.exp(math.log(5.0) - 3.218876 * jax.random.uniform(key_list[9], (NGEN,), jnp.float32) ** shard_levels(key_list[9], (NGEN,), ((0, 64),), -0.2, 0.2)), 0.2, 5.0)
    gen_cap_real = jnp.clip(jnp.exp(math.log(3.0) - 1.7917595 * jax.random.uniform(key_list[10], (NGEN,), jnp.float32) ** shard_levels(key_list[10], (NGEN,), ((0, 64),), -0.2, 0.2)), 0.5, 3.0)
    gen_cap_react = jnp.clip(jnp.exp(math.log(1.0) - 2.3025851 * jax.random.uniform(key_list[11], (NGEN,), jnp.float32) ** shard_levels(key_list[11], (NGEN,), ((0, 64),), -0.2, 0.2)), 0.1, 1.0)
    branch_from = plant(jax.random.randint(key_list[12], (NBR,), 0, B_DEV), jax.random.fold_in(key_list[12], 1), 0, B_DEV - 1).astype(jnp.int32)
    branch_to = plant(jax.random.randint(key_list[13], (NBR,), 0, B_DEV), jax.random.fold_in(key_list[13], 1), 0, B_DEV - 1).astype(jnp.int32)
    branch_cond = jnp.clip(jnp.exp(math.log(2.0) - 2.3025851 * jax.random.uniform(key_list[14], (NBR,), jnp.float32) ** shard_levels(key_list[14], (NBR,), ((0, 64),), -0.2, 0.2)), 0.2, 2.0)
    branch_susc = jnp.clip(-6.0 + 4.5 * jax.random.uniform(key_list[15], (NBR,), jnp.float32) ** shard_levels(key_list[15], (NBR,), ((0, 64),), -0.2, 0.2), -6.0, -1.5)
    branch_limit = jnp.clip(jnp.exp(math.log(4.0) - 2.0794415 * jax.random.uniform(key_list[16], (NBR,), jnp.float32) ** shard_levels(key_list[16], (NBR,), ((0, 64),), -0.2, 0.2)), 0.5, 4.0)
    branch_steps = plant(jax.random.randint(key_list[17], (NBR,), 1, INNER + 1), jax.random.fold_in(key_list[17], 1), 1, INNER).astype(jnp.int32)
    cut_near = plant(jax.random.randint(key_list[18], (NCUT,), 0, B_DEV), jax.random.fold_in(key_list[18], 1), 0, B_DEV - 1).astype(jnp.int32)
    cut_peer_keys = jax.random.split(jax.random.fold_in(key_list[19], 1), NCUT // CUT_DEV)
    cut_peer_turns = jax.random.permutation(jax.random.fold_in(key_list[19], 3), NCUT // CUT_DEV)
    cut_peer = jax.vmap(lambda own, number: assign_block(jax.random.fold_in(key_list[19], 2), own, number, CUT_DEV, N_NET, 1, CAP, 2))(cut_peer_keys, cut_peer_turns).reshape((NCUT, 1))
    cut_bus = plant(jax.random.randint(key_list[20], (NCUT,), 0, B_DEV), jax.random.fold_in(key_list[20], 1), 0, B_DEV - 1).astype(jnp.int32)
    cut_cond = jnp.clip(jnp.exp(math.log(2.0) - 2.3025851 * jax.random.uniform(key_list[21], (NCUT,), jnp.float32) ** shard_levels(key_list[21], (NCUT,), ((0, 64),), -0.2, 0.2)), 0.2, 2.0)
    cut_susc = jnp.clip(-6.0 + 4.5 * jax.random.uniform(key_list[22], (NCUT,), jnp.float32) ** shard_levels(key_list[22], (NCUT,), ((0, 64),), -0.2, 0.2), -6.0, -1.5)
    cut_limit = jnp.clip(jnp.exp(math.log(4.0) - 2.0794415 * jax.random.uniform(key_list[23], (NCUT,), jnp.float32) ** shard_levels(key_list[23], (NCUT,), ((0, 64),), -0.2, 0.2)), 0.5, 4.0)
    cut_steps = plant(jax.random.randint(key_list[24], (NCUT,), 1, INNER + 1), jax.random.fold_in(key_list[24], 1), 1, INNER).astype(jnp.int32)
    return dict(warm_mag=warm_mag, warm_angle=warm_angle, load_real=load_real, load_react=load_react, start_real=start_real, start_react=start_react, gen_bus=gen_bus, gen_linear=gen_linear, gen_quad=gen_quad, gen_ramp=gen_ramp, gen_cap_real=gen_cap_real, gen_cap_react=gen_cap_react, branch_from=branch_from, branch_to=branch_to, branch_cond=branch_cond, branch_susc=branch_susc, branch_limit=branch_limit, branch_steps=branch_steps, cut_near=cut_near, cut_peer=cut_peer, cut_bus=cut_bus, cut_cond=cut_cond, cut_susc=cut_susc, cut_limit=cut_limit, cut_steps=cut_steps)


STEP_SIZE = 0.0005
RADIUS = 0.05
BALANCE_WEIGHT = 2.0

def branch_flows(copies, conduct, suscept):
    mag_from = copies[0]
    mag_to = copies[2]
    angle_diff = copies[1] - copies[3]
    cosine = jnp.cos(angle_diff)
    sine_part = jnp.sin(angle_diff)
    product = mag_from * mag_to
    real_from = conduct * mag_from * mag_from - product * (conduct * cosine + suscept * sine_part)
    react_from = -suscept * mag_from * mag_from - product * (conduct * sine_part - suscept * cosine)
    real_to = conduct * mag_to * mag_to - product * (conduct * cosine - suscept * sine_part)
    react_to = -suscept * mag_to * mag_to + product * (conduct * sine_part + suscept * cosine)
    return jnp.stack([real_from, react_from, real_to, react_to])

def branch_energy(copies, target, flow_target, conduct, suscept, ceiling):
    flow_all = branch_flows(copies, conduct, suscept)
    excess_from = jnp.maximum(flow_all[0] * flow_all[0] + flow_all[1] * flow_all[1] - ceiling * ceiling, 0.0)
    excess_to = jnp.maximum(flow_all[2] * flow_all[2] + flow_all[3] * flow_all[3] - ceiling * ceiling, 0.0)
    return 0.5 * jnp.sum((copies - target) * (copies - target)) + 0.5 * jnp.sum((flow_all - flow_target) * (flow_all - flow_target)) + 0.5 * jnp.sum(excess_from * excess_from + excess_to * excess_to)

def branch_solve(copies, target, flow_target, conduct, suscept, ceiling, allowed):
    gradient_fn = jax.grad(branch_energy)
    for attempt in range(INNER):
        gradient = gradient_fn(copies, target, flow_target, conduct, suscept, ceiling)
        motion = jnp.clip(STEP_SIZE * gradient, -RADIUS, RADIUS)
        copies = jnp.where(attempt < allowed, copies - motion, copies)
    return copies

def solve_periods(copies, target, flow_target, conduct, suscept, ceiling, allowed):

    def one_period(items):
        return branch_solve(items[0], items[1], items[2], conduct, suscept, ceiling, allowed)
    moved = lax.map(one_period, (jnp.moveaxis(copies, 1, 0), jnp.moveaxis(target, 1, 0), jnp.moveaxis(flow_target, 1, 0)))
    return jnp.moveaxis(moved, 0, 1)

def accumulate(values, indices, count):
    summed = jax.ops.segment_sum(jnp.moveaxis(values, -1, 0), indices, num_segments=count)
    return jnp.moveaxis(summed, 0, -1)

def contributions(carry):
    copies, dual_volt, dual_flow, flow_prev = carry
    volt = copies + dual_volt
    flow = flow_prev + dual_flow
    return (jnp.stack([volt[0], volt[1], flow[0], flow[1]]), jnp.stack([volt[2], volt[3], flow[2], flow[3]]))

def bus_update(totals, supply, degree, gen_count, warm_mag, warm_angle, load_real, load_react):
    mag = (totals[0] + warm_mag) / (degree + 1.0)
    angle = (totals[1] + warm_angle) / (degree + 1.0)
    weight = 1.0 + BALANCE_WEIGHT * (gen_count + degree)
    price_real = BALANCE_WEIGHT * (supply[0] - totals[2] - load_real) / weight
    price_react = BALANCE_WEIGHT * (supply[1] - totals[3] - load_react) / weight
    return jnp.stack([mag, angle, price_real, price_react])

def reference(warm_mag, warm_angle, load_real, load_react, start_real, start_react, gen_bus, gen_linear, gen_quad, gen_ramp, gen_cap_real, gen_cap_react, branch_from, branch_to, branch_cond, branch_susc, branch_limit, branch_steps, cut_near, cut_peer, cut_bus, cut_cond, cut_susc, cut_limit, cut_steps):
    part_branch = jnp.arange(NBR, dtype=jnp.int32) // BR_DEV
    part_cut = jnp.arange(NCUT, dtype=jnp.int32) // CUT_DEV
    ends_from = jnp.concatenate([part_branch * B_DEV + branch_from, part_cut * B_DEV + cut_near]).astype(jnp.int32)
    ends_to = jnp.concatenate([part_branch * B_DEV + branch_to, cut_peer[:, 0] * B_DEV + cut_bus]).astype(jnp.int32)
    gen_all = (jnp.arange(NGEN, dtype=jnp.int32) // G_DEV * B_DEV + gen_bus).astype(jnp.int32)
    conduct = jnp.concatenate([branch_cond, cut_cond])
    suscept = jnp.concatenate([branch_susc, cut_susc])
    ceiling = jnp.concatenate([branch_limit, cut_limit])
    allowed = jnp.concatenate([branch_steps, cut_steps])
    unity = jnp.ones((NBR + NCUT,), jnp.float32)
    degree = jax.ops.segment_sum(unity, ends_from, num_segments=NB) + jax.ops.segment_sum(unity, ends_to, num_segments=NB)
    gen_count = jax.ops.segment_sum(jnp.ones((NGEN,), jnp.float32), gen_all, num_segments=NB)
    period_ids = jnp.arange(HORIZON, dtype=jnp.int32)
    neighbors = ((period_ids > 0).astype(jnp.float32) + (period_ids < HORIZON - 1).astype(jnp.float32))[:, None, None]
    zeros_bus = jnp.zeros_like(warm_mag)
    state = jnp.stack([warm_mag, warm_angle, zeros_bus, zeros_bus])
    gen_real = start_real
    gen_react = start_react
    dual_real = jnp.zeros_like(start_real)
    dual_react = jnp.zeros_like(start_react)
    carry = None
    for rounds in range(ITERS):
        near_state = jnp.take(state, ends_from, axis=-1)
        far_state = jnp.take(state, ends_to, axis=-1)
        bus_ends = jnp.stack([near_state[0], near_state[1], far_state[0], far_state[1]])
        price_ends = jnp.stack([near_state[2], near_state[3], far_state[2], far_state[3]])
        if carry is None:
            copies = bus_ends
            dual_volt = jnp.zeros_like(bus_ends)
            dual_flow = jnp.zeros_like(bus_ends)
            flow_prev = branch_flows(copies, conduct, suscept)
        else:
            copies, dual_volt, dual_flow, flow_prev = carry
        dual_volt = dual_volt + copies - bus_ends
        flow_target = flow_prev + dual_flow + 2.0 * price_ends
        dual_flow = -price_ends
        copies = solve_periods(copies, bus_ends - dual_volt, flow_target, conduct, suscept, ceiling, allowed)
        flow_prev = branch_flows(copies, conduct, suscept)
        carry = (copies, dual_volt, dual_flow, flow_prev)
        from_side, to_side = contributions(carry)
        totals = accumulate(from_side, ends_from, NB) + accumulate(to_side, ends_to, NB)
        gen_price = jnp.take(state[2:4], gen_all, axis=-1)
        target_real = gen_real + dual_real - 2.0 * gen_price[0]
        target_react = gen_react + dual_react - 2.0 * gen_price[1]
        dual_real = gen_price[0]
        dual_react = gen_price[1]
        padded = jnp.pad(gen_real, ((1, 1), (0, 0), (0, 0)))
        neighbor_sum = padded[:-2] + padded[2:]
        gen_real = jnp.clip((target_real - gen_linear + gen_ramp * neighbor_sum) / (2.0 * gen_quad + 1.0 + gen_ramp * neighbors), 0.0, gen_cap_real)
        gen_react = jnp.clip(target_react, -gen_cap_react, gen_cap_react)
        supply = accumulate(jnp.stack([gen_real + dual_real, gen_react + dual_react]), gen_all, NB)
        state = bus_update(totals, supply, degree, gen_count, warm_mag, warm_angle, load_real, load_react)
    return (state[0], state[1], state[2], gen_real, gen_react)
```

```python
import jax
import jax.numpy as jnp
from jax import lax
from jax.experimental import pallas as pl
from jax.experimental.pallas import tpu as pltpu
from jax.sharding import PartitionSpec as P

INNER = 4
STEP_SIZE = 0.0005
RADIUS = 0.05
BALANCE_WEIGHT = 2.0
HI = lax.Precision.HIGHEST
F32 = jnp.float32


def mm(a, b):
    return lax.dot_general(a, b, (((1,), (0,)), ((), ())), precision=HI, preferred_element_type=F32)


def mm_t(a, b):
    return lax.dot_general(a, b, (((1,), (1,)), ((), ())), precision=HI, preferred_element_type=F32)


def onehot(ids_row, count):
    n = ids_row.shape[1]
    return (lax.broadcasted_iota(jnp.int32, (count, n), 0) == ids_row).astype(F32)


def col_sum(inc):
    return mm_t(jnp.ones((8, inc.shape[1]), F32), inc)[0:1]


def rows(*parts):
    return jnp.concatenate(parts, axis=0)


def flows(x, g, b):
    mf, af, mt, at = x
    d = af - at
    c = jnp.cos(d)
    s = jnp.sin(d)
    p = mf * mt
    return (
        g * mf * mf - p * (g * c + b * s),
        -b * mf * mf - p * (g * s - b * c),
        g * mt * mt - p * (g * c - b * s),
        -b * mt * mt + p * (g * s + b * c),
    )


def energy_grad(x, t, ft, g, b, l2):
    mf, af, mt, at = x
    d = af - at
    c = jnp.cos(d)
    s = jnp.sin(d)
    p = mf * mt
    ka = g * c + b * s
    kb = g * s - b * c
    kc = g * c - b * s
    kd = g * s + b * c
    f0 = g * mf * mf - p * ka
    f1 = -b * mf * mf - p * kb
    f2 = g * mt * mt - p * kc
    f3 = -b * mt * mt + p * kd
    ef = jnp.maximum(f0 * f0 + f1 * f1 - l2, 0.0)
    et = jnp.maximum(f2 * f2 + f3 * f3 - l2, 0.0)
    w0 = (f0 - ft[0]) + 2.0 * ef * f0
    w1 = (f1 - ft[1]) + 2.0 * ef * f1
    w2 = (f2 - ft[2]) + 2.0 * et * f2
    w3 = (f3 - ft[3]) + 2.0 * et * f3
    g_mf = (mf - t[0]) + w0 * (2.0 * g * mf - mt * ka) - w1 * (2.0 * b * mf + mt * kb) - w2 * mt * kc + w3 * mt * kd
    g_mt = (mt - t[2]) - w0 * mf * ka - w1 * mf * kb + w2 * (2.0 * g * mt - mf * kc) - w3 * (2.0 * b * mt - mf * kd)
    g_d = p * (w0 * kb - w1 * ka + w2 * kd + w3 * kc)
    return (g_mf, (af - t[1]) + g_d, g_mt, (at - t[3]) - g_d)


def solve(x, t, ft, g, b, l2, steps):
    for attempt in range(INNER):
        grad = energy_grad(x, t, ft, g, b, l2)
        x = tuple(
            jnp.where(attempt < steps, xi - jnp.clip(STEP_SIZE * gi, -RADIUS, RADIUS), xi)
            for xi, gi in zip(x, grad)
        )
    return x


def advance(carry, near, far, prm):
    g, b, lim, steps = prm
    ends = (near[0], near[1], far[0], far[1])
    prices = (near[2], near[3], far[2], far[3])
    if carry is None:
        copies = ends
        flow_prev = flows(copies, g, b)
        volt = tuple(jnp.zeros_like(e) for e in ends)
        target = ends
        flow_target = flow_prev
        dual_flow = volt
    else:
        copies, flow_prev = carry
        volt = tuple(c - e for c, e in zip(copies, ends))
        target = tuple(e - v for e, v in zip(ends, volt))
        flow_target = tuple(f + 2.0 * q for f, q in zip(flow_prev, prices))
        dual_flow = tuple(-q for q in prices)
    copies = solve(copies, target, flow_target, g, b, lim * lim, steps)
    flow_prev = flows(copies, g, b)
    side_from = rows(
        copies[0] + volt[0], copies[1] + volt[1], flow_prev[0] + dual_flow[0], flow_prev[1] + dual_flow[1]
    )
    side_to = rows(
        copies[2] + volt[2], copies[3] + volt[3], flow_prev[2] + dual_flow[2], flow_prev[3] + dual_flow[3]
    )
    return (copies, flow_prev), side_from, side_to


def split4(a, n):
    return tuple(a[i * n:(i + 1) * n] for i in range(4))


def vmem_call(kernel, outs, *args):
    return pl.pallas_call(
        kernel,
        out_shape=outs,
        in_specs=[pl.BlockSpec(memory_space=pltpu.VMEM)] * len(args),
        out_specs=tuple(pl.BlockSpec(memory_space=pltpu.VMEM) for _ in outs),
        compiler_params=pltpu.CompilerParams(vmem_limit_bytes=48 * 1024 * 1024),
    )(*args)


def slot_table(peer_col, cap, slots):
    cuts = peer_col.shape[0]
    parts = slots // cap
    mine = (peer_col == lax.broadcasted_iota(jnp.int32, (cuts, parts), 1)).astype(F32)
    same = mm_t(mine, mine)
    earlier = lax.broadcasted_iota(jnp.int32, (cuts, cuts), 1) < lax.broadcasted_iota(jnp.int32, (cuts, cuts), 0)
    rank = jnp.sum(jnp.where(earlier, same, 0.0), axis=1, keepdims=True)
    position = peer_col.astype(F32) * cap + rank
    return (position == lax.broadcasted_iota(jnp.int32, (cuts, slots), 1).astype(F32)).astype(F32)


def on_device(
    warm_mag, warm_angle, load_real, load_react, start_real, start_react,
    gen_bus, gen_linear, gen_quad, gen_ramp, gen_cap_real, gen_cap_react,
    branch_from, branch_to, branch_cond, branch_susc, branch_limit, branch_steps,
    cut_near, cut_peer, cut_bus, cut_cond, cut_susc, cut_limit, cut_steps,
):
    periods, scen, buses = warm_mag.shape
    nrow = periods * scen
    cuts = cut_near.shape[0]
    parts = lax.axis_size("net")
    cap = max(2, cuts // parts * 2)
    slots = parts * cap
    gens = gen_bus.shape[0]
    ntm = lax.axis_size("tm")
    horizon = periods * ntm

    def row(v):
        return v.reshape(1, -1)

    wm = warm_mag.reshape(nrow, buses)
    wa = warm_angle.reshape(nrow, buses)
    lr = load_real.reshape(nrow, buses)
    lq = load_react.reshape(nrow, buses)
    sr = start_real.reshape(nrow, gens)
    sq = start_react.reshape(nrow, gens)
    halo = 2 * scen
    lo = lax.ppermute(sr[nrow - halo:], "tm", [(i, i + 1) for i in range(ntm - 1)])
    hi = lax.ppermute(sr[:halo], "tm", [(i + 1, i) for i in range(ntm - 1)])
    window = nrow + 2 * scen
    period_ext = (
        lax.axis_index("tm") * periods - 1 + jnp.arange(window, dtype=jnp.int32) // scen
    ).reshape(window, 1)
    gen_rows = (row(gen_bus), row(gen_linear), row(gen_quad), row(gen_ramp), row(gen_cap_real), row(gen_cap_react))
    br_rows = (row(branch_from), row(branch_to), row(branch_cond), row(branch_susc), row(branch_limit),
               row(branch_steps.astype(F32)))
    cut_rows = (row(cut_near), row(cut_cond), row(cut_susc), row(cut_limit), row(cut_steps.astype(F32)))
    cut_bus_row = row(cut_bus.astype(F32))
    nvals0 = 128

    def prep_kernel(peer_ref, near_ref, bus_ref, cond_ref, susc_ref, lim_ref, steps_ref, wm_ref, wa_ref,
                    slot_out, pay_out):
        slot_t = slot_table(peer_ref[...], cap, slots)
        slot_out[...] = slot_t
        inc_near = onehot(near_ref[...], buses)
        by_slot = mm(inc_near, slot_t)
        prm = rows(bus_ref[...] + 1.0, cond_ref[...], susc_ref[...], lim_ref[...], steps_ref[...],
                   jnp.zeros((3, cuts), F32))
        vals = rows(
            mm(prm, slot_t),
            mm(rows(wm_ref[...], wa_ref[...]), by_slot),
            jnp.zeros((nvals0 - 8 - 2 * nrow, slots), F32),
        )
        pay_out[...] = vals.T

    slot_t, pay_setup = vmem_call(
        prep_kernel,
        (jax.ShapeDtypeStruct((cuts, slots), F32), jax.ShapeDtypeStruct((slots, nvals0), F32)),
        cut_peer, cut_rows[0], cut_bus_row, cut_rows[1], cut_rows[2], cut_rows[3], cut_rows[4], wm, wa,
    )
    recv_setup = lax.all_to_all(pay_setup, "net", 0, 0, tiled=True)

    def mid_kernel(recv_ref, wm_ref, wa_ref, mirror_out, pay_out):
        mirror = recv_ref[...].T
        mirror_out[...] = mirror
        inc_recv = onehot(mirror[0:1].astype(jnp.int32) - 1, buses)
        vals = rows(mm(rows(wm_ref[...], wa_ref[...]), inc_recv), jnp.zeros((nvals0 - 2 * nrow, slots), F32))
        pay_out[...] = vals.T

    mirror_t, pay_0 = vmem_call(
        mid_kernel,
        (jax.ShapeDtypeStruct((nvals0, slots), F32), jax.ShapeDtypeStruct((slots, nvals0), F32)),
        recv_setup, wm, wa,
    )
    recv_0 = lax.all_to_all(pay_0, "net", 0, 0, tiled=True)

    def iteration(first, refs):
        (st_ref, wm_ref, wa_ref, lr_ref, lq_ref, recv_ref, mirror_ref, slot_ref,
         bf_ref, bt_ref, bc_ref, bs_ref, bl_ref, bn_ref,
         cn_ref, cc_ref, cs_ref, cl_ref, cstep_ref,
         gb_ref, gl_ref, gq_ref, gr_ref, gcr_ref, gcq_ref, pe_ref) = refs[:26]
        rest = refs[26:]
        wmv, wav = wm_ref[...], wa_ref[...]
        slot_t = slot_ref[...]
        mirror = mirror_ref[...]
        inc_from = onehot(bf_ref[...], buses)
        inc_to = onehot(bt_ref[...], buses)
        inc_near = onehot(cn_ref[...], buses)
        inc_recv = onehot(mirror[0:1].astype(jnp.int32) - 1, buses)
        inc_gen = onehot(gb_ref[...], buses)
        degree = col_sum(inc_from) + col_sum(inc_to) + col_sum(inc_near) + col_sum(inc_recv)
        gen_count = col_sum(inc_gen)
        zero_b = jnp.zeros((nrow, buses), F32)
        if first:
            state = (wmv, wav, zero_b, zero_b)
            (sr_lo_ref, sr_ref, sr_hi_ref, sq_ref) = rest[:4]
            outs = rest[4:]
            far_slot = recv_ref[...].T
            zc = jnp.zeros((nrow, cuts), F32)
            zm = jnp.zeros((nrow, slots), F32)
            far_c = mm_t(rows(far_slot[0:nrow], far_slot[nrow:2 * nrow]), slot_t)
            far_cross = (far_c[0:nrow], far_c[nrow:], zc, zc)
            near_mirror = (mirror[8:8 + nrow], mirror[8 + nrow:8 + 2 * nrow], zm, zm)
            carry_in = (None, None, None)
        else:
            state = tuple(st_ref[i] for i in range(4))
            (ci_ref, cc_in_ref, cm_ref, g0_ref, gq0_ref) = rest[:5]
            outs = rest[5:]
            both = recv_ref[...].T
            near_mirror = split4(both[0:4 * nrow], nrow)
            far_c = mm_t(both[4 * nrow:], slot_t)
            far_cross = split4(far_c, nrow)
            carry_in = tuple(
                (tuple(r[i] for i in range(4)), tuple(r[4 + i] for i in range(4))) for r in (ci_ref, cc_in_ref, cm_ref)
            )
        stack = rows(*state)
        pick_from = split4(mm(stack, inc_from), nrow)
        pick_to = split4(mm(stack, inc_to), nrow)
        pick_near = split4(mm(stack, inc_near), nrow)
        pick_recv = split4(mm(stack, inc_recv), nrow)
        prm_in = (bc_ref[...], bs_ref[...], bl_ref[...], bn_ref[...])
        prm_cut = (cc_ref[...], cs_ref[...], cl_ref[...], cstep_ref[...])
        prm_mir = (mirror[1:2], mirror[2:3], mirror[3:4], mirror[4:5])
        carry_i, fi, ti = advance(carry_in[0], pick_from, pick_to, prm_in)
        carry_c, fc, _ = advance(carry_in[1], pick_near, far_cross, prm_cut)
        carry_m, _, tmr = advance(carry_in[2], near_mirror, pick_recv, prm_mir)
        totals = mm_t(fi, inc_from) + mm_t(ti, inc_to) + mm_t(fc, inc_near) + mm_t(tmr, inc_recv)
        totals = split4(totals, nrow)

        lin, quad, ramp, capr, capq = gl_ref[...], gq_ref[...], gr_ref[...], gcr_ref[...], gcq_ref[...]
        per = pe_ref[...]
        nb = (per > 0).astype(F32) + (per < horizon - 1).astype(F32)
        denom = 2.0 * quad + 1.0 + ramp * nb
        if first:
            ext = rows(sr_lo_ref[...], sr_ref[...], sr_hi_ref[...])
            g0 = jnp.clip((ext[scen:scen + window] - lin + ramp * (ext[0:window] + ext[2 * scen:2 * scen + window]))
                          / denom, 0.0, capr)
            g0 = jnp.where((per >= 0) & (per < horizon), g0, 0.0)
            gen_real = g0[scen:scen + nrow]
            gen_react = jnp.clip(sq_ref[...], -capq, capq)
            supply = mm_t(rows(gen_real, gen_react), inc_gen)
        else:
            g0 = g0_ref[...]
            gp = mm(rows(state[2], state[3]), inc_gen)
            gp_r, gp_q = gp[0:nrow], gp[nrow:]
            gen_real = jnp.clip(
                (g0[scen:scen + nrow] - 2.0 * gp_r - lin + ramp * (g0[0:nrow] + g0[2 * scen:2 * scen + nrow]))
                / denom[scen:scen + nrow],
                0.0,
                capr,
            )
            gen_react = jnp.clip(gq0_ref[...] - 2.0 * gp_q, -capq, capq)
            supply = mm_t(rows(gen_real + gp_r, gen_react + gp_q), inc_gen)
        supply_r, supply_q = supply[0:nrow], supply[nrow:]
        mag = (totals[0] + wmv) / (degree + 1.0)
        ang = (totals[1] + wav) / (degree + 1.0)
        weight = 1.0 + BALANCE_WEIGHT * (gen_count + degree)
        pr = BALANCE_WEIGHT * (supply_r - totals[2] - lr_ref[...]) / weight
        pq = BALANCE_WEIGHT * (supply_q - totals[3] - lq_ref[...]) / weight
        if first:
            (st_out, ci_out, cc_out, cm_out, g0_out, gq0_out, pay_out) = outs
            st_out[0] = mag
            st_out[1] = ang
            st_out[2] = pr
            st_out[3] = pq
            for ref, carry in ((ci_out, carry_i), (cc_out, carry_c), (cm_out, carry_m)):
                for i in range(4):
                    ref[i] = carry[0][i]
                    ref[4 + i] = carry[1][i]
            g0_out[...] = g0
            gq0_out[...] = gen_react
            new_stack = rows(mag, ang, pr, pq)
            near_slot = mm(inc_near, slot_t)
            pay_out[...] = rows(mm(new_stack, near_slot), mm(new_stack, inc_recv)).T
        else:
            (mag_out, ang_out, pr_out, gr_out, gq_out) = outs
            mag_out[...] = mag
            ang_out[...] = ang
            pr_out[...] = pr
            gr_out[...] = gen_real
            gq_out[...] = gen_react

    common = (wm, wa, lr, lq)
    tail = (slot_t, *br_rows, *cut_rows, *gen_rows, period_ext)
    sds = jax.ShapeDtypeStruct
    st1, ci1, cc1, cm1, g0, gq0, pay_1 = vmem_call(
        lambda *refs: iteration(True, refs),
        (
            sds((4, nrow, buses), F32),
            sds((8, nrow, buses), F32),
            sds((8, nrow, cuts), F32),
            sds((8, nrow, slots), F32),
            sds((window, gens), F32),
            sds((nrow, gens), F32),
            sds((slots, 8 * nrow), F32),
        ),
        wm, *common, recv_0, mirror_t, *tail, lo, sr, hi, sq,
    )
    recv_1 = lax.all_to_all(pay_1, "net", 0, 0, tiled=True)
    mag, ang, pr, gr, gq = vmem_call(
        lambda *refs: iteration(False, refs),
        (
            sds((nrow, buses), F32),
            sds((nrow, buses), F32),
            sds((nrow, buses), F32),
            sds((nrow, gens), F32),
            sds((nrow, gens), F32),
        ),
        st1, *common, recv_1, mirror_t, *tail, ci1, cc1, cm1, g0, gq0,
    )
    shape_b = (periods, scen, buses)
    shape_g = (periods, scen, gens)
    return (mag.reshape(shape_b), ang.reshape(shape_b), pr.reshape(shape_b), gr.reshape(shape_g),
            gq.reshape(shape_g))


def solution(mesh):
    bus = P("tm", None, "net")
    one = P("net")
    return jax.shard_map(
        on_device,
        mesh=mesh,
        in_specs=(bus,) * 6 + (one,) * 12 + (one, P("net", None)) + (one,) * 5,
        out_specs=(bus,) * 5,
        check_vma=False,
    )
```

```python
import jax
import jax.numpy as jnp
from jax import lax
from jax.experimental import pallas as pl
from jax.experimental.pallas import tpu as pltpu
from jax.sharding import PartitionSpec as P

INNER = 4
STEP_SIZE = 0.0005
RADIUS = 0.05
BALANCE_WEIGHT = 2.0
HI = lax.Precision.HIGHEST
F32 = jnp.float32


def mm(a, b):
    return lax.dot_general(a, b, (((1,), (0,)), ((), ())), precision=HI, preferred_element_type=F32)


def mm_t(a, b):
    return lax.dot_general(a, b, (((1,), (1,)), ((), ())), precision=HI, preferred_element_type=F32)


def onehot(ids_row, count):
    n = ids_row.shape[1]
    return (lax.broadcasted_iota(jnp.int32, (count, n), 0) == ids_row).astype(F32)


def col_sum(inc):
    return mm_t(jnp.ones((8, inc.shape[1]), F32), inc)[0:1]


def rows(*parts):
    return jnp.concatenate(parts, axis=0)


def flows(x, g, b):
    mf, af, mt, at = x
    d = af - at
    c = jnp.cos(d)
    s = jnp.sin(d)
    p = mf * mt
    return (
        g * mf * mf - p * (g * c + b * s),
        -b * mf * mf - p * (g * s - b * c),
        g * mt * mt - p * (g * c - b * s),
        -b * mt * mt + p * (g * s + b * c),
    )


def energy_grad(x, t, ft, g, b, l2):
    mf, af, mt, at = x
    d = af - at
    c = jnp.cos(d)
    s = jnp.sin(d)
    p = mf * mt
    ka = g * c + b * s
    kb = g * s - b * c
    kc = g * c - b * s
    kd = g * s + b * c
    f0 = g * mf * mf - p * ka
    f1 = -b * mf * mf - p * kb
    f2 = g * mt * mt - p * kc
    f3 = -b * mt * mt + p * kd
    ef = jnp.maximum(f0 * f0 + f1 * f1 - l2, 0.0)
    et = jnp.maximum(f2 * f2 + f3 * f3 - l2, 0.0)
    w0 = (f0 - ft[0]) + 2.0 * ef * f0
    w1 = (f1 - ft[1]) + 2.0 * ef * f1
    w2 = (f2 - ft[2]) + 2.0 * et * f2
    w3 = (f3 - ft[3]) + 2.0 * et * f3
    g_mf = (mf - t[0]) + w0 * (2.0 * g * mf - mt * ka) - w1 * (2.0 * b * mf + mt * kb) - w2 * mt * kc + w3 * mt * kd
    g_mt = (mt - t[2]) - w0 * mf * ka - w1 * mf * kb + w2 * (2.0 * g * mt - mf * kc) - w3 * (2.0 * b * mt - mf * kd)
    g_d = p * (w0 * kb - w1 * ka + w2 * kd + w3 * kc)
    return (g_mf, (af - t[1]) + g_d, g_mt, (at - t[3]) - g_d)


def solve(x, t, ft, g, b, l2, steps):
    for attempt in range(INNER):
        grad = energy_grad(x, t, ft, g, b, l2)
        x = tuple(
            jnp.where(attempt < steps, xi - jnp.clip(STEP_SIZE * gi, -RADIUS, RADIUS), xi)
            for xi, gi in zip(x, grad)
        )
    return x


def advance(carry, near, far, prm):
    g, b, lim, steps = prm
    ends = (near[0], near[1], far[0], far[1])
    prices = (near[2], near[3], far[2], far[3])
    if carry is None:
        copies = ends
        flow_prev = flows(copies, g, b)
        volt = tuple(jnp.zeros_like(e) for e in ends)
        target = ends
        flow_target = flow_prev
        dual_flow = volt
    else:
        copies, flow_prev = carry
        volt = tuple(c - e for c, e in zip(copies, ends))
        target = tuple(e - v for e, v in zip(ends, volt))
        flow_target = tuple(f + 2.0 * q for f, q in zip(flow_prev, prices))
        dual_flow = tuple(-q for q in prices)
    copies = solve(copies, target, flow_target, g, b, lim * lim, steps)
    flow_prev = flows(copies, g, b)
    side_from = rows(
        copies[0] + volt[0], copies[1] + volt[1], flow_prev[0] + dual_flow[0], flow_prev[1] + dual_flow[1]
    )
    side_to = rows(
        copies[2] + volt[2], copies[3] + volt[3], flow_prev[2] + dual_flow[2], flow_prev[3] + dual_flow[3]
    )
    return (copies, flow_prev), side_from, side_to


def split4(a, n):
    return tuple(a[i * n:(i + 1) * n] for i in range(4))


def vmem_call(kernel, outs, *args):
    return pl.pallas_call(
        kernel,
        out_shape=outs,
        in_specs=[pl.BlockSpec(memory_space=pltpu.VMEM)] * len(args),
        out_specs=tuple(pl.BlockSpec(memory_space=pltpu.VMEM) for _ in outs),
        compiler_params=pltpu.CompilerParams(vmem_limit_bytes=48 * 1024 * 1024),
    )(*args)


def slot_table(peer_col, cap, slots):
    cuts = peer_col.shape[0]
    parts = slots // cap
    mine = (peer_col == lax.broadcasted_iota(jnp.int32, (cuts, parts), 1)).astype(F32)
    same = mm_t(mine, mine)
    earlier = lax.broadcasted_iota(jnp.int32, (cuts, cuts), 1) < lax.broadcasted_iota(jnp.int32, (cuts, cuts), 0)
    rank = jnp.sum(jnp.where(earlier, same, 0.0), axis=1, keepdims=True)
    position = peer_col.astype(F32) * cap + rank
    return (position == lax.broadcasted_iota(jnp.int32, (cuts, slots), 1).astype(F32)).astype(F32)


def on_device(
    warm_mag, warm_angle, load_real, load_react, start_real, start_react,
    gen_bus, gen_linear, gen_quad, gen_ramp, gen_cap_real, gen_cap_react,
    branch_from, branch_to, branch_cond, branch_susc, branch_limit, branch_steps,
    cut_near, cut_peer, cut_bus, cut_cond, cut_susc, cut_limit, cut_steps,
):
    periods, scen, buses = warm_mag.shape
    nrow = periods * scen
    cuts = cut_near.shape[0]
    parts = lax.axis_size("net")
    cap = max(2, cuts // parts * 2)
    slots = parts * cap
    gens = gen_bus.shape[0]
    ntm = lax.axis_size("tm")
    horizon = periods * ntm

    def row(v):
        return v.reshape(1, -1)

    wm = warm_mag.reshape(nrow, buses)
    wa = warm_angle.reshape(nrow, buses)
    lr = load_real.reshape(nrow, buses)
    lq = load_react.reshape(nrow, buses)
    sr = start_real.reshape(nrow, gens)
    sq = start_react.reshape(nrow, gens)
    halo = 2 * scen
    lo = lax.ppermute(sr[nrow - halo:], "tm", [(i, i + 1) for i in range(ntm - 1)])
    hi = lax.ppermute(sr[:halo], "tm", [(i + 1, i) for i in range(ntm - 1)])
    window = nrow + 2 * scen
    period_ext = (
        lax.axis_index("tm") * periods - 1 + jnp.arange(window, dtype=jnp.int32) // scen
    ).reshape(window, 1)
    gen_rows = (row(gen_bus), row(gen_linear), row(gen_quad), row(gen_ramp), row(gen_cap_real), row(gen_cap_react))
    br_rows = (row(branch_from), row(branch_to), row(branch_cond), row(branch_susc), row(branch_limit),
               row(branch_steps.astype(F32)))
    cut_rows = (row(cut_near), row(cut_cond), row(cut_susc), row(cut_limit), row(cut_steps.astype(F32)))
    cut_bus_row = row(cut_bus.astype(F32))
    nvals0 = 128

    def prep_kernel(peer_ref, near_ref, bus_ref, cond_ref, susc_ref, lim_ref, steps_ref, wm_ref, wa_ref,
                    slot_out, pay_out):
        slot_t = slot_table(peer_ref[...], cap, slots)
        slot_out[...] = slot_t
        inc_near = onehot(near_ref[...], buses)
        by_slot = mm(inc_near, slot_t)
        prm = rows(bus_ref[...] + 1.0, cond_ref[...], susc_ref[...], lim_ref[...], steps_ref[...],
                   jnp.zeros((3, cuts), F32))
        vals = rows(
            mm(prm, slot_t),
            mm(rows(wm_ref[...], wa_ref[...]), by_slot),
            jnp.zeros((nvals0 - 8 - 2 * nrow, slots), F32),
        )
        pay_out[...] = vals.T

    slot_t, pay_setup = vmem_call(
        prep_kernel,
        (jax.ShapeDtypeStruct((cuts, slots), F32), jax.ShapeDtypeStruct((slots, nvals0), F32)),
        cut_peer, cut_rows[0], cut_bus_row, cut_rows[1], cut_rows[2], cut_rows[3], cut_rows[4], wm, wa,
    )
    recv_setup = lax.all_to_all(pay_setup, "net", 0, 0, tiled=True)

    def mid_kernel(recv_ref, wm_ref, wa_ref, mirror_out, pay_out):
        mirror = recv_ref[...].T
        mirror_out[...] = mirror
        inc_recv = onehot(mirror[0:1].astype(jnp.int32) - 1, buses)
        vals = rows(mm(rows(wm_ref[...], wa_ref[...]), inc_recv), jnp.zeros((nvals0 - 2 * nrow, slots), F32))
        pay_out[...] = vals.T

    mirror_t, pay_0 = vmem_call(
        mid_kernel,
        (jax.ShapeDtypeStruct((nvals0, slots), F32), jax.ShapeDtypeStruct((slots, nvals0), F32)),
        recv_setup, wm, wa,
    )
    recv_0 = lax.all_to_all(pay_0, "net", 0, 0, tiled=True)

    def local_part(first, refs):
        if first:
            (wm_ref, wa_ref, bf_ref, bt_ref, bc_ref, bs_ref, bl_ref, bn_ref,
             gb_ref, gl_ref, gq_ref, gr_ref, gcr_ref, gcq_ref, pe_ref,
             sr_lo_ref, sr_ref, sr_hi_ref, sq_ref,
             tot_out, sup_out, ci_out, g0_out, gq0_out) = refs
            zero_b = jnp.zeros((nrow, buses), F32)
            state = (wm_ref[...], wa_ref[...], zero_b, zero_b)
            carry_in = None
        else:
            (st_ref, bf_ref, bt_ref, bc_ref, bs_ref, bl_ref, bn_ref,
             gb_ref, gl_ref, gq_ref, gr_ref, gcr_ref, gcq_ref, pe_ref,
             ci_ref, g0_ref, gq0_ref,
             tot_out, sup_out, gr_out, gq_out) = refs
            state = tuple(st_ref[i] for i in range(4))
            carry_in = (tuple(ci_ref[i] for i in range(4)), tuple(ci_ref[4 + i] for i in range(4)))
        inc_from = onehot(bf_ref[...], buses)
        inc_to = onehot(bt_ref[...], buses)
        inc_gen = onehot(gb_ref[...], buses)
        stack = rows(*state)
        pick_from = split4(mm(stack, inc_from), nrow)
        pick_to = split4(mm(stack, inc_to), nrow)
        prm_in = (bc_ref[...], bs_ref[...], bl_ref[...], bn_ref[...])
        carry_i, fi, ti = advance(carry_in, pick_from, pick_to, prm_in)
        totals = mm_t(fi, inc_from) + mm_t(ti, inc_to)
        for i in range(4):
            tot_out[i] = totals[i * nrow:(i + 1) * nrow]
        lin, quad, ramp, capr, capq = gl_ref[...], gq_ref[...], gr_ref[...], gcr_ref[...], gcq_ref[...]
        per = pe_ref[...]
        nb = (per > 0).astype(F32) + (per < horizon - 1).astype(F32)
        denom = 2.0 * quad + 1.0 + ramp * nb
        if first:
            ext = rows(sr_lo_ref[...], sr_ref[...], sr_hi_ref[...])
            g0 = jnp.clip((ext[scen:scen + window] - lin + ramp * (ext[0:window] + ext[2 * scen:2 * scen + window]))
                          / denom, 0.0, capr)
            g0 = jnp.where((per >= 0) & (per < horizon), g0, 0.0)
            gen_real = g0[scen:scen + nrow]
            gen_react = jnp.clip(sq_ref[...], -capq, capq)
            supply = mm_t(rows(gen_real, gen_react), inc_gen)
            for i in range(4):
                ci_out[i] = carry_i[0][i]
                ci_out[4 + i] = carry_i[1][i]
            g0_out[...] = g0
            gq0_out[...] = gen_react
        else:
            g0 = g0_ref[...]
            gp = mm(rows(state[2], state[3]), inc_gen)
            gp_r, gp_q = gp[0:nrow], gp[nrow:]
            gen_real = jnp.clip(
                (g0[scen:scen + nrow] - 2.0 * gp_r - lin + ramp * (g0[0:nrow] + g0[2 * scen:2 * scen + nrow]))
                / denom[scen:scen + nrow],
                0.0,
                capr,
            )
            gen_react = jnp.clip(gq0_ref[...] - 2.0 * gp_q, -capq, capq)
            supply = mm_t(rows(gen_real + gp_r, gen_react + gp_q), inc_gen)
            gr_out[...] = gen_real
            gq_out[...] = gen_react
        sup_out[0] = supply[0:nrow]
        sup_out[1] = supply[nrow:]

    def mirror0_kernel(mirror_ref, wm_ref, wa_ref, tot_out, cm_out):
        mirror = mirror_ref[...]
        inc_recv = onehot(mirror[0:1].astype(jnp.int32) - 1, buses)
        zm = jnp.zeros((nrow, slots), F32)
        zero_b = jnp.zeros((nrow, buses), F32)
        stack = rows(wm_ref[...], wa_ref[...], zero_b, zero_b)
        pick_recv = split4(mm(stack, inc_recv), nrow)
        near_mirror = (mirror[8:8 + nrow], mirror[8 + nrow:8 + 2 * nrow], zm, zm)
        prm_mir = (mirror[1:2], mirror[2:3], mirror[3:4], mirror[4:5])
        carry_m, _, tmr = advance(None, near_mirror, pick_recv, prm_mir)
        totals = mm_t(tmr, inc_recv)
        for i in range(4):
            tot_out[i] = totals[i * nrow:(i + 1) * nrow]
            cm_out[i] = carry_m[0][i]
            cm_out[4 + i] = carry_m[1][i]

    def cut_part(first, refs):
        (st_ref, wm_ref, wa_ref, lr_ref, lq_ref, recv_ref, mirror_ref, slot_ref,
         bf_ref, bt_ref, cn_ref, cc_ref, cs_ref, cl_ref, cstep_ref, gb_ref,
         tin_ref, sup_ref, tm_ref) = refs[:19]
        rest = refs[19:]
        wmv, wav = wm_ref[...], wa_ref[...]
        slot_t = slot_ref[...]
        mirror = mirror_ref[...]
        inc_near = onehot(cn_ref[...], buses)
        inc_recv = onehot(mirror[0:1].astype(jnp.int32) - 1, buses)
        degree = (col_sum(onehot(bf_ref[...], buses)) + col_sum(onehot(bt_ref[...], buses)) + col_sum(inc_near)
                  + col_sum(inc_recv))
        gen_count = col_sum(onehot(gb_ref[...], buses))
        prm_cut = (cc_ref[...], cs_ref[...], cl_ref[...], cstep_ref[...])
        if first:
            (cc_out, st_out, pay_out) = rest
            zero_b = jnp.zeros((nrow, buses), F32)
            state = (wmv, wav, zero_b, zero_b)
            far_slot = recv_ref[...].T
            zc = jnp.zeros((nrow, cuts), F32)
            far_c = mm_t(rows(far_slot[0:nrow], far_slot[nrow:2 * nrow]), slot_t)
            far_cross = (far_c[0:nrow], far_c[nrow:], zc, zc)
            stack = rows(*state)
            pick_near = split4(mm(stack, inc_near), nrow)
            carry_c, fc, _ = advance(None, pick_near, far_cross, prm_cut)
            totals = tin_ref[...] + tm_ref[...] + mm_t(fc, inc_near).reshape(4, nrow, buses)
        else:
            (cc_in_ref, cm_ref, mag_out, ang_out, pr_out) = rest
            state = tuple(st_ref[i] for i in range(4))
            both = recv_ref[...].T
            near_mirror = split4(both[0:4 * nrow], nrow)
            far_cross = split4(mm_t(both[4 * nrow:], slot_t), nrow)
            stack = rows(*state)
            pick_near = split4(mm(stack, inc_near), nrow)
            pick_recv = split4(mm(stack, inc_recv), nrow)
            carry_c_in = (tuple(cc_in_ref[i] for i in range(4)), tuple(cc_in_ref[4 + i] for i in range(4)))
            carry_m_in = (tuple(cm_ref[i] for i in range(4)), tuple(cm_ref[4 + i] for i in range(4)))
            _, fc, _ = advance(carry_c_in, pick_near, far_cross, prm_cut)
            prm_mir = (mirror[1:2], mirror[2:3], mirror[3:4], mirror[4:5])
            _, _, tmr = advance(carry_m_in, near_mirror, pick_recv, prm_mir)
            totals = tin_ref[...] + (mm_t(fc, inc_near) + mm_t(tmr, inc_recv)).reshape(4, nrow, buses)
        mag = (totals[0] + wmv) / (degree + 1.0)
        ang = (totals[1] + wav) / (degree + 1.0)
        weight = 1.0 + BALANCE_WEIGHT * (gen_count + degree)
        pr = BALANCE_WEIGHT * (sup_ref[0] - totals[2] - lr_ref[...]) / weight
        pq = BALANCE_WEIGHT * (sup_ref[1] - totals[3] - lq_ref[...]) / weight
        if first:
            for i in range(4):
                cc_out[i] = carry_c[0][i]
                cc_out[4 + i] = carry_c[1][i]
            st_out[0] = mag
            st_out[1] = ang
            st_out[2] = pr
            st_out[3] = pq
            new_stack = rows(mag, ang, pr, pq)
            near_slot = mm(inc_near, slot_t)
            pay_out[...] = rows(mm(new_stack, near_slot), mm(new_stack, inc_recv)).T
        else:
            mag_out[...] = mag
            ang_out[...] = ang
            pr_out[...] = pr

    sds = jax.ShapeDtypeStruct
    tot_shape = sds((4, nrow, buses), F32)
    br_all = br_rows
    gen_all = (*gen_rows, period_ext)
    tin0, sup0, ci1, g0, gq0 = vmem_call(
        lambda *refs: local_part(True, refs),
        (tot_shape, sds((2, nrow, buses), F32), sds((8, nrow, buses), F32), sds((window, gens), F32),
         sds((nrow, gens), F32)),
        wm, wa, *br_all, *gen_all, lo, sr, hi, sq,
    )
    tm0, cm1 = vmem_call(
        mirror0_kernel, (tot_shape, sds((8, nrow, slots), F32)), mirror_t, wm, wa,
    )
    cut_in = (*cut_rows, gen_rows[0])
    cc1, st1, pay_1 = vmem_call(
        lambda *refs: cut_part(True, refs),
        (sds((8, nrow, cuts), F32), tot_shape, sds((slots, 8 * nrow), F32)),
        wm, wm, wa, lr, lq, recv_0, mirror_t, slot_t, br_rows[0], br_rows[1], *cut_in, tin0, sup0, tm0,
    )
    recv_1 = lax.all_to_all(pay_1, "net", 0, 0, tiled=True)
    tin1, sup1, gr, gq = vmem_call(
        lambda *refs: local_part(False, refs),
        (tot_shape, sds((2, nrow, buses), F32), sds((nrow, gens), F32), sds((nrow, gens), F32)),
        st1, *br_all, *gen_all, ci1, g0, gq0,
    )
    mag, ang, pr = vmem_call(
        lambda *refs: cut_part(False, refs),
        (sds((nrow, buses), F32), sds((nrow, buses), F32), sds((nrow, buses), F32)),
        st1, wm, wa, lr, lq, recv_1, mirror_t, slot_t, br_rows[0], br_rows[1], *cut_in, tin1, sup1, tin1,
        cc1, cm1,
    )
    shape_b = (periods, scen, buses)
    shape_g = (periods, scen, gens)
    return (mag.reshape(shape_b), ang.reshape(shape_b), pr.reshape(shape_b), gr.reshape(shape_g),
            gq.reshape(shape_g))


def solution(mesh):
    bus = P("tm", None, "net")
    one = P("net")
    return jax.shard_map(
        on_device,
        mesh=mesh,
        in_specs=(bus,) * 6 + (one,) * 12 + (one, P("net", None)) + (one,) * 5,
        out_specs=(bus,) * 5,
        check_vma=False,
    )
```

```python
import jax
import jax.numpy as jnp
from jax import lax
from jax.experimental import pallas as pl
from jax.experimental.pallas import tpu as pltpu
from jax.sharding import PartitionSpec as P

INNER = 4
STEP_SIZE = 0.0005
RADIUS = 0.05
BALANCE_WEIGHT = 2.0
HI = lax.Precision.HIGHEST
F32 = jnp.float32


def mm(a, b):
    return lax.dot_general(a, b, (((1,), (0,)), ((), ())), precision=HI, preferred_element_type=F32)


def mm_t(a, b):
    return lax.dot_general(a, b, (((1,), (1,)), ((), ())), precision=HI, preferred_element_type=F32)


def onehot(ids_row, count):
    n = ids_row.shape[1]
    return (lax.broadcasted_iota(jnp.int32, (count, n), 0) == ids_row).astype(F32)


def col_sum(inc):
    return mm_t(jnp.ones((8, inc.shape[1]), F32), inc)[0:1]


def rows(*parts):
    return jnp.concatenate(parts, axis=0)


def trig(x):
    d = x[1] - x[3]
    return (jnp.cos(d), jnp.sin(d))


def flows(x, cs, g, b):
    mf, _, mt, _ = x
    c, s = cs
    p = mf * mt
    return (
        g * mf * mf - p * (g * c + b * s),
        -b * mf * mf - p * (g * s - b * c),
        g * mt * mt - p * (g * c - b * s),
        -b * mt * mt + p * (g * s + b * c),
    )


def energy_grad(x, cs, f, t, ft, g, b, l2):
    mf, af, mt, at = x
    c, s = cs
    p = mf * mt
    ka = g * c + b * s
    kb = g * s - b * c
    kc = g * c - b * s
    kd = g * s + b * c
    if f is None:
        f = (g * mf * mf - p * ka, -b * mf * mf - p * kb, g * mt * mt - p * kc, -b * mt * mt + p * kd)
    f0, f1, f2, f3 = f
    ef = jnp.maximum(f0 * f0 + f1 * f1 - l2, 0.0)
    et = jnp.maximum(f2 * f2 + f3 * f3 - l2, 0.0)
    w0 = (f0 - ft[0]) + 2.0 * ef * f0
    w1 = (f1 - ft[1]) + 2.0 * ef * f1
    w2 = (f2 - ft[2]) + 2.0 * et * f2
    w3 = (f3 - ft[3]) + 2.0 * et * f3
    g_mf = (mf - t[0]) + w0 * (2.0 * g * mf - mt * ka) - w1 * (2.0 * b * mf + mt * kb) - w2 * mt * kc + w3 * mt * kd
    g_mt = (mt - t[2]) - w0 * mf * ka - w1 * mf * kb + w2 * (2.0 * g * mt - mf * kc) - w3 * (2.0 * b * mt - mf * kd)
    g_d = p * (w0 * kb - w1 * ka + w2 * kd + w3 * kc)
    return (g_mf, (af - t[1]) + g_d, g_mt, (at - t[3]) - g_d)


def solve(x, cs, f, t, ft, g, b, l2, steps):
    for attempt in range(INNER):
        if cs is None:
            cs = trig(x)
        grad = energy_grad(x, cs, f, t, ft, g, b, l2)
        x = tuple(
            jnp.where(attempt < steps, xi - jnp.clip(STEP_SIZE * gi, -RADIUS, RADIUS), xi)
            for xi, gi in zip(x, grad)
        )
        cs, f = None, None
    return x


def advance(carry, near, far, prm):
    g, b, lim, steps = prm
    ends = (near[0], near[1], far[0], far[1])
    prices = (near[2], near[3], far[2], far[3])
    if carry is None:
        copies = ends
        cs = trig(copies)
        flow_prev = flows(copies, cs, g, b)
        volt = tuple(jnp.zeros_like(e) for e in ends)
        target = ends
        flow_target = flow_prev
        dual_flow = volt
    else:
        copies, flow_prev, cs = carry
        volt = tuple(c - e for c, e in zip(copies, ends))
        target = tuple(e - v for e, v in zip(ends, volt))
        flow_target = tuple(f + 2.0 * q for f, q in zip(flow_prev, prices))
        dual_flow = tuple(-q for q in prices)
    copies = solve(copies, cs, flow_prev, target, flow_target, g, b, lim * lim, steps)
    cs = trig(copies)
    flow_prev = flows(copies, cs, g, b)
    side_from = rows(
        copies[0] + volt[0], copies[1] + volt[1], flow_prev[0] + dual_flow[0], flow_prev[1] + dual_flow[1]
    )
    side_to = rows(
        copies[2] + volt[2], copies[3] + volt[3], flow_prev[2] + dual_flow[2], flow_prev[3] + dual_flow[3]
    )
    return (copies, flow_prev, cs), side_from, side_to


def store_carry(ref, carry):
    for i in range(4):
        ref[i] = carry[0][i]
        ref[4 + i] = carry[1][i]
    ref[8] = carry[2][0]
    ref[9] = carry[2][1]


def load_carry(ref):
    return (tuple(ref[i] for i in range(4)), tuple(ref[4 + i] for i in range(4)), (ref[8], ref[9]))


def split4(a, n):
    return tuple(a[i * n:(i + 1) * n] for i in range(4))


def vmem_call(kernel, outs, *args):
    return pl.pallas_call(
        kernel,
        out_shape=outs,
        in_specs=[pl.BlockSpec(memory_space=pltpu.VMEM)] * len(args),
        out_specs=tuple(pl.BlockSpec(memory_space=pltpu.VMEM) for _ in outs),
        compiler_params=pltpu.CompilerParams(vmem_limit_bytes=48 * 1024 * 1024),
    )(*args)


def slot_table(peer_col, cap, slots):
    cuts = peer_col.shape[0]
    parts = slots // cap
    mine = (peer_col == lax.broadcasted_iota(jnp.int32, (cuts, parts), 1)).astype(F32)
    same = mm_t(mine, mine)
    earlier = lax.broadcasted_iota(jnp.int32, (cuts, cuts), 1) < lax.broadcasted_iota(jnp.int32, (cuts, cuts), 0)
    rank = jnp.sum(jnp.where(earlier, same, 0.0), axis=1, keepdims=True)
    position = peer_col.astype(F32) * cap + rank
    return (position == lax.broadcasted_iota(jnp.int32, (cuts, slots), 1).astype(F32)).astype(F32)


def on_device(
    warm_mag, warm_angle, load_real, load_react, start_real, start_react,
    gen_bus, gen_linear, gen_quad, gen_ramp, gen_cap_real, gen_cap_react,
    branch_from, branch_to, branch_cond, branch_susc, branch_limit, branch_steps,
    cut_near, cut_peer, cut_bus, cut_cond, cut_susc, cut_limit, cut_steps,
):
    periods, scen, buses = warm_mag.shape
    nrow = periods * scen
    cuts = cut_near.shape[0]
    parts = lax.axis_size("net")
    cap = max(2, cuts // parts * 2)
    slots = parts * cap
    gens = gen_bus.shape[0]
    ntm = lax.axis_size("tm")
    horizon = periods * ntm

    def row(v):
        return v.reshape(1, -1)

    wm = warm_mag.reshape(nrow, buses)
    wa = warm_angle.reshape(nrow, buses)
    lr = load_real.reshape(nrow, buses)
    lq = load_react.reshape(nrow, buses)
    sr = start_real.reshape(nrow, gens)
    sq = start_react.reshape(nrow, gens)
    halo = 2 * scen
    lo = lax.ppermute(sr[nrow - halo:], "tm", [(i, i + 1) for i in range(ntm - 1)])
    hi = lax.ppermute(sr[:halo], "tm", [(i + 1, i) for i in range(ntm - 1)])
    window = nrow + 2 * scen
    period_ext = (
        lax.axis_index("tm") * periods - 1 + jnp.arange(window, dtype=jnp.int32) // scen
    ).reshape(window, 1)
    gen_rows = (row(gen_bus), row(gen_linear), row(gen_quad), row(gen_ramp), row(gen_cap_real), row(gen_cap_react))
    br_rows = (row(branch_from), row(branch_to), row(branch_cond), row(branch_susc), row(branch_limit),
               row(branch_steps.astype(F32)))
    cut_rows = (row(cut_near), row(cut_cond), row(cut_susc), row(cut_limit), row(cut_steps.astype(F32)))
    cut_bus_row = row(cut_bus.astype(F32))
    nvals0 = 128

    def prep_kernel(peer_ref, near_ref, bus_ref, cond_ref, susc_ref, lim_ref, steps_ref, wm_ref, wa_ref,
                    slot_out, pay_out):
        slot_t = slot_table(peer_ref[...], cap, slots)
        slot_out[...] = slot_t
        inc_near = onehot(near_ref[...], buses)
        by_slot = mm(inc_near, slot_t)
        prm = rows(bus_ref[...] + 1.0, cond_ref[...], susc_ref[...], lim_ref[...], steps_ref[...],
                   jnp.zeros((3, cuts), F32))
        vals = rows(
            mm(prm, slot_t),
            mm(rows(wm_ref[...], wa_ref[...]), by_slot),
            jnp.zeros((nvals0 - 8 - 2 * nrow, slots), F32),
        )
        pay_out[...] = vals.T

    slot_t, pay_setup = vmem_call(
        prep_kernel,
        (jax.ShapeDtypeStruct((cuts, slots), F32), jax.ShapeDtypeStruct((slots, nvals0), F32)),
        cut_peer, cut_rows[0], cut_bus_row, cut_rows[1], cut_rows[2], cut_rows[3], cut_rows[4], wm, wa,
    )
    recv_setup = lax.all_to_all(pay_setup, "net", 0, 0, tiled=True)

    def mid_kernel(recv_ref, wm_ref, wa_ref, mirror_out, pay_out):
        mirror = recv_ref[...].T
        mirror_out[...] = mirror
        inc_recv = onehot(mirror[0:1].astype(jnp.int32) - 1, buses)
        vals = rows(mm(rows(wm_ref[...], wa_ref[...]), inc_recv), jnp.zeros((nvals0 - 2 * nrow, slots), F32))
        pay_out[...] = vals.T

    mirror_t, pay_0 = vmem_call(
        mid_kernel,
        (jax.ShapeDtypeStruct((nvals0, slots), F32), jax.ShapeDtypeStruct((slots, nvals0), F32)),
        recv_setup, wm, wa,
    )
    recv_0 = lax.all_to_all(pay_0, "net", 0, 0, tiled=True)

    def local_part(first, refs):
        if first:
            (wm_ref, wa_ref, bf_ref, bt_ref, bc_ref, bs_ref, bl_ref, bn_ref,
             gb_ref, gl_ref, gq_ref, gr_ref, gcr_ref, gcq_ref, pe_ref,
             sr_lo_ref, sr_ref, sr_hi_ref, sq_ref,
             tot_out, sup_out, ci_out, g0_out, gq0_out) = refs
            zero_b = jnp.zeros((nrow, buses), F32)
            state = (wm_ref[...], wa_ref[...], zero_b, zero_b)
            carry_in = None
        else:
            (st_ref, bf_ref, bt_ref, bc_ref, bs_ref, bl_ref, bn_ref,
             gb_ref, gl_ref, gq_ref, gr_ref, gcr_ref, gcq_ref, pe_ref,
             ci_ref, g0_ref, gq0_ref,
             tot_out, sup_out, gr_out, gq_out) = refs
            state = tuple(st_ref[i] for i in range(4))
            carry_in = load_carry(ci_ref)
        inc_from = onehot(bf_ref[...], buses)
        inc_to = onehot(bt_ref[...], buses)
        inc_gen = onehot(gb_ref[...], buses)
        stack = rows(*state)
        pick_from = split4(mm(stack, inc_from), nrow)
        pick_to = split4(mm(stack, inc_to), nrow)
        prm_in = (bc_ref[...], bs_ref[...], bl_ref[...], bn_ref[...])
        carry_i, fi, ti = advance(carry_in, pick_from, pick_to, prm_in)
        totals = mm_t(fi, inc_from) + mm_t(ti, inc_to)
        for i in range(4):
            tot_out[i] = totals[i * nrow:(i + 1) * nrow]
        lin, quad, ramp, capr, capq = gl_ref[...], gq_ref[...], gr_ref[...], gcr_ref[...], gcq_ref[...]
        per = pe_ref[...]
        nb = (per > 0).astype(F32) + (per < horizon - 1).astype(F32)
        denom = 2.0 * quad + 1.0 + ramp * nb
        if first:
            ext = rows(sr_lo_ref[...], sr_ref[...], sr_hi_ref[...])
            g0 = jnp.clip((ext[scen:scen + window] - lin + ramp * (ext[0:window] + ext[2 * scen:2 * scen + window]))
                          / denom, 0.0, capr)
            g0 = jnp.where((per >= 0) & (per < horizon), g0, 0.0)
            gen_real = g0[scen:scen + nrow]
            gen_react = jnp.clip(sq_ref[...], -capq, capq)
            supply = mm_t(rows(gen_real, gen_react), inc_gen)
            store_carry(ci_out, carry_i)
            g0_out[...] = g0
            gq0_out[...] = gen_react
        else:
            g0 = g0_ref[...]
            gp = mm(rows(state[2], state[3]), inc_gen)
            gp_r, gp_q = gp[0:nrow], gp[nrow:]
            gen_real = jnp.clip(
                (g0[scen:scen + nrow] - 2.0 * gp_r - lin + ramp * (g0[0:nrow] + g0[2 * scen:2 * scen + nrow]))
                / denom[scen:scen + nrow],
                0.0,
                capr,
            )
            gen_react = jnp.clip(gq0_ref[...] - 2.0 * gp_q, -capq, capq)
            supply = mm_t(rows(gen_real + gp_r, gen_react + gp_q), inc_gen)
            gr_out[...] = gen_real
            gq_out[...] = gen_react
        sup_out[0] = supply[0:nrow]
        sup_out[1] = supply[nrow:]

    def mirror0_kernel(mirror_ref, wm_ref, wa_ref, bf_ref, bt_ref, cn_ref, gb_ref, tot_out, cm_out, dg_out):
        mirror = mirror_ref[...]
        inc_recv = onehot(mirror[0:1].astype(jnp.int32) - 1, buses)
        degree = (col_sum(onehot(bf_ref[...], buses)) + col_sum(onehot(bt_ref[...], buses))
                  + col_sum(onehot(cn_ref[...], buses)) + col_sum(inc_recv))
        dg_out[...] = rows(degree, col_sum(onehot(gb_ref[...], buses)), jnp.zeros((6, buses), F32))
        zm = jnp.zeros((nrow, slots), F32)
        zero_b = jnp.zeros((nrow, buses), F32)
        stack = rows(wm_ref[...], wa_ref[...], zero_b, zero_b)
        pick_recv = split4(mm(stack, inc_recv), nrow)
        near_mirror = (mirror[8:8 + nrow], mirror[8 + nrow:8 + 2 * nrow], zm, zm)
        prm_mir = (mirror[1:2], mirror[2:3], mirror[3:4], mirror[4:5])
        carry_m, _, tmr = advance(None, near_mirror, pick_recv, prm_mir)
        totals = mm_t(tmr, inc_recv)
        for i in range(4):
            tot_out[i] = totals[i * nrow:(i + 1) * nrow]
        store_carry(cm_out, carry_m)

    def cut_part(first, refs):
        (st_ref, wm_ref, wa_ref, lr_ref, lq_ref, recv_ref, mirror_ref, slot_ref,
         dg_ref, cn_ref, cc_ref, cs_ref, cl_ref, cstep_ref,
         tin_ref, sup_ref, tm_ref) = refs[:17]
        rest = refs[17:]
        wmv, wav = wm_ref[...], wa_ref[...]
        slot_t = slot_ref[...]
        mirror = mirror_ref[...]
        inc_near = onehot(cn_ref[...], buses)
        inc_recv = onehot(mirror[0:1].astype(jnp.int32) - 1, buses)
        degree = dg_ref[0:1]
        gen_count = dg_ref[1:2]
        prm_cut = (cc_ref[...], cs_ref[...], cl_ref[...], cstep_ref[...])
        if first:
            (cc_out, st_out, pay_out) = rest
            zero_b = jnp.zeros((nrow, buses), F32)
            state = (wmv, wav, zero_b, zero_b)
            far_slot = recv_ref[...].T
            zc = jnp.zeros((nrow, cuts), F32)
            far_c = mm_t(rows(far_slot[0:nrow], far_slot[nrow:2 * nrow]), slot_t)
            far_cross = (far_c[0:nrow], far_c[nrow:], zc, zc)
            stack = rows(*state)
            pick_near = split4(mm(stack, inc_near), nrow)
            carry_c, fc, _ = advance(None, pick_near, far_cross, prm_cut)
            totals = tin_ref[...] + tm_ref[...] + mm_t(fc, inc_near).reshape(4, nrow, buses)
        else:
            (cc_in_ref, cm_ref, mag_out, ang_out, pr_out) = rest
            state = tuple(st_ref[i] for i in range(4))
            both = recv_ref[...].T
            near_mirror = split4(both[0:4 * nrow], nrow)
            far_cross = split4(mm_t(both[4 * nrow:], slot_t), nrow)
            stack = rows(*state)
            pick_near = split4(mm(stack, inc_near), nrow)
            pick_recv = split4(mm(stack, inc_recv), nrow)
            carry_c_in = load_carry(cc_in_ref)
            carry_m_in = load_carry(cm_ref)
            _, fc, _ = advance(carry_c_in, pick_near, far_cross, prm_cut)
            prm_mir = (mirror[1:2], mirror[2:3], mirror[3:4], mirror[4:5])
            _, _, tmr = advance(carry_m_in, near_mirror, pick_recv, prm_mir)
            totals = tin_ref[...] + (mm_t(fc, inc_near) + mm_t(tmr, inc_recv)).reshape(4, nrow, buses)
        mag = (totals[0] + wmv) / (degree + 1.0)
        ang = (totals[1] + wav) / (degree + 1.0)
        weight = 1.0 + BALANCE_WEIGHT * (gen_count + degree)
        pr = BALANCE_WEIGHT * (sup_ref[0] - totals[2] - lr_ref[...]) / weight
        pq = BALANCE_WEIGHT * (sup_ref[1] - totals[3] - lq_ref[...]) / weight
        if first:
            store_carry(cc_out, carry_c)
            st_out[0] = mag
            st_out[1] = ang
            st_out[2] = pr
            st_out[3] = pq
            new_stack = rows(mag, ang, pr, pq)
            near_slot = mm(inc_near, slot_t)
            pay_out[...] = rows(mm(new_stack, near_slot), mm(new_stack, inc_recv)).T
        else:
            mag_out[...] = mag
            ang_out[...] = ang
            pr_out[...] = pr

    sds = jax.ShapeDtypeStruct
    tot_shape = sds((4, nrow, buses), F32)
    br_all = br_rows
    gen_all = (*gen_rows, period_ext)
    tin0, sup0, ci1, g0, gq0 = vmem_call(
        lambda *refs: local_part(True, refs),
        (tot_shape, sds((2, nrow, buses), F32), sds((10, nrow, buses), F32), sds((window, gens), F32),
         sds((nrow, gens), F32)),
        wm, wa, *br_all, *gen_all, lo, sr, hi, sq,
    )
    tm0, cm1, dg = vmem_call(
        mirror0_kernel, (tot_shape, sds((10, nrow, slots), F32), sds((8, buses), F32)), mirror_t, wm, wa,
        br_rows[0], br_rows[1], cut_rows[0], gen_rows[0],
    )
    cut_in = cut_rows
    cc1, st1, pay_1 = vmem_call(
        lambda *refs: cut_part(True, refs),
        (sds((10, nrow, cuts), F32), tot_shape, sds((slots, 8 * nrow), F32)),
        wm, wm, wa, lr, lq, recv_0, mirror_t, slot_t, dg, *cut_in, tin0, sup0, tm0,
    )
    recv_1 = lax.all_to_all(pay_1, "net", 0, 0, tiled=True)
    tin1, sup1, gr, gq = vmem_call(
        lambda *refs: local_part(False, refs),
        (tot_shape, sds((2, nrow, buses), F32), sds((nrow, gens), F32), sds((nrow, gens), F32)),
        st1, *br_all, *gen_all, ci1, g0, gq0,
    )
    mag, ang, pr = vmem_call(
        lambda *refs: cut_part(False, refs),
        (sds((nrow, buses), F32), sds((nrow, buses), F32), sds((nrow, buses), F32)),
        st1, wm, wa, lr, lq, recv_1, mirror_t, slot_t, dg, *cut_in, tin1, sup1, tin1,
        cc1, cm1,
    )
    shape_b = (periods, scen, buses)
    shape_g = (periods, scen, gens)
    return (mag.reshape(shape_b), ang.reshape(shape_b), pr.reshape(shape_b), gr.reshape(shape_g),
            gq.reshape(shape_g))


def solution(mesh):
    bus = P("tm", None, "net")
    one = P("net")
    return jax.shard_map(
        on_device,
        mesh=mesh,
        in_specs=(bus,) * 6 + (one,) * 12 + (one, P("net", None)) + (one,) * 5,
        out_specs=(bus,) * 5,
        check_vma=False,
    )
```

```python
import jax
import jax.numpy as jnp
from jax import lax
from jax.experimental import pallas as pl
from jax.experimental.pallas import tpu as pltpu
from jax.sharding import PartitionSpec as P

INNER = 4
STEP_SIZE = 0.0005
RADIUS = 0.05
BALANCE_WEIGHT = 2.0
HI = lax.Precision.HIGHEST
F32 = jnp.float32


def mm(a, b):
    return lax.dot_general(a, b, (((1,), (0,)), ((), ())), precision=HI, preferred_element_type=F32)


def mm_t(a, b):
    return lax.dot_general(a, b, (((1,), (1,)), ((), ())), precision=HI, preferred_element_type=F32)


def onehot(ids_row, count):
    n = ids_row.shape[1]
    return (lax.broadcasted_iota(jnp.int32, (count, n), 0) == ids_row).astype(F32)


def col_sum(inc):
    return mm_t(jnp.ones((8, inc.shape[1]), F32), inc)[0:1]


def rows(*parts):
    return jnp.concatenate(parts, axis=0)


def trig(x):
    d = x[1] - x[3]
    return (jnp.cos(d), jnp.sin(d))


def flows(x, cs, g, b):
    mf, _, mt, _ = x
    c, s = cs
    p = mf * mt
    return (
        g * mf * mf - p * (g * c + b * s),
        -b * mf * mf - p * (g * s - b * c),
        g * mt * mt - p * (g * c - b * s),
        -b * mt * mt + p * (g * s + b * c),
    )


def energy_grad(x, cs, f, t, ft, g, b, l2):
    mf, af, mt, at = x
    c, s = cs
    p = mf * mt
    ka = g * c + b * s
    kb = g * s - b * c
    kc = g * c - b * s
    kd = g * s + b * c
    if f is None:
        f = (g * mf * mf - p * ka, -b * mf * mf - p * kb, g * mt * mt - p * kc, -b * mt * mt + p * kd)
    f0, f1, f2, f3 = f
    ef = jnp.maximum(f0 * f0 + f1 * f1 - l2, 0.0)
    et = jnp.maximum(f2 * f2 + f3 * f3 - l2, 0.0)
    w0 = (f0 - ft[0]) + 2.0 * ef * f0
    w1 = (f1 - ft[1]) + 2.0 * ef * f1
    w2 = (f2 - ft[2]) + 2.0 * et * f2
    w3 = (f3 - ft[3]) + 2.0 * et * f3
    g_mf = (mf - t[0]) + w0 * (2.0 * g * mf - mt * ka) - w1 * (2.0 * b * mf + mt * kb) - w2 * mt * kc + w3 * mt * kd
    g_mt = (mt - t[2]) - w0 * mf * ka - w1 * mf * kb + w2 * (2.0 * g * mt - mf * kc) - w3 * (2.0 * b * mt - mf * kd)
    g_d = p * (w0 * kb - w1 * ka + w2 * kd + w3 * kc)
    return (g_mf, (af - t[1]) + g_d, g_mt, (at - t[3]) - g_d)


def solve(x, cs, f, t, ft, g, b, l2, steps):
    for attempt in range(INNER):
        if cs is None:
            cs = trig(x)
        grad = energy_grad(x, cs, f, t, ft, g, b, l2)
        x = tuple(
            jnp.where(attempt < steps, xi - jnp.clip(STEP_SIZE * gi, -RADIUS, RADIUS), xi)
            for xi, gi in zip(x, grad)
        )
        cs, f = None, None
    return x


def advance(carry, near, far, prm):
    g, b, lim, steps = prm
    ends = (near[0], near[1], far[0], far[1])
    prices = (near[2], near[3], far[2], far[3])
    if carry is None:
        copies = ends
        cs = trig(copies)
        flow_prev = flows(copies, cs, g, b)
        volt = tuple(jnp.zeros_like(e) for e in ends)
        target = ends
        flow_target = flow_prev
        dual_flow = volt
    else:
        copies, flow_prev, cs = carry
        volt = tuple(c - e for c, e in zip(copies, ends))
        target = tuple(e - v for e, v in zip(ends, volt))
        flow_target = tuple(f + 2.0 * q for f, q in zip(flow_prev, prices))
        dual_flow = tuple(-q for q in prices)
    copies = solve(copies, cs, flow_prev, target, flow_target, g, b, lim * lim, steps)
    cs = trig(copies)
    flow_prev = flows(copies, cs, g, b)
    side_from = rows(
        copies[0] + volt[0], copies[1] + volt[1], flow_prev[0] + dual_flow[0], flow_prev[1] + dual_flow[1]
    )
    side_to = rows(
        copies[2] + volt[2], copies[3] + volt[3], flow_prev[2] + dual_flow[2], flow_prev[3] + dual_flow[3]
    )
    return (copies, flow_prev, cs), side_from, side_to


def store_carry(ref, carry):
    for i in range(4):
        ref[i] = carry[0][i]
        ref[4 + i] = carry[1][i]
    ref[8] = carry[2][0]
    ref[9] = carry[2][1]


def load_carry(ref):
    return (tuple(ref[i] for i in range(4)), tuple(ref[4 + i] for i in range(4)), (ref[8], ref[9]))


def split4(a, n):
    return tuple(a[i * n:(i + 1) * n] for i in range(4))


def vmem_call(kernel, outs, *args):
    return pl.pallas_call(
        kernel,
        out_shape=outs,
        in_specs=[pl.BlockSpec(memory_space=pltpu.VMEM)] * len(args),
        out_specs=tuple(pl.BlockSpec(memory_space=pltpu.VMEM) for _ in outs),
        compiler_params=pltpu.CompilerParams(vmem_limit_bytes=48 * 1024 * 1024),
    )(*args)


def slot_table(peer_col, cap, slots):
    cuts = peer_col.shape[0]
    parts = slots // cap
    mine = (peer_col == lax.broadcasted_iota(jnp.int32, (cuts, parts), 1)).astype(F32)
    same = mm_t(mine, mine)
    earlier = lax.broadcasted_iota(jnp.int32, (cuts, cuts), 1) < lax.broadcasted_iota(jnp.int32, (cuts, cuts), 0)
    rank = jnp.sum(jnp.where(earlier, same, 0.0), axis=1, keepdims=True)
    position = peer_col.astype(F32) * cap + rank
    return (position == lax.broadcasted_iota(jnp.int32, (cuts, slots), 1).astype(F32)).astype(F32)


def on_device(
    warm_mag, warm_angle, load_real, load_react, start_real, start_react,
    gen_bus, gen_linear, gen_quad, gen_ramp, gen_cap_real, gen_cap_react,
    branch_from, branch_to, branch_cond, branch_susc, branch_limit, branch_steps,
    cut_near, cut_peer, cut_bus, cut_cond, cut_susc, cut_limit, cut_steps,
):
    periods, scen, buses = warm_mag.shape
    nrow = periods * scen
    cuts = cut_near.shape[0]
    parts = lax.axis_size("net")
    cap = max(2, cuts // parts * 2)
    slots = parts * cap
    gens = gen_bus.shape[0]
    ntm = lax.axis_size("tm")
    horizon = periods * ntm

    def row(v):
        return v.reshape(1, -1)

    wm = warm_mag.reshape(nrow, buses)
    wa = warm_angle.reshape(nrow, buses)
    lr = load_real.reshape(nrow, buses)
    lq = load_react.reshape(nrow, buses)
    sr = start_real.reshape(nrow, gens)
    sq = start_react.reshape(nrow, gens)
    halo = 2 * scen
    lo = lax.ppermute(sr[nrow - halo:], "tm", [(i, i + 1) for i in range(ntm - 1)])
    hi = lax.ppermute(sr[:halo], "tm", [(i + 1, i) for i in range(ntm - 1)])
    window = nrow + 2 * scen
    period_ext = (
        lax.axis_index("tm") * periods - 1 + jnp.arange(window, dtype=jnp.int32) // scen
    ).reshape(window, 1)
    gen_rows = (row(gen_bus), row(gen_linear), row(gen_quad), row(gen_ramp), row(gen_cap_real), row(gen_cap_react))
    br_rows = (row(branch_from), row(branch_to), row(branch_cond), row(branch_susc), row(branch_limit),
               row(branch_steps.astype(F32)))
    cut_rows = (row(cut_near), row(cut_cond), row(cut_susc), row(cut_limit), row(cut_steps.astype(F32)))
    cut_bus_row = row(cut_bus.astype(F32))
    nvals0 = 128

    def prep_kernel(peer_hbm, near_hbm, bus_hbm, cond_hbm, susc_hbm, lim_hbm, steps_hbm, wm_hbm, wa_hbm,
                    slot_out, pay_out,
                    peer_ref, near_ref, bus_ref, cond_ref, susc_ref, lim_ref, steps_ref, wm_ref, wa_ref, sems):
        pairs = ((peer_hbm, peer_ref), (near_hbm, near_ref), (bus_hbm, bus_ref), (cond_hbm, cond_ref),
                 (susc_hbm, susc_ref), (lim_hbm, lim_ref), (steps_hbm, steps_ref), (wm_hbm, wm_ref),
                 (wa_hbm, wa_ref))
        copies = [pltpu.make_async_copy(src, dst, sems.at[i]) for i, (src, dst) in enumerate(pairs)]
        for cp in copies:
            cp.start()
        for cp in copies:
            cp.wait()
        peer = peer_ref[...]
        mine_t = (lax.broadcasted_iota(jnp.int32, (parts, cuts), 0) == peer).astype(F32)
        same = mm(mine_t.T, mine_t)
        earlier = lax.broadcasted_iota(jnp.int32, (cuts, cuts), 0) < lax.broadcasted_iota(jnp.int32, (cuts, cuts), 1)
        rank = jnp.sum(jnp.where(earlier, same, 0.0), axis=0, keepdims=True)
        position = peer.astype(F32) * cap + rank
        slot_t = (lax.broadcasted_iota(jnp.int32, (slots, cuts), 0).astype(F32) == position).astype(F32).T
        slot_out[...] = slot_t
        inc_near = onehot(near_ref[...], buses)
        by_slot = mm(inc_near, slot_t)
        prm = rows(bus_ref[...].astype(F32) + 1.0, cond_ref[...], susc_ref[...], lim_ref[...],
                   steps_ref[...].astype(F32), jnp.zeros((3, cuts), F32))
        vals = rows(
            mm(prm, slot_t),
            mm(rows(wm_ref[...], wa_ref[...]), by_slot),
            jnp.zeros((nvals0 - 8 - 2 * nrow, slots), F32),
        )
        pay_out[...] = vals.T

    prep_args = (row(cut_peer), cut_rows[0], row(cut_bus), cut_rows[1], cut_rows[2], cut_rows[3], row(cut_steps),
                 wm, wa)
    slot_t, pay_setup = pl.pallas_call(
        prep_kernel,
        out_shape=(jax.ShapeDtypeStruct((cuts, slots), F32), jax.ShapeDtypeStruct((slots, nvals0), F32)),
        in_specs=[pl.BlockSpec(memory_space=pl.ANY)] * len(prep_args),
        out_specs=(pl.BlockSpec(memory_space=pltpu.VMEM), pl.BlockSpec(memory_space=pltpu.VMEM)),
        scratch_shapes=[pltpu.VMEM(a.shape, a.dtype) for a in prep_args] + [pltpu.SemaphoreType.DMA((len(prep_args),))],
    )(*prep_args)
    recv_setup = lax.all_to_all(pay_setup, "net", 0, 0, tiled=True)

    def mid_kernel(recv_ref, wm_ref, wa_ref, mirror_out, pay_out):
        mirror = recv_ref[...].T
        mirror_out[...] = mirror
        inc_recv = onehot(mirror[0:1].astype(jnp.int32) - 1, buses)
        vals = rows(mm(rows(wm_ref[...], wa_ref[...]), inc_recv), jnp.zeros((nvals0 - 2 * nrow, slots), F32))
        pay_out[...] = vals.T

    mirror_t, pay_0 = vmem_call(
        mid_kernel,
        (jax.ShapeDtypeStruct((nvals0, slots), F32), jax.ShapeDtypeStruct((slots, nvals0), F32)),
        recv_setup, wm, wa,
    )
    recv_0 = lax.all_to_all(pay_0, "net", 0, 0, tiled=True)

    def local_part(first, refs):
        if first:
            (wm_ref, wa_ref, bf_ref, bt_ref, bc_ref, bs_ref, bl_ref, bn_ref,
             gb_ref, gl_ref, gq_ref, gr_ref, gcr_ref, gcq_ref, pe_ref,
             sr_lo_ref, sr_ref, sr_hi_ref, sq_ref,
             tot_out, sup_out, ci_out, g0_out, gq0_out) = refs
            zero_b = jnp.zeros((nrow, buses), F32)
            state = (wm_ref[...], wa_ref[...], zero_b, zero_b)
            carry_in = None
        else:
            (st_ref, bf_ref, bt_ref, bc_ref, bs_ref, bl_ref, bn_ref,
             gb_ref, gl_ref, gq_ref, gr_ref, gcr_ref, gcq_ref, pe_ref,
             ci_ref, g0_ref, gq0_ref,
             tot_out, sup_out, gr_out, gq_out) = refs
            state = tuple(st_ref[i] for i in range(4))
            carry_in = load_carry(ci_ref)
        inc_from = onehot(bf_ref[...], buses)
        inc_to = onehot(bt_ref[...], buses)
        inc_gen = onehot(gb_ref[...], buses)
        stack = rows(*state)
        pick_from = split4(mm(stack, inc_from), nrow)
        pick_to = split4(mm(stack, inc_to), nrow)
        prm_in = (bc_ref[...], bs_ref[...], bl_ref[...], bn_ref[...])
        carry_i, fi, ti = advance(carry_in, pick_from, pick_to, prm_in)
        totals = mm_t(fi, inc_from) + mm_t(ti, inc_to)
        for i in range(4):
            tot_out[i] = totals[i * nrow:(i + 1) * nrow]
        lin, quad, ramp, capr, capq = gl_ref[...], gq_ref[...], gr_ref[...], gcr_ref[...], gcq_ref[...]
        per = pe_ref[...]
        nb = (per > 0).astype(F32) + (per < horizon - 1).astype(F32)
        denom = 2.0 * quad + 1.0 + ramp * nb
        if first:
            ext = rows(sr_lo_ref[...], sr_ref[...], sr_hi_ref[...])
            g0 = jnp.clip((ext[scen:scen + window] - lin + ramp * (ext[0:window] + ext[2 * scen:2 * scen + window]))
                          / denom, 0.0, capr)
            g0 = jnp.where((per >= 0) & (per < horizon), g0, 0.0)
            gen_real = g0[scen:scen + nrow]
            gen_react = jnp.clip(sq_ref[...], -capq, capq)
            supply = mm_t(rows(gen_real, gen_react), inc_gen)
            store_carry(ci_out, carry_i)
            g0_out[...] = g0
            gq0_out[...] = gen_react
        else:
            g0 = g0_ref[...]
            gp = mm(rows(state[2], state[3]), inc_gen)
            gp_r, gp_q = gp[0:nrow], gp[nrow:]
            gen_real = jnp.clip(
                (g0[scen:scen + nrow] - 2.0 * gp_r - lin + ramp * (g0[0:nrow] + g0[2 * scen:2 * scen + nrow]))
                / denom[scen:scen + nrow],
                0.0,
                capr,
            )
            gen_react = jnp.clip(gq0_ref[...] - 2.0 * gp_q, -capq, capq)
            supply = mm_t(rows(gen_real + gp_r, gen_react + gp_q), inc_gen)
            gr_out[...] = gen_real
            gq_out[...] = gen_react
        sup_out[0] = supply[0:nrow]
        sup_out[1] = supply[nrow:]

    def mirror0_kernel(mirror_ref, wm_ref, wa_ref, bf_ref, bt_ref, cn_ref, gb_ref, tot_out, cm_out, dg_out):
        mirror = mirror_ref[...]
        inc_recv = onehot(mirror[0:1].astype(jnp.int32) - 1, buses)
        degree = (col_sum(onehot(bf_ref[...], buses)) + col_sum(onehot(bt_ref[...], buses))
                  + col_sum(onehot(cn_ref[...], buses)) + col_sum(inc_recv))
        dg_out[...] = rows(degree, col_sum(onehot(gb_ref[...], buses)), jnp.zeros((6, buses), F32))
        zm = jnp.zeros((nrow, slots), F32)
        zero_b = jnp.zeros((nrow, buses), F32)
        stack = rows(wm_ref[...], wa_ref[...], zero_b, zero_b)
        pick_recv = split4(mm(stack, inc_recv), nrow)
        near_mirror = (mirror[8:8 + nrow], mirror[8 + nrow:8 + 2 * nrow], zm, zm)
        prm_mir = (mirror[1:2], mirror[2:3], mirror[3:4], mirror[4:5])
        carry_m, _, tmr = advance(None, near_mirror, pick_recv, prm_mir)
        totals = mm_t(tmr, inc_recv)
        for i in range(4):
            tot_out[i] = totals[i * nrow:(i + 1) * nrow]
        store_carry(cm_out, carry_m)

    def cut_part(first, refs):
        (st_ref, wm_ref, wa_ref, lr_ref, lq_ref, recv_ref, mirror_ref, slot_ref,
         dg_ref, cn_ref, cc_ref, cs_ref, cl_ref, cstep_ref,
         tin_ref, sup_ref, tm_ref) = refs[:17]
        rest = refs[17:]
        wmv, wav = wm_ref[...], wa_ref[...]
        slot_t = slot_ref[...]
        mirror = mirror_ref[...]
        inc_near = onehot(cn_ref[...], buses)
        inc_recv = onehot(mirror[0:1].astype(jnp.int32) - 1, buses)
        degree = dg_ref[0:1]
        gen_count = dg_ref[1:2]
        prm_cut = (cc_ref[...], cs_ref[...], cl_ref[...], cstep_ref[...])
        if first:
            (cc_out, st_out, pay_out) = rest
            zero_b = jnp.zeros((nrow, buses), F32)
            state = (wmv, wav, zero_b, zero_b)
            far_slot = recv_ref[...].T
            zc = jnp.zeros((nrow, cuts), F32)
            far_c = mm_t(rows(far_slot[0:nrow], far_slot[nrow:2 * nrow]), slot_t)
            far_cross = (far_c[0:nrow], far_c[nrow:], zc, zc)
            stack = rows(*state)
            pick_near = split4(mm(stack, inc_near), nrow)
            carry_c, fc, _ = advance(None, pick_near, far_cross, prm_cut)
            totals = tin_ref[...] + tm_ref[...] + mm_t(fc, inc_near).reshape(4, nrow, buses)
        else:
            (cc_in_ref, cm_ref, mag_out, ang_out, pr_out) = rest
            state = tuple(st_ref[i] for i in range(4))
            both = recv_ref[...].T
            near_mirror = split4(both[0:4 * nrow], nrow)
            far_cross = split4(mm_t(both[4 * nrow:], slot_t), nrow)
            stack = rows(*state)
            pick_near = split4(mm(stack, inc_near), nrow)
            pick_recv = split4(mm(stack, inc_recv), nrow)
            carry_c_in = load_carry(cc_in_ref)
            carry_m_in = load_carry(cm_ref)
            _, fc, _ = advance(carry_c_in, pick_near, far_cross, prm_cut)
            prm_mir = (mirror[1:2], mirror[2:3], mirror[3:4], mirror[4:5])
            _, _, tmr = advance(carry_m_in, near_mirror, pick_recv, prm_mir)
            totals = tin_ref[...] + (mm_t(fc, inc_near) + mm_t(tmr, inc_recv)).reshape(4, nrow, buses)
        mag = (totals[0] + wmv) / (degree + 1.0)
        ang = (totals[1] + wav) / (degree + 1.0)
        weight = 1.0 + BALANCE_WEIGHT * (gen_count + degree)
        pr = BALANCE_WEIGHT * (sup_ref[0] - totals[2] - lr_ref[...]) / weight
        pq = BALANCE_WEIGHT * (sup_ref[1] - totals[3] - lq_ref[...]) / weight
        if first:
            store_carry(cc_out, carry_c)
            st_out[0] = mag
            st_out[1] = ang
            st_out[2] = pr
            st_out[3] = pq
            new_stack = rows(mag, ang, pr, pq)
            near_slot = mm(inc_near, slot_t)
            pay_out[...] = rows(mm(new_stack, near_slot), mm(new_stack, inc_recv)).T
        else:
            mag_out[...] = mag
            ang_out[...] = ang
            pr_out[...] = pr

    sds = jax.ShapeDtypeStruct
    tot_shape = sds((4, nrow, buses), F32)
    br_all = br_rows
    gen_all = (*gen_rows, period_ext)
    tin0, sup0, ci1, g0, gq0 = vmem_call(
        lambda *refs: local_part(True, refs),
        (tot_shape, sds((2, nrow, buses), F32), sds((10, nrow, buses), F32), sds((window, gens), F32),
         sds((nrow, gens), F32)),
        wm, wa, *br_all, *gen_all, lo, sr, hi, sq,
    )
    tm0, cm1, dg = vmem_call(
        mirror0_kernel, (tot_shape, sds((10, nrow, slots), F32), sds((8, buses), F32)), mirror_t, wm, wa,
        br_rows[0], br_rows[1], cut_rows[0], gen_rows[0],
    )
    cut_in = cut_rows
    cc1, st1, pay_1 = vmem_call(
        lambda *refs: cut_part(True, refs),
        (sds((10, nrow, cuts), F32), tot_shape, sds((slots, 8 * nrow), F32)),
        wm, wm, wa, lr, lq, recv_0, mirror_t, slot_t, dg, *cut_in, tin0, sup0, tm0,
    )
    recv_1 = lax.all_to_all(pay_1, "net", 0, 0, tiled=True)
    tin1, sup1, gr, gq = vmem_call(
        lambda *refs: local_part(False, refs),
        (tot_shape, sds((2, nrow, buses), F32), sds((nrow, gens), F32), sds((nrow, gens), F32)),
        st1, *br_all, *gen_all, ci1, g0, gq0,
    )
    mag, ang, pr = vmem_call(
        lambda *refs: cut_part(False, refs),
        (sds((nrow, buses), F32), sds((nrow, buses), F32), sds((nrow, buses), F32)),
        st1, wm, wa, lr, lq, recv_1, mirror_t, slot_t, dg, *cut_in, tin1, sup1, tin1,
        cc1, cm1,
    )
    shape_b = (periods, scen, buses)
    shape_g = (periods, scen, gens)
    return (mag.reshape(shape_b), ang.reshape(shape_b), pr.reshape(shape_b), gr.reshape(shape_g),
            gq.reshape(shape_g))


def solution(mesh):
    bus = P("tm", None, "net")
    one = P("net")
    return jax.shard_map(
        on_device,
        mesh=mesh,
        in_specs=(bus,) * 6 + (one,) * 12 + (one, P("net", None)) + (one,) * 5,
        out_specs=(bus,) * 5,
        check_vma=False,
    )
```

```python
import jax
import jax.numpy as jnp
from jax import lax
from jax.experimental import pallas as pl
from jax.experimental.pallas import tpu as pltpu
from jax.sharding import PartitionSpec as P

INNER = 4
STEP_SIZE = 0.0005
RADIUS = 0.05
BALANCE_WEIGHT = 2.0
HI = lax.Precision.HIGHEST
F32 = jnp.float32


def mm(a, b):
    return lax.dot_general(a, b, (((1,), (0,)), ((), ())), precision=HI, preferred_element_type=F32)


def mm_t(a, b):
    return lax.dot_general(a, b, (((1,), (1,)), ((), ())), precision=HI, preferred_element_type=F32)


def onehot(ids_row, count):
    n = ids_row.shape[1]
    return (lax.broadcasted_iota(jnp.int32, (count, n), 0) == ids_row).astype(F32)


def col_sum(inc):
    return mm_t(jnp.ones((8, inc.shape[1]), F32), inc)[0:1]


def rows(*parts):
    return jnp.concatenate(parts, axis=0)


def trig(x):
    d = x[1] - x[3]
    return (jnp.cos(d), jnp.sin(d))


def flows(x, cs, g, b):
    mf, _, mt, _ = x
    c, s = cs
    p = mf * mt
    return (
        g * mf * mf - p * (g * c + b * s),
        -b * mf * mf - p * (g * s - b * c),
        g * mt * mt - p * (g * c - b * s),
        -b * mt * mt + p * (g * s + b * c),
    )


def energy_grad(x, cs, f, t, ft, g, b, l2):
    mf, af, mt, at = x
    c, s = cs
    p = mf * mt
    ka = g * c + b * s
    kb = g * s - b * c
    kc = g * c - b * s
    kd = g * s + b * c
    if f is None:
        f = (g * mf * mf - p * ka, -b * mf * mf - p * kb, g * mt * mt - p * kc, -b * mt * mt + p * kd)
    f0, f1, f2, f3 = f
    ef = jnp.maximum(f0 * f0 + f1 * f1 - l2, 0.0)
    et = jnp.maximum(f2 * f2 + f3 * f3 - l2, 0.0)
    w0 = (f0 - ft[0]) + 2.0 * ef * f0
    w1 = (f1 - ft[1]) + 2.0 * ef * f1
    w2 = (f2 - ft[2]) + 2.0 * et * f2
    w3 = (f3 - ft[3]) + 2.0 * et * f3
    g_mf = (mf - t[0]) + w0 * (2.0 * g * mf - mt * ka) - w1 * (2.0 * b * mf + mt * kb) - w2 * mt * kc + w3 * mt * kd
    g_mt = (mt - t[2]) - w0 * mf * ka - w1 * mf * kb + w2 * (2.0 * g * mt - mf * kc) - w3 * (2.0 * b * mt - mf * kd)
    g_d = p * (w0 * kb - w1 * ka + w2 * kd + w3 * kc)
    return (g_mf, (af - t[1]) + g_d, g_mt, (at - t[3]) - g_d)


def solve(x, cs, f, t, ft, g, b, l2, steps):
    for attempt in range(INNER):
        if cs is None:
            cs = trig(x)
        grad = energy_grad(x, cs, f, t, ft, g, b, l2)
        x = tuple(
            jnp.where(attempt < steps, xi - jnp.clip(STEP_SIZE * gi, -RADIUS, RADIUS), xi)
            for xi, gi in zip(x, grad)
        )
        cs, f = None, None
    return x


def advance(carry, near, far, prm):
    g, b, lim, steps = prm
    ends = (near[0], near[1], far[0], far[1])
    prices = (near[2], near[3], far[2], far[3])
    if carry is None:
        copies = ends
        cs = trig(copies)
        flow_prev = flows(copies, cs, g, b)
        volt = tuple(jnp.zeros_like(e) for e in ends)
        target = ends
        flow_target = flow_prev
        dual_flow = volt
    else:
        copies, flow_prev, cs = carry
        volt = tuple(c - e for c, e in zip(copies, ends))
        target = tuple(e - v for e, v in zip(ends, volt))
        flow_target = tuple(f + 2.0 * q for f, q in zip(flow_prev, prices))
        dual_flow = tuple(-q for q in prices)
    copies = solve(copies, cs, flow_prev, target, flow_target, g, b, lim * lim, steps)
    cs = trig(copies)
    flow_prev = flows(copies, cs, g, b)
    side_from = rows(
        copies[0] + volt[0], copies[1] + volt[1], flow_prev[0] + dual_flow[0], flow_prev[1] + dual_flow[1]
    )
    side_to = rows(
        copies[2] + volt[2], copies[3] + volt[3], flow_prev[2] + dual_flow[2], flow_prev[3] + dual_flow[3]
    )
    return (copies, flow_prev, cs), side_from, side_to


def store_carry(ref, carry):
    for i in range(4):
        ref[i] = carry[0][i]
        ref[4 + i] = carry[1][i]
    ref[8] = carry[2][0]
    ref[9] = carry[2][1]


def load_carry(ref):
    return (tuple(ref[i] for i in range(4)), tuple(ref[4 + i] for i in range(4)), (ref[8], ref[9]))


def split4(a, n):
    return tuple(a[i * n:(i + 1) * n] for i in range(4))


def vmem_call(kernel, outs, *args):
    return pl.pallas_call(
        kernel,
        out_shape=outs,
        in_specs=[pl.BlockSpec(memory_space=pltpu.VMEM)] * len(args),
        out_specs=tuple(pl.BlockSpec(memory_space=pltpu.VMEM) for _ in outs),
        compiler_params=pltpu.CompilerParams(vmem_limit_bytes=48 * 1024 * 1024),
    )(*args)


def slot_table(peer_col, cap, slots):
    cuts = peer_col.shape[0]
    parts = slots // cap
    mine = (peer_col == lax.broadcasted_iota(jnp.int32, (cuts, parts), 1)).astype(F32)
    same = mm_t(mine, mine)
    earlier = lax.broadcasted_iota(jnp.int32, (cuts, cuts), 1) < lax.broadcasted_iota(jnp.int32, (cuts, cuts), 0)
    rank = jnp.sum(jnp.where(earlier, same, 0.0), axis=1, keepdims=True)
    position = peer_col.astype(F32) * cap + rank
    return (position == lax.broadcasted_iota(jnp.int32, (cuts, slots), 1).astype(F32)).astype(F32)


def on_device(
    warm_mag, warm_angle, load_real, load_react, start_real, start_react,
    gen_bus, gen_linear, gen_quad, gen_ramp, gen_cap_real, gen_cap_react,
    branch_from, branch_to, branch_cond, branch_susc, branch_limit, branch_steps,
    cut_near, cut_peer, cut_bus, cut_cond, cut_susc, cut_limit, cut_steps,
):
    periods, scen, buses = warm_mag.shape
    nrow = periods * scen
    cuts = cut_near.shape[0]
    parts = lax.axis_size("net")
    cap = max(2, cuts // parts * 2)
    slots = parts * cap
    gens = gen_bus.shape[0]
    ntm = lax.axis_size("tm")
    horizon = periods * ntm

    def row(v):
        return v.reshape(1, -1)

    wm = warm_mag.reshape(nrow, buses)
    wa = warm_angle.reshape(nrow, buses)
    lr = load_real.reshape(nrow, buses)
    lq = load_react.reshape(nrow, buses)
    sr = start_real.reshape(nrow, gens)
    sq = start_react.reshape(nrow, gens)
    halo = 2 * scen
    lo = lax.ppermute(sr[nrow - halo:], "tm", [(i, i + 1) for i in range(ntm - 1)])
    hi = lax.ppermute(sr[:halo], "tm", [(i + 1, i) for i in range(ntm - 1)])
    window = nrow + 2 * scen
    period_ext = (
        lax.axis_index("tm") * periods - 1 + jnp.arange(window, dtype=jnp.int32) // scen
    ).reshape(window, 1)
    gen_rows = (row(gen_bus), row(gen_linear), row(gen_quad), row(gen_ramp), row(gen_cap_real), row(gen_cap_react))
    br_rows = (row(branch_from), row(branch_to), row(branch_cond), row(branch_susc), row(branch_limit),
               row(branch_steps.astype(F32)))
    cut_rows = (row(cut_near), row(cut_cond), row(cut_susc), row(cut_limit), row(cut_steps.astype(F32)))
    cut_bus_row = row(cut_bus.astype(F32))
    nvals0 = 128

    def prep_kernel(peer_hbm, near_hbm, bus_hbm, cond_hbm, susc_hbm, lim_hbm, steps_hbm, wm_hbm, wa_hbm,
                    slot_out, pay_out,
                    peer_ref, near_ref, bus_ref, cond_ref, susc_ref, lim_ref, steps_ref, wm_ref, wa_ref, sems):
        pairs = ((peer_hbm, peer_ref), (near_hbm, near_ref), (bus_hbm, bus_ref), (cond_hbm, cond_ref),
                 (susc_hbm, susc_ref), (lim_hbm, lim_ref), (steps_hbm, steps_ref), (wm_hbm, wm_ref),
                 (wa_hbm, wa_ref))
        copies = [pltpu.make_async_copy(src, dst, sems.at[i]) for i, (src, dst) in enumerate(pairs)]
        for cp in copies:
            cp.start()
        for cp in copies:
            cp.wait()
        peer = peer_ref[...]
        mine_t = (lax.broadcasted_iota(jnp.int32, (parts, cuts), 0) == peer).astype(F32)
        same = mm(mine_t.T, mine_t)
        earlier = lax.broadcasted_iota(jnp.int32, (cuts, cuts), 0) < lax.broadcasted_iota(jnp.int32, (cuts, cuts), 1)
        rank = jnp.sum(jnp.where(earlier, same, 0.0), axis=0, keepdims=True)
        position = peer.astype(F32) * cap + rank
        slot_t = (lax.broadcasted_iota(jnp.int32, (slots, cuts), 0).astype(F32) == position).astype(F32).T
        slot_out[...] = slot_t
        inc_near = onehot(near_ref[...], buses)
        by_slot = mm(inc_near, slot_t)
        prm = rows(bus_ref[...].astype(F32) + 1.0, cond_ref[...], susc_ref[...], lim_ref[...],
                   steps_ref[...].astype(F32), jnp.zeros((3, cuts), F32))
        vals = rows(
            mm(prm, slot_t),
            mm(rows(wm_ref[...], wa_ref[...]), by_slot),
            jnp.zeros((nvals0 - 8 - 2 * nrow, slots), F32),
        )
        pay_out[...] = vals.T

    prep_args = (row(cut_peer), cut_rows[0], row(cut_bus), cut_rows[1], cut_rows[2], cut_rows[3], row(cut_steps),
                 wm, wa)
    slot_t, pay_setup = pl.pallas_call(
        prep_kernel,
        out_shape=(jax.ShapeDtypeStruct((cuts, slots), F32), jax.ShapeDtypeStruct((slots, nvals0), F32)),
        in_specs=[pl.BlockSpec(memory_space=pl.ANY)] * len(prep_args),
        out_specs=(pl.BlockSpec(memory_space=pltpu.VMEM), pl.BlockSpec(memory_space=pltpu.VMEM)),
        scratch_shapes=[pltpu.VMEM(a.shape, a.dtype) for a in prep_args] + [pltpu.SemaphoreType.DMA((len(prep_args),))],
    )(*prep_args)
    recv_setup = lax.all_to_all(pay_setup, "net", 0, 0, tiled=True)

    def mid_kernel(recv_ref, wm_ref, wa_ref, mirror_out, pay_out):
        mirror = recv_ref[...].T
        mirror_out[...] = mirror
        inc_recv = onehot(mirror[0:1].astype(jnp.int32) - 1, buses)
        vals = rows(mm(rows(wm_ref[...], wa_ref[...]), inc_recv), jnp.zeros((nvals0 - 2 * nrow, slots), F32))
        pay_out[...] = vals.T

    mirror_t, pay_0 = vmem_call(
        mid_kernel,
        (jax.ShapeDtypeStruct((nvals0, slots), F32), jax.ShapeDtypeStruct((slots, nvals0), F32)),
        recv_setup, wm, wa,
    )
    recv_0 = lax.all_to_all(pay_0, "net", 0, 0, tiled=True)

    def spread(p):
        return (lax.broadcasted_iota(jnp.int32, (3 * slots, slots), 0)
                == 3 * lax.broadcasted_iota(jnp.int32, (3 * slots, slots), 1) + p).astype(F32)

    def local_part(first, refs):
        if first:
            (wm_ref, wa_ref, bf_ref, bt_ref, bc_ref, bs_ref, bl_ref, bn_ref,
             gb_ref, gl_ref, gq_ref, gr_ref, gcr_ref, gcq_ref, pe_ref,
             sr_lo_ref, sr_ref, sr_hi_ref, sq_ref,
             tot_out, sup_out, ci_out, g0_out, gq0_out) = refs
            zero_b = jnp.zeros((nrow, buses), F32)
            state = (wm_ref[...], wa_ref[...], zero_b, zero_b)
            carry_in = None
        else:
            (st_ref, bf_ref, bt_ref, bc_ref, bs_ref, bl_ref, bn_ref,
             gb_ref, gl_ref, gq_ref, gr_ref, gcr_ref, gcq_ref, pe_ref,
             ci_ref, g0_ref, gq0_ref,
             tot_out, sup_out, gr_out, gq_out) = refs
            state = tuple(st_ref[i] for i in range(4))
            carry_in = load_carry(ci_ref)
        inc_from = onehot(bf_ref[...], buses)
        inc_to = onehot(bt_ref[...], buses)
        inc_gen = onehot(gb_ref[...], buses)
        stack = rows(*state)
        pick_from = split4(mm(stack, inc_from), nrow)
        pick_to = split4(mm(stack, inc_to), nrow)
        prm_in = (bc_ref[...], bs_ref[...], bl_ref[...], bn_ref[...])
        carry_i, fi, ti = advance(carry_in, pick_from, pick_to, prm_in)
        totals = mm_t(fi, inc_from) + mm_t(ti, inc_to)
        for i in range(4):
            tot_out[i] = totals[i * nrow:(i + 1) * nrow]
        lin, quad, ramp, capr, capq = gl_ref[...], gq_ref[...], gr_ref[...], gcr_ref[...], gcq_ref[...]
        per = pe_ref[...]
        nb = (per > 0).astype(F32) + (per < horizon - 1).astype(F32)
        denom = 2.0 * quad + 1.0 + ramp * nb
        if first:
            ext = rows(sr_lo_ref[...], sr_ref[...], sr_hi_ref[...])
            g0 = jnp.clip((ext[scen:scen + window] - lin + ramp * (ext[0:window] + ext[2 * scen:2 * scen + window]))
                          / denom, 0.0, capr)
            g0 = jnp.where((per >= 0) & (per < horizon), g0, 0.0)
            gen_real = g0[scen:scen + nrow]
            gen_react = jnp.clip(sq_ref[...], -capq, capq)
            supply = mm_t(rows(gen_real, gen_react), inc_gen)
            store_carry(ci_out, carry_i)
            g0_out[...] = g0
            gq0_out[...] = gen_react
        else:
            g0 = g0_ref[...]
            gp = mm(rows(state[2], state[3]), inc_gen)
            gp_r, gp_q = gp[0:nrow], gp[nrow:]
            gen_real = jnp.clip(
                (g0[scen:scen + nrow] - 2.0 * gp_r - lin + ramp * (g0[0:nrow] + g0[2 * scen:2 * scen + nrow]))
                / denom[scen:scen + nrow],
                0.0,
                capr,
            )
            gen_react = jnp.clip(gq0_ref[...] - 2.0 * gp_q, -capq, capq)
            supply = mm_t(rows(gen_real + gp_r, gen_react + gp_q), inc_gen)
            gr_out[...] = gen_real
            gq_out[...] = gen_react
        sup_out[0] = supply[0:nrow]
        sup_out[1] = supply[nrow:]

    def mirror0_kernel(mirror_ref, wm_ref, wa_ref, bf_ref, bt_ref, cn_ref, gb_ref, tot_out, cm_out, dg_out):
        mirror = mirror_ref[...]
        inc_recv = onehot(mirror[0:1].astype(jnp.int32) - 1, buses)
        degree = (col_sum(onehot(bf_ref[...], buses)) + col_sum(onehot(bt_ref[...], buses))
                  + col_sum(onehot(cn_ref[...], buses)) + col_sum(inc_recv))
        dg_out[...] = rows(degree, col_sum(onehot(gb_ref[...], buses)), jnp.zeros((6, buses), F32))
        zm = jnp.zeros((nrow, slots), F32)
        zero_b = jnp.zeros((nrow, buses), F32)
        stack = rows(wm_ref[...], wa_ref[...], zero_b, zero_b)
        pick_recv = split4(mm(stack, inc_recv), nrow)
        near_mirror = (mirror[8:8 + nrow], mirror[8 + nrow:8 + 2 * nrow], zm, zm)
        prm_mir = (mirror[1:2], mirror[2:3], mirror[3:4], mirror[4:5])
        carry_m, _, tmr = advance(None, near_mirror, pick_recv, prm_mir)
        totals = mm_t(tmr, inc_recv)
        for i in range(4):
            tot_out[i] = totals[i * nrow:(i + 1) * nrow]
        store_carry(cm_out, carry_m)

    def cut_part(first, refs):
        (st_ref, wm_ref, wa_ref, lr_ref, lq_ref, recv_ref, mirror_ref, slot_ref,
         dg_ref, cp_ref, tin_ref, sup_ref, tm_ref) = refs[:13]
        rest = refs[13:]
        cprm_v = cp_ref[...]
        wmv, wav = wm_ref[...], wa_ref[...]
        slot_t = slot_ref[...]
        mirror = mirror_ref[...]
        inc_near = onehot(cprm_v[0:1].astype(jnp.int32), buses)
        inc_recv = onehot(mirror[0:1].astype(jnp.int32) - 1, buses)
        degree = dg_ref[0:1]
        gen_count = dg_ref[1:2]
        prm_cut = (cprm_v[1:2], cprm_v[2:3], cprm_v[3:4], cprm_v[4:5])
        if first:
            (cc_out, st_out, pay_out) = rest
            zero_b = jnp.zeros((nrow, buses), F32)
            state = (wmv, wav, zero_b, zero_b)
            far_slot = recv_ref[...].T
            zc = jnp.zeros((nrow, cuts), F32)
            far_c = mm_t(rows(far_slot[0:nrow], far_slot[nrow:2 * nrow]), slot_t)
            far_cross = (far_c[0:nrow], far_c[nrow:], zc, zc)
            stack = rows(*state)
            pick_near = split4(mm(stack, inc_near), nrow)
            carry_c, fc, _ = advance(None, pick_near, far_cross, prm_cut)
            totals = tin_ref[...] + tm_ref[...] + mm_t(fc, inc_near).reshape(4, nrow, buses)
        else:
            (cc_in_ref, cm_ref, mag_out, ang_out, pr_out) = rest
            state = tuple(st_ref[i] for i in range(4))
            got = recv_ref[...]
            both = rows(*(mm(spread(p).T, got).T for p in range(3)))
            near_mirror = split4(both[0:4 * nrow], nrow)
            far_cross = split4(mm_t(both[4 * nrow:], slot_t), nrow)
            stack = rows(*state)
            pick_near = split4(mm(stack, inc_near), nrow)
            pick_recv = split4(mm(stack, inc_recv), nrow)
            carry_c_in = load_carry(cc_in_ref)
            carry_m_in = load_carry(cm_ref)
            _, fc, _ = advance(carry_c_in, pick_near, far_cross, prm_cut)
            prm_mir = (mirror[1:2], mirror[2:3], mirror[3:4], mirror[4:5])
            _, _, tmr = advance(carry_m_in, near_mirror, pick_recv, prm_mir)
            totals = tin_ref[...] + (mm_t(fc, inc_near) + mm_t(tmr, inc_recv)).reshape(4, nrow, buses)
        mag = (totals[0] + wmv) / (degree + 1.0)
        ang = (totals[1] + wav) / (degree + 1.0)
        weight = 1.0 + BALANCE_WEIGHT * (gen_count + degree)
        pr = BALANCE_WEIGHT * (sup_ref[0] - totals[2] - lr_ref[...]) / weight
        pq = BALANCE_WEIGHT * (sup_ref[1] - totals[3] - lq_ref[...]) / weight
        if first:
            store_carry(cc_out, carry_c)
            st_out[0] = mag
            st_out[1] = ang
            st_out[2] = pr
            st_out[3] = pq
            new_stack = rows(mag, ang, pr, pq)
            near_slot = mm(inc_near, slot_t)
            vals = rows(mm(new_stack, near_slot), mm(new_stack, inc_recv))
            pay_out[...] = sum(mm_t(spread(p), vals[p * 128:(p + 1) * 128]) for p in range(3))
        else:
            mag_out[...] = mag
            ang_out[...] = ang
            pr_out[...] = pr

    sds = jax.ShapeDtypeStruct
    tot_shape = sds((4, nrow, buses), F32)
    br_all = br_rows
    gen_all = (*gen_rows, period_ext)
    tin0, sup0, ci1, g0, gq0 = vmem_call(
        lambda *refs: local_part(True, refs),
        (tot_shape, sds((2, nrow, buses), F32), sds((10, nrow, buses), F32), sds((window, gens), F32),
         sds((nrow, gens), F32)),
        wm, wa, *br_all, *gen_all, lo, sr, hi, sq,
    )
    tm0, cm1, dg = vmem_call(
        mirror0_kernel, (tot_shape, sds((10, nrow, slots), F32), sds((8, buses), F32)), mirror_t, wm, wa,
        br_rows[0], br_rows[1], cut_rows[0], gen_rows[0],
    )
    cprm = jnp.concatenate([cut_rows[0].astype(F32), *cut_rows[1:], jnp.zeros((3, cuts), F32)], axis=0)
    cc1, st1, pay_1 = vmem_call(
        lambda *refs: cut_part(True, refs),
        (sds((10, nrow, cuts), F32), tot_shape, sds((3 * slots, 128), F32)),
        wm, wm, wa, lr, lq, recv_0, mirror_t, slot_t, dg, cprm, tin0, sup0, tm0,
    )
    recv_1 = lax.all_to_all(pay_1.reshape(3 * parts, 2, 128), "net", 0, 0, tiled=True).reshape(3 * slots, 128)
    tin1, sup1, gr, gq = vmem_call(
        lambda *refs: local_part(False, refs),
        (tot_shape, sds((2, nrow, buses), F32), sds((nrow, gens), F32), sds((nrow, gens), F32)),
        st1, *br_all, *gen_all, ci1, g0, gq0,
    )
    mag, ang, pr = vmem_call(
        lambda *refs: cut_part(False, refs),
        (sds((nrow, buses), F32), sds((nrow, buses), F32), sds((nrow, buses), F32)),
        st1, wm, wa, lr, lq, recv_1, mirror_t, slot_t, dg, cprm, tin1, sup1, tin1,
        cc1, cm1,
    )
    shape_b = (periods, scen, buses)
    shape_g = (periods, scen, gens)
    return (mag.reshape(shape_b), ang.reshape(shape_b), pr.reshape(shape_b), gr.reshape(shape_g),
            gq.reshape(shape_g))


def solution(mesh):
    bus = P("tm", None, "net")
    one = P("net")
    return jax.shard_map(
        on_device,
        mesh=mesh,
        in_specs=(bus,) * 6 + (one,) * 12 + (one, P("net", None)) + (one,) * 5,
        out_specs=(bus,) * 5,
        check_vma=False,
    )
```

```python
import jax
import jax.numpy as jnp
from jax import lax
from jax.experimental import pallas as pl
from jax.experimental.pallas import tpu as pltpu
from jax.sharding import PartitionSpec as P

INNER = 4
STEP_SIZE = 0.0005
RADIUS = 0.05
BALANCE_WEIGHT = 2.0
HI = lax.Precision.HIGHEST
F32 = jnp.float32


NN = (((1,), (0,)), ((), ()))
NT = (((1,), (1,)), ((), ()))
BF = jnp.bfloat16


def split3(x):
    hi = x.astype(BF)
    r = x - hi.astype(F32)
    mid = r.astype(BF)
    lo = (r - mid.astype(F32)).astype(BF)
    return hi, mid, lo


def dot(a, b, dims):
    return lax.dot_general(a, b, dims, preferred_element_type=F32)


def take(vals, oh):
    hi, mid, lo = split3(vals)
    return (dot(hi, oh, NN) + dot(mid, oh, NN)) + dot(lo, oh, NN)


def give(vals, oh):
    hi, mid, lo = split3(vals)
    return (dot(hi, oh, NT) + dot(mid, oh, NT)) + dot(lo, oh, NT)


def take_left(oh, vals):
    hi, mid, lo = split3(vals)
    return (dot(oh, hi, NN) + dot(oh, mid, NN)) + dot(oh, lo, NN)


def give_left(oh, vals):
    hi, mid, lo = split3(vals)
    return (dot(oh, hi, NT) + dot(oh, mid, NT)) + dot(oh, lo, NT)


def onehot(ids_row, count):
    n = ids_row.shape[1]
    return (lax.broadcasted_iota(jnp.int32, (count, n), 0) == ids_row).astype(BF)


def col_sum(inc):
    return dot(jnp.ones((8, inc.shape[1]), BF), inc, NT)[0:1]


def rows(*parts):
    return jnp.concatenate(parts, axis=0)


def trig(x):
    d = x[1] - x[3]
    return (jnp.cos(d), jnp.sin(d))


def flows(x, cs, g, b):
    mf, _, mt, _ = x
    c, s = cs
    p = mf * mt
    return (
        g * mf * mf - p * (g * c + b * s),
        -b * mf * mf - p * (g * s - b * c),
        g * mt * mt - p * (g * c - b * s),
        -b * mt * mt + p * (g * s + b * c),
    )


def energy_grad(x, cs, f, t, ft, g, b, l2):
    mf, af, mt, at = x
    c, s = cs
    p = mf * mt
    ka = g * c + b * s
    kb = g * s - b * c
    kc = g * c - b * s
    kd = g * s + b * c
    if f is None:
        f = (g * mf * mf - p * ka, -b * mf * mf - p * kb, g * mt * mt - p * kc, -b * mt * mt + p * kd)
    f0, f1, f2, f3 = f
    ef = jnp.maximum(f0 * f0 + f1 * f1 - l2, 0.0)
    et = jnp.maximum(f2 * f2 + f3 * f3 - l2, 0.0)
    w0 = (f0 - ft[0]) + 2.0 * ef * f0
    w1 = (f1 - ft[1]) + 2.0 * ef * f1
    w2 = (f2 - ft[2]) + 2.0 * et * f2
    w3 = (f3 - ft[3]) + 2.0 * et * f3
    g_mf = (mf - t[0]) + w0 * (2.0 * g * mf - mt * ka) - w1 * (2.0 * b * mf + mt * kb) - w2 * mt * kc + w3 * mt * kd
    g_mt = (mt - t[2]) - w0 * mf * ka - w1 * mf * kb + w2 * (2.0 * g * mt - mf * kc) - w3 * (2.0 * b * mt - mf * kd)
    g_d = p * (w0 * kb - w1 * ka + w2 * kd + w3 * kc)
    return (g_mf, (af - t[1]) + g_d, g_mt, (at - t[3]) - g_d)


def solve(x, cs, f, t, ft, g, b, l2, steps):
    for attempt in range(INNER):
        if cs is None:
            cs = trig(x)
        grad = energy_grad(x, cs, f, t, ft, g, b, l2)
        x = tuple(
            jnp.where(attempt < steps, xi - jnp.clip(STEP_SIZE * gi, -RADIUS, RADIUS), xi)
            for xi, gi in zip(x, grad)
        )
        cs, f = None, None
    return x


def advance(carry, near, far, prm):
    g, b, lim, steps = prm
    ends = (near[0], near[1], far[0], far[1])
    prices = (near[2], near[3], far[2], far[3])
    if carry is None:
        copies = ends
        cs = trig(copies)
        flow_prev = flows(copies, cs, g, b)
        volt = tuple(jnp.zeros_like(e) for e in ends)
        target = ends
        flow_target = flow_prev
        dual_flow = volt
    else:
        copies, flow_prev, cs = carry
        volt = tuple(c - e for c, e in zip(copies, ends))
        target = tuple(e - v for e, v in zip(ends, volt))
        flow_target = tuple(f + 2.0 * q for f, q in zip(flow_prev, prices))
        dual_flow = tuple(-q for q in prices)
    copies = solve(copies, cs, flow_prev, target, flow_target, g, b, lim * lim, steps)
    cs = trig(copies)
    flow_prev = flows(copies, cs, g, b)
    side_from = rows(
        copies[0] + volt[0], copies[1] + volt[1], flow_prev[0] + dual_flow[0], flow_prev[1] + dual_flow[1]
    )
    side_to = rows(
        copies[2] + volt[2], copies[3] + volt[3], flow_prev[2] + dual_flow[2], flow_prev[3] + dual_flow[3]
    )
    return (copies, flow_prev, cs), side_from, side_to


def store_carry(ref, carry):
    for i in range(4):
        ref[i] = carry[0][i]
        ref[4 + i] = carry[1][i]
    ref[8] = carry[2][0]
    ref[9] = carry[2][1]


def load_carry(ref):
    return (tuple(ref[i] for i in range(4)), tuple(ref[4 + i] for i in range(4)), (ref[8], ref[9]))


def split4(a, n):
    return tuple(a[i * n:(i + 1) * n] for i in range(4))


def vmem_call(kernel, outs, *args):
    return pl.pallas_call(
        kernel,
        out_shape=outs,
        in_specs=[pl.BlockSpec(memory_space=pltpu.VMEM)] * len(args),
        out_specs=tuple(pl.BlockSpec(memory_space=pltpu.VMEM) for _ in outs),
        compiler_params=pltpu.CompilerParams(vmem_limit_bytes=48 * 1024 * 1024),
    )(*args)


def on_device(
    warm_mag, warm_angle, load_real, load_react, start_real, start_react,
    gen_bus, gen_linear, gen_quad, gen_ramp, gen_cap_real, gen_cap_react,
    branch_from, branch_to, branch_cond, branch_susc, branch_limit, branch_steps,
    cut_near, cut_peer, cut_bus, cut_cond, cut_susc, cut_limit, cut_steps,
):
    periods, scen, buses = warm_mag.shape
    nrow = periods * scen
    cuts = cut_near.shape[0]
    parts = lax.axis_size("net")
    cap = max(2, cuts // parts * 2)
    slots = parts * cap
    gens = gen_bus.shape[0]
    ntm = lax.axis_size("tm")
    horizon = periods * ntm

    def row(v):
        return v.reshape(1, -1)

    wm = warm_mag.reshape(nrow, buses)
    wa = warm_angle.reshape(nrow, buses)
    lr = load_real.reshape(nrow, buses)
    lq = load_react.reshape(nrow, buses)
    sr = start_real.reshape(nrow, gens)
    sq = start_react.reshape(nrow, gens)
    halo = 2 * scen
    lo = lax.ppermute(sr[nrow - halo:], "tm", [(i, i + 1) for i in range(ntm - 1)])
    hi = lax.ppermute(sr[:halo], "tm", [(i + 1, i) for i in range(ntm - 1)])
    window = nrow + 2 * scen
    period_ext = (
        lax.axis_index("tm") * periods - 1 + jnp.arange(window, dtype=jnp.int32) // scen
    ).reshape(window, 1)
    gen_rows = (row(gen_bus), row(gen_linear), row(gen_quad), row(gen_ramp), row(gen_cap_real), row(gen_cap_react))
    br_rows = (row(branch_from), row(branch_to), row(branch_cond), row(branch_susc), row(branch_limit),
               row(branch_steps.astype(F32)))
    cut_rows = (row(cut_near), row(cut_cond), row(cut_susc), row(cut_limit), row(cut_steps.astype(F32)))
    cut_bus_row = row(cut_bus.astype(F32))
    nvals0 = 128

    def prep_kernel(peer_hbm, near_hbm, bus_hbm, cond_hbm, susc_hbm, lim_hbm, steps_hbm, wm_hbm, wa_hbm,
                    slot_out, pay_out,
                    peer_ref, near_ref, bus_ref, cond_ref, susc_ref, lim_ref, steps_ref, wm_ref, wa_ref, sems):
        pairs = ((peer_hbm, peer_ref), (near_hbm, near_ref), (bus_hbm, bus_ref), (cond_hbm, cond_ref),
                 (susc_hbm, susc_ref), (lim_hbm, lim_ref), (steps_hbm, steps_ref), (wm_hbm, wm_ref),
                 (wa_hbm, wa_ref))
        copies = [pltpu.make_async_copy(src, dst, sems.at[i]) for i, (src, dst) in enumerate(pairs)]
        for cp in copies:
            cp.start()
        for cp in copies:
            cp.wait()
        peer = peer_ref[...]
        mine_t = (lax.broadcasted_iota(jnp.int32, (parts, cuts), 0) == peer).astype(F32)
        same = dot(mine_t.T.astype(BF), mine_t.astype(BF), NN)
        earlier = lax.broadcasted_iota(jnp.int32, (cuts, cuts), 0) < lax.broadcasted_iota(jnp.int32, (cuts, cuts), 1)
        rank = jnp.sum(jnp.where(earlier, same, 0.0), axis=0, keepdims=True)
        position = peer.astype(F32) * cap + rank
        slot_t = (lax.broadcasted_iota(jnp.int32, (slots, cuts), 0).astype(F32) == position).astype(F32).T
        slot_b = slot_t.astype(BF)
        slot_out[...] = slot_t
        inc_near = onehot(near_ref[...], buses)
        by_slot = dot(inc_near, slot_b, NN).astype(BF)
        prm = rows(bus_ref[...].astype(F32) + 1.0, cond_ref[...], susc_ref[...], lim_ref[...],
                   steps_ref[...].astype(F32), jnp.zeros((3, cuts), F32))
        vals = rows(
            take(prm, slot_b),
            take(rows(wm_ref[...], wa_ref[...]), by_slot),
            jnp.zeros((nvals0 - 8 - 2 * nrow, slots), F32),
        )
        pay_out[...] = vals.T

    prep_args = (row(cut_peer), cut_rows[0], row(cut_bus), cut_rows[1], cut_rows[2], cut_rows[3], row(cut_steps),
                 wm, wa)
    slot_t, pay_setup = pl.pallas_call(
        prep_kernel,
        out_shape=(jax.ShapeDtypeStruct((cuts, slots), F32), jax.ShapeDtypeStruct((slots, nvals0), F32)),
        in_specs=[pl.BlockSpec(memory_space=pl.ANY)] * len(prep_args),
        out_specs=(pl.BlockSpec(memory_space=pltpu.VMEM), pl.BlockSpec(memory_space=pltpu.VMEM)),
        scratch_shapes=[pltpu.VMEM(a.shape, a.dtype) for a in prep_args] + [pltpu.SemaphoreType.DMA((len(prep_args),))],
    )(*prep_args)
    recv_setup = lax.all_to_all(pay_setup, "net", 0, 0, tiled=True)

    def mid_kernel(recv_ref, wm_ref, wa_ref, mirror_out, pay_out):
        mirror = recv_ref[...].T
        mirror_out[...] = mirror
        inc_recv = onehot(mirror[0:1].astype(jnp.int32) - 1, buses)
        vals = rows(take(rows(wm_ref[...], wa_ref[...]), inc_recv), jnp.zeros((nvals0 - 2 * nrow, slots), F32))
        pay_out[...] = vals.T

    mirror_t, pay_0 = vmem_call(
        mid_kernel,
        (jax.ShapeDtypeStruct((nvals0, slots), F32), jax.ShapeDtypeStruct((slots, nvals0), F32)),
        recv_setup, wm, wa,
    )
    recv_0 = lax.all_to_all(pay_0, "net", 0, 0, tiled=True)

    def spread(p):
        return (lax.broadcasted_iota(jnp.int32, (3 * slots, slots), 0)
                == 3 * lax.broadcasted_iota(jnp.int32, (3 * slots, slots), 1) + p).astype(BF)

    def local_part(first, refs):
        if first:
            (wm_ref, wa_ref, bf_ref, bt_ref, bc_ref, bs_ref, bl_ref, bn_ref,
             gb_ref, gl_ref, gq_ref, gr_ref, gcr_ref, gcq_ref, pe_ref,
             sr_lo_ref, sr_ref, sr_hi_ref, sq_ref,
             tot_out, sup_out, ci_out, g0_out, gq0_out) = refs
            zero_b = jnp.zeros((nrow, buses), F32)
            state = (wm_ref[...], wa_ref[...], zero_b, zero_b)
            carry_in = None
        else:
            (st_ref, bf_ref, bt_ref, bc_ref, bs_ref, bl_ref, bn_ref,
             gb_ref, gl_ref, gq_ref, gr_ref, gcr_ref, gcq_ref, pe_ref,
             ci_ref, g0_ref, gq0_ref,
             tot_out, sup_out, gr_out, gq_out) = refs
            state = tuple(st_ref[i] for i in range(4))
            carry_in = load_carry(ci_ref)
        inc_from = onehot(bf_ref[...], buses)
        inc_to = onehot(bt_ref[...], buses)
        inc_gen = onehot(gb_ref[...], buses)
        stack = rows(*state)
        pick_from = split4(take(stack, inc_from), nrow)
        pick_to = split4(take(stack, inc_to), nrow)
        prm_in = (bc_ref[...], bs_ref[...], bl_ref[...], bn_ref[...])
        carry_i, fi, ti = advance(carry_in, pick_from, pick_to, prm_in)
        totals = give(fi, inc_from) + give(ti, inc_to)
        for i in range(4):
            tot_out[i] = totals[i * nrow:(i + 1) * nrow]
        lin, quad, ramp, capr, capq = gl_ref[...], gq_ref[...], gr_ref[...], gcr_ref[...], gcq_ref[...]
        per = pe_ref[...]
        nb = (per > 0).astype(F32) + (per < horizon - 1).astype(F32)
        denom = 2.0 * quad + 1.0 + ramp * nb
        if first:
            ext = rows(sr_lo_ref[...], sr_ref[...], sr_hi_ref[...])
            g0 = jnp.clip((ext[scen:scen + window] - lin + ramp * (ext[0:window] + ext[2 * scen:2 * scen + window]))
                          / denom, 0.0, capr)
            g0 = jnp.where((per >= 0) & (per < horizon), g0, 0.0)
            gen_real = g0[scen:scen + nrow]
            gen_react = jnp.clip(sq_ref[...], -capq, capq)
            supply = give(rows(gen_real, gen_react), inc_gen)
            store_carry(ci_out, carry_i)
            g0_out[...] = g0
            gq0_out[...] = gen_react
        else:
            g0 = g0_ref[...]
            gp = take(rows(state[2], state[3]), inc_gen)
            gp_r, gp_q = gp[0:nrow], gp[nrow:]
            gen_real = jnp.clip(
                (g0[scen:scen + nrow] - 2.0 * gp_r - lin + ramp * (g0[0:nrow] + g0[2 * scen:2 * scen + nrow]))
                / denom[scen:scen + nrow],
                0.0,
                capr,
            )
            gen_react = jnp.clip(gq0_ref[...] - 2.0 * gp_q, -capq, capq)
            supply = give(rows(gen_real + gp_r, gen_react + gp_q), inc_gen)
            gr_out[...] = gen_real
            gq_out[...] = gen_react
        sup_out[0] = supply[0:nrow]
        sup_out[1] = supply[nrow:]

    def mirror0_kernel(mirror_ref, wm_ref, wa_ref, bf_ref, bt_ref, cn_ref, gb_ref, tot_out, cm_out, dg_out):
        mirror = mirror_ref[...]
        inc_recv = onehot(mirror[0:1].astype(jnp.int32) - 1, buses)
        degree = (col_sum(onehot(bf_ref[...], buses)) + col_sum(onehot(bt_ref[...], buses))
                  + col_sum(onehot(cn_ref[...], buses)) + col_sum(inc_recv))
        dg_out[...] = rows(degree, col_sum(onehot(gb_ref[...], buses)), jnp.zeros((6, buses), F32))
        zm = jnp.zeros((nrow, slots), F32)
        zero_b = jnp.zeros((nrow, buses), F32)
        stack = rows(wm_ref[...], wa_ref[...], zero_b, zero_b)
        pick_recv = split4(take(stack, inc_recv), nrow)
        near_mirror = (mirror[8:8 + nrow], mirror[8 + nrow:8 + 2 * nrow], zm, zm)
        prm_mir = (mirror[1:2], mirror[2:3], mirror[3:4], mirror[4:5])
        carry_m, _, tmr = advance(None, near_mirror, pick_recv, prm_mir)
        totals = give(tmr, inc_recv)
        for i in range(4):
            tot_out[i] = totals[i * nrow:(i + 1) * nrow]
        store_carry(cm_out, carry_m)

    def cut_part(first, refs):
        (st_ref, wm_ref, wa_ref, lr_ref, lq_ref, recv_ref, mirror_ref, slot_ref,
         dg_ref, cp_ref, tin_ref, sup_ref, tm_ref) = refs[:13]
        rest = refs[13:]
        cprm_v = cp_ref[...]
        wmv, wav = wm_ref[...], wa_ref[...]
        slot_t = slot_ref[...].astype(BF)
        mirror = mirror_ref[...]
        inc_near = onehot(cprm_v[0:1].astype(jnp.int32), buses)
        inc_recv = onehot(mirror[0:1].astype(jnp.int32) - 1, buses)
        degree = dg_ref[0:1]
        gen_count = dg_ref[1:2]
        prm_cut = (cprm_v[1:2], cprm_v[2:3], cprm_v[3:4], cprm_v[4:5])
        if first:
            (cc_out, st_out, pay_out) = rest
            zero_b = jnp.zeros((nrow, buses), F32)
            state = (wmv, wav, zero_b, zero_b)
            far_slot = recv_ref[...].T
            zc = jnp.zeros((nrow, cuts), F32)
            far_c = give(rows(far_slot[0:nrow], far_slot[nrow:2 * nrow]), slot_t)
            far_cross = (far_c[0:nrow], far_c[nrow:], zc, zc)
            stack = rows(*state)
            pick_near = split4(take(stack, inc_near), nrow)
            carry_c, fc, _ = advance(None, pick_near, far_cross, prm_cut)
            totals = tin_ref[...] + tm_ref[...] + give(fc, inc_near).reshape(4, nrow, buses)
        else:
            (cc_in_ref, cm_ref, mag_out, ang_out, pr_out) = rest
            state = tuple(st_ref[i] for i in range(4))
            got = recv_ref[...]
            both = rows(*(take_left(spread(p).T, got).T for p in range(3)))
            near_mirror = split4(both[0:4 * nrow], nrow)
            far_cross = split4(give(both[4 * nrow:], slot_t), nrow)
            stack = rows(*state)
            pick_near = split4(take(stack, inc_near), nrow)
            pick_recv = split4(take(stack, inc_recv), nrow)
            carry_c_in = load_carry(cc_in_ref)
            carry_m_in = load_carry(cm_ref)
            _, fc, _ = advance(carry_c_in, pick_near, far_cross, prm_cut)
            prm_mir = (mirror[1:2], mirror[2:3], mirror[3:4], mirror[4:5])
            _, _, tmr = advance(carry_m_in, near_mirror, pick_recv, prm_mir)
            totals = tin_ref[...] + (give(fc, inc_near) + give(tmr, inc_recv)).reshape(4, nrow, buses)
        mag = (totals[0] + wmv) / (degree + 1.0)
        ang = (totals[1] + wav) / (degree + 1.0)
        weight = 1.0 + BALANCE_WEIGHT * (gen_count + degree)
        pr = BALANCE_WEIGHT * (sup_ref[0] - totals[2] - lr_ref[...]) / weight
        pq = BALANCE_WEIGHT * (sup_ref[1] - totals[3] - lq_ref[...]) / weight
        if first:
            store_carry(cc_out, carry_c)
            st_out[0] = mag
            st_out[1] = ang
            st_out[2] = pr
            st_out[3] = pq
            new_stack = rows(mag, ang, pr, pq)
            near_slot = dot(inc_near, slot_t, NN).astype(BF)
            vals = rows(take(new_stack, near_slot), take(new_stack, inc_recv))
            pay_out[...] = sum(give_left(spread(p), vals[p * 128:(p + 1) * 128]) for p in range(3))
        else:
            mag_out[...] = mag
            ang_out[...] = ang
            pr_out[...] = pr

    sds = jax.ShapeDtypeStruct
    tot_shape = sds((4, nrow, buses), F32)
    br_all = br_rows
    gen_all = (*gen_rows, period_ext)
    tin0, sup0, ci1, g0, gq0 = vmem_call(
        lambda *refs: local_part(True, refs),
        (tot_shape, sds((2, nrow, buses), F32), sds((10, nrow, buses), F32), sds((window, gens), F32),
         sds((nrow, gens), F32)),
        wm, wa, *br_all, *gen_all, lo, sr, hi, sq,
    )
    tm0, cm1, dg = vmem_call(
        mirror0_kernel, (tot_shape, sds((10, nrow, slots), F32), sds((8, buses), F32)), mirror_t, wm, wa,
        br_rows[0], br_rows[1], cut_rows[0], gen_rows[0],
    )
    cprm = jnp.concatenate([cut_rows[0].astype(F32), *cut_rows[1:], jnp.zeros((3, cuts), F32)], axis=0)
    cc1, st1, pay_1 = vmem_call(
        lambda *refs: cut_part(True, refs),
        (sds((10, nrow, cuts), F32), tot_shape, sds((3 * slots, 128), F32)),
        wm, wm, wa, lr, lq, recv_0, mirror_t, slot_t, dg, cprm, tin0, sup0, tm0,
    )
    recv_1 = lax.all_to_all(pay_1.reshape(3 * parts, 2, 128), "net", 0, 0, tiled=True).reshape(3 * slots, 128)
    tin1, sup1, gr, gq = vmem_call(
        lambda *refs: local_part(False, refs),
        (tot_shape, sds((2, nrow, buses), F32), sds((nrow, gens), F32), sds((nrow, gens), F32)),
        st1, *br_all, *gen_all, ci1, g0, gq0,
    )
    mag, ang, pr = vmem_call(
        lambda *refs: cut_part(False, refs),
        (sds((nrow, buses), F32), sds((nrow, buses), F32), sds((nrow, buses), F32)),
        st1, wm, wa, lr, lq, recv_1, mirror_t, slot_t, dg, cprm, tin1, sup1, tin1,
        cc1, cm1,
    )
    shape_b = (periods, scen, buses)
    shape_g = (periods, scen, gens)
    return (mag.reshape(shape_b), ang.reshape(shape_b), pr.reshape(shape_b), gr.reshape(shape_g),
            gq.reshape(shape_g))


def solution(mesh):
    bus = P("tm", None, "net")
    one = P("net")
    return jax.shard_map(
        on_device,
        mesh=mesh,
        in_specs=(bus,) * 6 + (one,) * 12 + (one, P("net", None)) + (one,) * 5,
        out_specs=(bus,) * 5,
        check_vma=False,
    )
```

```python
import jax
import jax.numpy as jnp
from jax import lax
from jax.experimental import pallas as pl
from jax.experimental.pallas import tpu as pltpu
from jax.sharding import PartitionSpec as P

INNER = 4
STEP_SIZE = 0.0005
RADIUS = 0.05
BALANCE_WEIGHT = 2.0
HI = lax.Precision.HIGHEST
F32 = jnp.float32


NN = (((1,), (0,)), ((), ()))
NT = (((1,), (1,)), ((), ()))
BF = jnp.bfloat16


def split3(x):
    hi = x.astype(BF)
    r = x - hi.astype(F32)
    mid = r.astype(BF)
    lo = (r - mid.astype(F32)).astype(BF)
    return hi, mid, lo


def dot(a, b, dims):
    return lax.dot_general(a, b, dims, preferred_element_type=F32)


def take(vals, oh):
    hi, mid, lo = split3(vals)
    return (dot(hi, oh, NN) + dot(mid, oh, NN)) + dot(lo, oh, NN)


def give(vals, oh):
    hi, mid, lo = split3(vals)
    return (dot(hi, oh, NT) + dot(mid, oh, NT)) + dot(lo, oh, NT)


def take_left(oh, vals):
    hi, mid, lo = split3(vals)
    return (dot(oh, hi, NN) + dot(oh, mid, NN)) + dot(oh, lo, NN)


def give_left(oh, vals):
    hi, mid, lo = split3(vals)
    return (dot(oh, hi, NT) + dot(oh, mid, NT)) + dot(oh, lo, NT)


def onehot(ids_row, count):
    n = ids_row.shape[1]
    return (lax.broadcasted_iota(jnp.int32, (count, n), 0) == ids_row).astype(BF)


def col_sum(inc):
    return dot(jnp.ones((8, inc.shape[1]), BF), inc, NT)[0:1]


def rows(*parts):
    return jnp.concatenate(parts, axis=0)


def trig(x):
    d = x[1] - x[3]
    return (jnp.cos(d), jnp.sin(d))


def flows(x, cs, g, b):
    mf, _, mt, _ = x
    c, s = cs
    p = mf * mt
    return (
        g * mf * mf - p * (g * c + b * s),
        -b * mf * mf - p * (g * s - b * c),
        g * mt * mt - p * (g * c - b * s),
        -b * mt * mt + p * (g * s + b * c),
    )


def energy_grad(x, cs, f, t, ft, g, b, l2):
    mf, af, mt, at = x
    c, s = cs
    p = mf * mt
    ka = g * c + b * s
    kb = g * s - b * c
    kc = g * c - b * s
    kd = g * s + b * c
    if f is None:
        f = (g * mf * mf - p * ka, -b * mf * mf - p * kb, g * mt * mt - p * kc, -b * mt * mt + p * kd)
    f0, f1, f2, f3 = f
    ef = jnp.maximum(f0 * f0 + f1 * f1 - l2, 0.0)
    et = jnp.maximum(f2 * f2 + f3 * f3 - l2, 0.0)
    w0 = (f0 - ft[0]) + 2.0 * ef * f0
    w1 = (f1 - ft[1]) + 2.0 * ef * f1
    w2 = (f2 - ft[2]) + 2.0 * et * f2
    w3 = (f3 - ft[3]) + 2.0 * et * f3
    g_mf = (mf - t[0]) + w0 * (2.0 * g * mf - mt * ka) - w1 * (2.0 * b * mf + mt * kb) - w2 * mt * kc + w3 * mt * kd
    g_mt = (mt - t[2]) - w0 * mf * ka - w1 * mf * kb + w2 * (2.0 * g * mt - mf * kc) - w3 * (2.0 * b * mt - mf * kd)
    g_d = p * (w0 * kb - w1 * ka + w2 * kd + w3 * kc)
    return (g_mf, (af - t[1]) + g_d, g_mt, (at - t[3]) - g_d)


def solve(x, cs, f, t, ft, g, b, l2, steps):
    for attempt in range(INNER):
        if cs is None:
            cs = trig(x)
        grad = energy_grad(x, cs, f, t, ft, g, b, l2)
        x = tuple(
            jnp.where(attempt < steps, xi - jnp.clip(STEP_SIZE * gi, -RADIUS, RADIUS), xi)
            for xi, gi in zip(x, grad)
        )
        cs, f = None, None
    return x


def advance(carry, near, far, prm):
    g, b, lim, steps = prm
    ends = (near[0], near[1], far[0], far[1])
    prices = (near[2], near[3], far[2], far[3])
    if carry is None:
        copies = ends
        cs = trig(copies)
        flow_prev = flows(copies, cs, g, b)
        volt = tuple(jnp.zeros_like(e) for e in ends)
        target = ends
        flow_target = flow_prev
        dual_flow = volt
    else:
        copies, flow_prev, cs = carry
        volt = tuple(c - e for c, e in zip(copies, ends))
        target = tuple(e - v for e, v in zip(ends, volt))
        flow_target = tuple(f + 2.0 * q for f, q in zip(flow_prev, prices))
        dual_flow = tuple(-q for q in prices)
    copies = solve(copies, cs, flow_prev, target, flow_target, g, b, lim * lim, steps)
    cs = trig(copies)
    flow_prev = flows(copies, cs, g, b)
    side_from = rows(
        copies[0] + volt[0], copies[1] + volt[1], flow_prev[0] + dual_flow[0], flow_prev[1] + dual_flow[1]
    )
    side_to = rows(
        copies[2] + volt[2], copies[3] + volt[3], flow_prev[2] + dual_flow[2], flow_prev[3] + dual_flow[3]
    )
    return (copies, flow_prev, cs), side_from, side_to


def store_carry(ref, carry):
    for i in range(4):
        ref[i] = carry[0][i]
        ref[4 + i] = carry[1][i]
    ref[8] = carry[2][0]
    ref[9] = carry[2][1]


def load_carry(ref):
    return (tuple(ref[i] for i in range(4)), tuple(ref[4 + i] for i in range(4)), (ref[8], ref[9]))


def split4(a, n):
    return tuple(a[i * n:(i + 1) * n] for i in range(4))


def vmem_call(kernel, outs, *args, scratch=()):
    return pl.pallas_call(
        kernel,
        out_shape=outs,
        in_specs=[pl.BlockSpec(memory_space=pltpu.VMEM)] * len(args),
        out_specs=tuple(pl.BlockSpec(memory_space=pltpu.VMEM) for _ in outs),
        scratch_shapes=scratch,
        compiler_params=pltpu.CompilerParams(vmem_limit_bytes=48 * 1024 * 1024),
    )(*args)


def on_device(
    warm_mag, warm_angle, load_real, load_react, start_real, start_react,
    gen_bus, gen_linear, gen_quad, gen_ramp, gen_cap_real, gen_cap_react,
    branch_from, branch_to, branch_cond, branch_susc, branch_limit, branch_steps,
    cut_near, cut_peer, cut_bus, cut_cond, cut_susc, cut_limit, cut_steps,
):
    periods, scen, buses = warm_mag.shape
    nrow = periods * scen
    cuts = cut_near.shape[0]
    parts = lax.axis_size("net")
    cap = max(2, cuts // parts * 2)
    slots = parts * cap
    gens = gen_bus.shape[0]
    ntm = lax.axis_size("tm")
    horizon = periods * ntm

    def row(v):
        return v.reshape(1, -1)

    wm = warm_mag.reshape(nrow, buses)
    wa = warm_angle.reshape(nrow, buses)
    lr = load_real.reshape(nrow, buses)
    lq = load_react.reshape(nrow, buses)
    sr = start_real.reshape(nrow, gens)
    sq = start_react.reshape(nrow, gens)
    halo = 2 * scen
    lo = lax.ppermute(sr[nrow - halo:], "tm", [(i, i + 1) for i in range(ntm - 1)])
    hi = lax.ppermute(sr[:halo], "tm", [(i + 1, i) for i in range(ntm - 1)])
    window = nrow + 2 * scen
    period_ext = (
        lax.axis_index("tm") * periods - 1 + jnp.arange(window, dtype=jnp.int32) // scen
    ).reshape(window, 1)
    gen_rows = (row(gen_bus), row(gen_linear), row(gen_quad), row(gen_ramp), row(gen_cap_real), row(gen_cap_react))
    br_rows = (row(branch_from), row(branch_to), row(branch_cond), row(branch_susc), row(branch_limit),
               row(branch_steps.astype(F32)))
    cut_rows = (row(cut_near), row(cut_cond), row(cut_susc), row(cut_limit), row(cut_steps.astype(F32)))
    cut_bus_row = row(cut_bus.astype(F32))
    nvals0 = 128

    def prep_kernel(peer_hbm, near_hbm, bus_hbm, cond_hbm, susc_hbm, lim_hbm, steps_hbm, wm_hbm, wa_hbm,
                    slot_out, pay_out,
                    peer_ref, near_ref, bus_ref, cond_ref, susc_ref, lim_ref, steps_ref, wm_ref, wa_ref, sems):
        pairs = ((peer_hbm, peer_ref), (near_hbm, near_ref), (bus_hbm, bus_ref), (cond_hbm, cond_ref),
                 (susc_hbm, susc_ref), (lim_hbm, lim_ref), (steps_hbm, steps_ref), (wm_hbm, wm_ref),
                 (wa_hbm, wa_ref))
        copies = [pltpu.make_async_copy(src, dst, sems.at[i]) for i, (src, dst) in enumerate(pairs)]
        for cp in copies:
            cp.start()
        for cp in copies:
            cp.wait()
        peer = peer_ref[...]
        mine_t = (lax.broadcasted_iota(jnp.int32, (parts, cuts), 0) == peer).astype(F32)
        same = dot(mine_t.T.astype(BF), mine_t.astype(BF), NN)
        earlier = lax.broadcasted_iota(jnp.int32, (cuts, cuts), 0) < lax.broadcasted_iota(jnp.int32, (cuts, cuts), 1)
        rank = jnp.sum(jnp.where(earlier, same, 0.0), axis=0, keepdims=True)
        position = peer.astype(F32) * cap + rank
        slot_t = (lax.broadcasted_iota(jnp.int32, (slots, cuts), 0).astype(F32) == position).astype(F32).T
        slot_b = slot_t.astype(BF)
        slot_out[...] = slot_t
        inc_near = onehot(near_ref[...], buses)
        by_slot = dot(inc_near, slot_b, NN).astype(BF)
        prm = rows(bus_ref[...].astype(F32) + 1.0, cond_ref[...], susc_ref[...], lim_ref[...],
                   steps_ref[...].astype(F32), jnp.zeros((3, cuts), F32))
        vals = rows(
            take(prm, slot_b),
            take(rows(wm_ref[...], wa_ref[...]), by_slot),
            jnp.zeros((nvals0 - 8 - 2 * nrow, slots), F32),
        )
        pay_out[...] = vals.T

    prep_args = (row(cut_peer), cut_rows[0], row(cut_bus), cut_rows[1], cut_rows[2], cut_rows[3], row(cut_steps),
                 wm, wa)
    slot_t, pay_setup = pl.pallas_call(
        prep_kernel,
        out_shape=(jax.ShapeDtypeStruct((cuts, slots), F32), jax.ShapeDtypeStruct((slots, nvals0), F32)),
        in_specs=[pl.BlockSpec(memory_space=pl.ANY)] * len(prep_args),
        out_specs=(pl.BlockSpec(memory_space=pltpu.VMEM), pl.BlockSpec(memory_space=pltpu.VMEM)),
        scratch_shapes=[pltpu.VMEM(a.shape, a.dtype) for a in prep_args] + [pltpu.SemaphoreType.DMA((len(prep_args),))],
    )(*prep_args)
    recv_setup = lax.all_to_all(pay_setup, "net", 0, 0, tiled=True)

    def mid_kernel(recv_ref, wm_ref, wa_ref, mirror_out, pay_out):
        mirror = recv_ref[...].T
        mirror_out[...] = mirror
        inc_recv = onehot(mirror[0:1].astype(jnp.int32) - 1, buses)
        vals = rows(take(rows(wm_ref[...], wa_ref[...]), inc_recv), jnp.zeros((nvals0 - 2 * nrow, slots), F32))
        pay_out[...] = vals.T

    mirror_t, pay_0 = vmem_call(
        mid_kernel,
        (jax.ShapeDtypeStruct((nvals0, slots), F32), jax.ShapeDtypeStruct((slots, nvals0), F32)),
        recv_setup, wm, wa,
    )
    recv_0 = lax.all_to_all(pay_0, "net", 0, 0, tiled=True)

    def spread(p):
        return (lax.broadcasted_iota(jnp.int32, (3 * slots, slots), 0)
                == 3 * lax.broadcasted_iota(jnp.int32, (3 * slots, slots), 1) + p).astype(BF)

    def local_part(first, refs):
        if first:
            (wm_ref, wa_ref, bf_ref, bt_ref, bc_ref, bs_ref, bl_ref, bn_ref,
             gb_ref, gl_ref, gq_ref, gr_ref, gcr_ref, gcq_ref, pe_ref,
             sr_lo_ref, sr_ref, sr_hi_ref, sq_ref,
             tot_out, sup_out, ci_out, g0_out, gq0_out) = refs
            zero_b = jnp.zeros((nrow, buses), F32)
            state = (wm_ref[...], wa_ref[...], zero_b, zero_b)
            carry_in = None
        else:
            (st_ref, bf_ref, bt_ref, bc_ref, bs_ref, bl_ref, bn_ref,
             gb_ref, gl_ref, gq_ref, gr_ref, gcr_ref, gcq_ref, pe_ref,
             ci_ref, g0_ref, gq0_ref,
             tot_out, sup_out, gr_out, gq_out) = refs
            state = tuple(st_ref[i] for i in range(4))
            carry_in = load_carry(ci_ref)
        inc_from = onehot(bf_ref[...], buses)
        inc_to = onehot(bt_ref[...], buses)
        inc_gen = onehot(gb_ref[...], buses)
        stack = rows(*state)
        pick_from = split4(take(stack, inc_from), nrow)
        pick_to = split4(take(stack, inc_to), nrow)
        prm_in = (bc_ref[...], bs_ref[...], bl_ref[...], bn_ref[...])
        carry_i, fi, ti = advance(carry_in, pick_from, pick_to, prm_in)
        totals = give(fi, inc_from) + give(ti, inc_to)
        for i in range(4):
            tot_out[i] = totals[i * nrow:(i + 1) * nrow]
        lin, quad, ramp, capr, capq = gl_ref[...], gq_ref[...], gr_ref[...], gcr_ref[...], gcq_ref[...]
        per = pe_ref[...]
        nb = (per > 0).astype(F32) + (per < horizon - 1).astype(F32)
        denom = 2.0 * quad + 1.0 + ramp * nb
        if first:
            ext = rows(sr_lo_ref[...], sr_ref[...], sr_hi_ref[...])
            g0 = jnp.clip((ext[scen:scen + window] - lin + ramp * (ext[0:window] + ext[2 * scen:2 * scen + window]))
                          / denom, 0.0, capr)
            g0 = jnp.where((per >= 0) & (per < horizon), g0, 0.0)
            gen_real = g0[scen:scen + nrow]
            gen_react = jnp.clip(sq_ref[...], -capq, capq)
            supply = give(rows(gen_real, gen_react), inc_gen)
            store_carry(ci_out, carry_i)
            g0_out[...] = g0
            gq0_out[...] = gen_react
        else:
            g0 = g0_ref[...]
            gp = take(rows(state[2], state[3]), inc_gen)
            gp_r, gp_q = gp[0:nrow], gp[nrow:]
            gen_real = jnp.clip(
                (g0[scen:scen + nrow] - 2.0 * gp_r - lin + ramp * (g0[0:nrow] + g0[2 * scen:2 * scen + nrow]))
                / denom[scen:scen + nrow],
                0.0,
                capr,
            )
            gen_react = jnp.clip(gq0_ref[...] - 2.0 * gp_q, -capq, capq)
            supply = give(rows(gen_real + gp_r, gen_react + gp_q), inc_gen)
            gr_out[...] = gen_real
            gq_out[...] = gen_react
        sup_out[0] = supply[0:nrow]
        sup_out[1] = supply[nrow:]

    def mirror0_kernel(mirror_ref, wm_ref, wa_ref, bf_ref, bt_ref, cn_ref, gb_ref, tot_out, cm_out, dg_out):
        mirror = mirror_ref[...]
        inc_recv = onehot(mirror[0:1].astype(jnp.int32) - 1, buses)
        degree = (col_sum(onehot(bf_ref[...], buses)) + col_sum(onehot(bt_ref[...], buses))
                  + col_sum(onehot(cn_ref[...], buses)) + col_sum(inc_recv))
        dg_out[...] = rows(degree, col_sum(onehot(gb_ref[...], buses)), jnp.zeros((6, buses), F32))
        zm = jnp.zeros((nrow, slots), F32)
        zero_b = jnp.zeros((nrow, buses), F32)
        stack = rows(wm_ref[...], wa_ref[...], zero_b, zero_b)
        pick_recv = split4(take(stack, inc_recv), nrow)
        near_mirror = (mirror[8:8 + nrow], mirror[8 + nrow:8 + 2 * nrow], zm, zm)
        prm_mir = (mirror[1:2], mirror[2:3], mirror[3:4], mirror[4:5])
        carry_m, _, tmr = advance(None, near_mirror, pick_recv, prm_mir)
        totals = give(tmr, inc_recv)
        for i in range(4):
            tot_out[i] = totals[i * nrow:(i + 1) * nrow]
        store_carry(cm_out, carry_m)

    def cut_part(first, refs):
        (st_ref, wm_ref, wa_ref, lr_ref, lq_ref, recv_ref, mirror_ref, slot_ref,
         dg_ref, cp_ref, tin_ref, sup_ref, tm_ref) = refs[:13]
        rest = refs[13:]
        cprm_v = cp_ref[...]
        wmv, wav = wm_ref[...], wa_ref[...]
        slot_t = slot_ref[...].astype(BF)
        mirror = mirror_ref[...]
        inc_near = onehot(cprm_v[0:1].astype(jnp.int32), buses)
        inc_recv = onehot(mirror[0:1].astype(jnp.int32) - 1, buses)
        degree = dg_ref[0:1]
        gen_count = dg_ref[1:2]
        prm_cut = (cprm_v[1:2], cprm_v[2:3], cprm_v[3:4], cprm_v[4:5])
        if first:
            (cc_out, st_out, pay_out, plane_ref) = rest
            zero_b = jnp.zeros((nrow, buses), F32)
            state = (wmv, wav, zero_b, zero_b)
            far_slot = recv_ref[...].T
            zc = jnp.zeros((nrow, cuts), F32)
            far_c = give(rows(far_slot[0:nrow], far_slot[nrow:2 * nrow]), slot_t)
            far_cross = (far_c[0:nrow], far_c[nrow:], zc, zc)
            stack = rows(*state)
            pick_near = split4(take(stack, inc_near), nrow)
            carry_c, fc, _ = advance(None, pick_near, far_cross, prm_cut)
            totals = tin_ref[...] + tm_ref[...] + give(fc, inc_near).reshape(4, nrow, buses)
        else:
            (cc_in_ref, cm_ref, mag_out, ang_out, pr_out, plane_ref) = rest
            state = tuple(st_ref[i] for i in range(4))
            blocks = []
            for p in range(3):
                for k in range(cap):
                    plane_ref[pl.ds(k, parts, stride=cap), :] = recv_ref[pl.ds(p * cap + k, parts, stride=3 * cap), :]
                blocks.append(plane_ref[...].T)
            both = rows(*blocks)
            near_mirror = split4(both[0:4 * nrow], nrow)
            far_cross = split4(give(both[4 * nrow:], slot_t), nrow)
            stack = rows(*state)
            pick_near = split4(take(stack, inc_near), nrow)
            pick_recv = split4(take(stack, inc_recv), nrow)
            carry_c_in = load_carry(cc_in_ref)
            carry_m_in = load_carry(cm_ref)
            _, fc, _ = advance(carry_c_in, pick_near, far_cross, prm_cut)
            prm_mir = (mirror[1:2], mirror[2:3], mirror[3:4], mirror[4:5])
            _, _, tmr = advance(carry_m_in, near_mirror, pick_recv, prm_mir)
            totals = tin_ref[...] + (give(fc, inc_near) + give(tmr, inc_recv)).reshape(4, nrow, buses)
        mag = (totals[0] + wmv) / (degree + 1.0)
        ang = (totals[1] + wav) / (degree + 1.0)
        weight = 1.0 + BALANCE_WEIGHT * (gen_count + degree)
        pr = BALANCE_WEIGHT * (sup_ref[0] - totals[2] - lr_ref[...]) / weight
        pq = BALANCE_WEIGHT * (sup_ref[1] - totals[3] - lq_ref[...]) / weight
        if first:
            store_carry(cc_out, carry_c)
            st_out[0] = mag
            st_out[1] = ang
            st_out[2] = pr
            st_out[3] = pq
            new_stack = rows(mag, ang, pr, pq)
            near_slot = dot(inc_near, slot_t, NN).astype(BF)
            vals = rows(take(new_stack, near_slot), take(new_stack, inc_recv))
            for p in range(3):
                plane_ref[...] = vals[p * 128:(p + 1) * 128].T
                for k in range(cap):
                    pay_out[pl.ds(p * cap + k, parts, stride=3 * cap), :] = plane_ref[pl.ds(k, parts, stride=cap), :]
        else:
            mag_out[...] = mag
            ang_out[...] = ang
            pr_out[...] = pr

    sds = jax.ShapeDtypeStruct
    tot_shape = sds((4, nrow, buses), F32)
    br_all = br_rows
    gen_all = (*gen_rows, period_ext)
    tin0, sup0, ci1, g0, gq0 = vmem_call(
        lambda *refs: local_part(True, refs),
        (tot_shape, sds((2, nrow, buses), F32), sds((10, nrow, buses), F32), sds((window, gens), F32),
         sds((nrow, gens), F32)),
        wm, wa, *br_all, *gen_all, lo, sr, hi, sq,
    )
    tm0, cm1, dg = vmem_call(
        mirror0_kernel, (tot_shape, sds((10, nrow, slots), F32), sds((8, buses), F32)), mirror_t, wm, wa,
        br_rows[0], br_rows[1], cut_rows[0], gen_rows[0],
    )
    cprm = jnp.concatenate([cut_rows[0].astype(F32), *cut_rows[1:], jnp.zeros((3, cuts), F32)], axis=0)
    cc1, st1, pay_1 = vmem_call(
        lambda *refs: cut_part(True, refs),
        (sds((10, nrow, cuts), F32), tot_shape, sds((3 * slots, 128), F32)),
        wm, wm, wa, lr, lq, recv_0, mirror_t, slot_t, dg, cprm, tin0, sup0, tm0,
        scratch=[pltpu.VMEM((slots, 128), F32)],
    )
    recv_1 = lax.all_to_all(pay_1.reshape(3 * parts, 2, 128), "net", 0, 0, tiled=True).reshape(3 * slots, 128)
    tin1, sup1, gr, gq = vmem_call(
        lambda *refs: local_part(False, refs),
        (tot_shape, sds((2, nrow, buses), F32), sds((nrow, gens), F32), sds((nrow, gens), F32)),
        st1, *br_all, *gen_all, ci1, g0, gq0,
    )
    mag, ang, pr = vmem_call(
        lambda *refs: cut_part(False, refs),
        (sds((nrow, buses), F32), sds((nrow, buses), F32), sds((nrow, buses), F32)),
        st1, wm, wa, lr, lq, recv_1, mirror_t, slot_t, dg, cprm, tin1, sup1, tin1,
        cc1, cm1,
        scratch=[pltpu.VMEM((slots, 128), F32)],
    )
    shape_b = (periods, scen, buses)
    shape_g = (periods, scen, gens)
    return (mag.reshape(shape_b), ang.reshape(shape_b), pr.reshape(shape_b), gr.reshape(shape_g),
            gq.reshape(shape_g))


def solution(mesh):
    bus = P("tm", None, "net")
    one = P("net")
    return jax.shard_map(
        on_device,
        mesh=mesh,
        in_specs=(bus,) * 6 + (one,) * 12 + (one, P("net", None)) + (one,) * 5,
        out_specs=(bus,) * 5,
        check_vma=False,
    )
```

```python
import jax
import jax.numpy as jnp
from jax import lax
from jax.experimental import pallas as pl
from jax.experimental.pallas import tpu as pltpu
from jax.sharding import PartitionSpec as P

INNER = 4
STEP_SIZE = 0.0005
RADIUS = 0.05
BALANCE_WEIGHT = 2.0
HI = lax.Precision.HIGHEST
F32 = jnp.float32


NN = (((1,), (0,)), ((), ()))
NT = (((1,), (1,)), ((), ()))
BF = jnp.bfloat16


def split3(x):
    hi = x.astype(BF)
    r = x - hi.astype(F32)
    mid = r.astype(BF)
    lo = (r - mid.astype(F32)).astype(BF)
    return hi, mid, lo


def dot(a, b, dims):
    return lax.dot_general(a, b, dims, preferred_element_type=F32)


def take_split(parts, oh):
    hi, mid, lo = parts
    return (dot(hi, oh, NN) + dot(mid, oh, NN)) + dot(lo, oh, NN)


def take(vals, oh):
    hi, mid, lo = split3(vals)
    return (dot(hi, oh, NN) + dot(mid, oh, NN)) + dot(lo, oh, NN)


def give(vals, oh):
    hi, mid, lo = split3(vals)
    return (dot(hi, oh, NT) + dot(mid, oh, NT)) + dot(lo, oh, NT)


def take_left(oh, vals):
    hi, mid, lo = split3(vals)
    return (dot(oh, hi, NN) + dot(oh, mid, NN)) + dot(oh, lo, NN)


def give_left(oh, vals):
    hi, mid, lo = split3(vals)
    return (dot(oh, hi, NT) + dot(oh, mid, NT)) + dot(oh, lo, NT)


def onehot(ids_row, count):
    n = ids_row.shape[1]
    return (lax.broadcasted_iota(jnp.int32, (count, n), 0) == ids_row).astype(BF)


def col_sum(inc):
    return dot(jnp.ones((8, inc.shape[1]), BF), inc, NT)[0:1]


def rows(*parts):
    return jnp.concatenate(parts, axis=0)


def trig(x):
    d = x[1] - x[3]
    return (jnp.cos(d), jnp.sin(d))


def flows(x, cs, g, b):
    mf, _, mt, _ = x
    c, s = cs
    p = mf * mt
    return (
        g * mf * mf - p * (g * c + b * s),
        -b * mf * mf - p * (g * s - b * c),
        g * mt * mt - p * (g * c - b * s),
        -b * mt * mt + p * (g * s + b * c),
    )


def energy_grad(x, cs, f, t, ft, g, b, l2):
    mf, af, mt, at = x
    c, s = cs
    p = mf * mt
    ka = g * c + b * s
    kb = g * s - b * c
    kc = g * c - b * s
    kd = g * s + b * c
    if f is None:
        f = (g * mf * mf - p * ka, -b * mf * mf - p * kb, g * mt * mt - p * kc, -b * mt * mt + p * kd)
    f0, f1, f2, f3 = f
    ef = jnp.maximum(f0 * f0 + f1 * f1 - l2, 0.0)
    et = jnp.maximum(f2 * f2 + f3 * f3 - l2, 0.0)
    w0 = (f0 - ft[0]) + 2.0 * ef * f0
    w1 = (f1 - ft[1]) + 2.0 * ef * f1
    w2 = (f2 - ft[2]) + 2.0 * et * f2
    w3 = (f3 - ft[3]) + 2.0 * et * f3
    g_mf = (mf - t[0]) + w0 * (2.0 * g * mf - mt * ka) - w1 * (2.0 * b * mf + mt * kb) - w2 * mt * kc + w3 * mt * kd
    g_mt = (mt - t[2]) - w0 * mf * ka - w1 * mf * kb + w2 * (2.0 * g * mt - mf * kc) - w3 * (2.0 * b * mt - mf * kd)
    g_d = p * (w0 * kb - w1 * ka + w2 * kd + w3 * kc)
    return (g_mf, (af - t[1]) + g_d, g_mt, (at - t[3]) - g_d)


def solve(x, cs, f, t, ft, g, b, l2, steps):
    for attempt in range(INNER):
        if cs is None:
            cs = trig(x)
        grad = energy_grad(x, cs, f, t, ft, g, b, l2)
        x = tuple(
            jnp.where(attempt < steps, xi - jnp.clip(STEP_SIZE * gi, -RADIUS, RADIUS), xi)
            for xi, gi in zip(x, grad)
        )
        cs, f = None, None
    return x


def advance(carry, near, far, prm):
    g, b, lim, steps = prm
    ends = (near[0], near[1], far[0], far[1])
    prices = (near[2], near[3], far[2], far[3])
    if carry is None:
        copies = ends
        cs = trig(copies)
        flow_prev = flows(copies, cs, g, b)
        volt = tuple(jnp.zeros_like(e) for e in ends)
        target = ends
        flow_target = flow_prev
        dual_flow = volt
    else:
        copies, flow_prev, cs = carry
        volt = tuple(c - e for c, e in zip(copies, ends))
        target = tuple(e - v for e, v in zip(ends, volt))
        flow_target = tuple(f + 2.0 * q for f, q in zip(flow_prev, prices))
        dual_flow = tuple(-q for q in prices)
    copies = solve(copies, cs, flow_prev, target, flow_target, g, b, lim * lim, steps)
    cs = trig(copies)
    flow_prev = flows(copies, cs, g, b)
    side_from = rows(
        copies[0] + volt[0], copies[1] + volt[1], flow_prev[0] + dual_flow[0], flow_prev[1] + dual_flow[1]
    )
    side_to = rows(
        copies[2] + volt[2], copies[3] + volt[3], flow_prev[2] + dual_flow[2], flow_prev[3] + dual_flow[3]
    )
    return (copies, flow_prev, cs), side_from, side_to


def store_carry(ref, carry):
    for i in range(4):
        ref[i] = carry[0][i]
        ref[4 + i] = carry[1][i]
    ref[8] = carry[2][0]
    ref[9] = carry[2][1]


def load_carry(ref):
    return (tuple(ref[i] for i in range(4)), tuple(ref[4 + i] for i in range(4)), (ref[8], ref[9]))


def split4(a, n):
    return tuple(a[i * n:(i + 1) * n] for i in range(4))


def vmem_call(kernel, outs, *args, scratch=()):
    return pl.pallas_call(
        kernel,
        out_shape=outs,
        in_specs=[pl.BlockSpec(memory_space=pltpu.VMEM)] * len(args),
        out_specs=tuple(pl.BlockSpec(memory_space=pltpu.VMEM) for _ in outs),
        scratch_shapes=scratch,
        compiler_params=pltpu.CompilerParams(vmem_limit_bytes=48 * 1024 * 1024),
    )(*args)


def on_device(
    warm_mag, warm_angle, load_real, load_react, start_real, start_react,
    gen_bus, gen_linear, gen_quad, gen_ramp, gen_cap_real, gen_cap_react,
    branch_from, branch_to, branch_cond, branch_susc, branch_limit, branch_steps,
    cut_near, cut_peer, cut_bus, cut_cond, cut_susc, cut_limit, cut_steps,
):
    periods, scen, buses = warm_mag.shape
    nrow = periods * scen
    cuts = cut_near.shape[0]
    parts = lax.axis_size("net")
    cap = max(2, cuts // parts * 2)
    slots = parts * cap
    gens = gen_bus.shape[0]
    ntm = lax.axis_size("tm")
    horizon = periods * ntm

    def row(v):
        return v.reshape(1, -1)

    wm = warm_mag.reshape(nrow, buses)
    wa = warm_angle.reshape(nrow, buses)
    lr = load_real.reshape(nrow, buses)
    lq = load_react.reshape(nrow, buses)
    sr = start_real.reshape(nrow, gens)
    sq = start_react.reshape(nrow, gens)
    halo = 2 * scen
    lo = lax.ppermute(sr[nrow - halo:], "tm", [(i, i + 1) for i in range(ntm - 1)])
    hi = lax.ppermute(sr[:halo], "tm", [(i + 1, i) for i in range(ntm - 1)])
    window = nrow + 2 * scen
    period_ext = (
        lax.axis_index("tm") * periods - 1 + jnp.arange(window, dtype=jnp.int32) // scen
    ).reshape(window, 1)
    gen_rows = (row(gen_bus), row(gen_linear), row(gen_quad), row(gen_ramp), row(gen_cap_real), row(gen_cap_react))
    br_rows = (row(branch_from), row(branch_to), row(branch_cond), row(branch_susc), row(branch_limit),
               row(branch_steps.astype(F32)))
    cut_rows = (row(cut_near), row(cut_cond), row(cut_susc), row(cut_limit), row(cut_steps.astype(F32)))
    cut_bus_row = row(cut_bus.astype(F32))
    nvals0 = 128

    def prep_kernel(peer_hbm, near_hbm, bus_hbm, cond_hbm, susc_hbm, lim_hbm, steps_hbm, wm_hbm, wa_hbm,
                    slot_out, pay_out,
                    peer_ref, near_ref, bus_ref, cond_ref, susc_ref, lim_ref, steps_ref, wm_ref, wa_ref, sems):
        pairs = ((peer_hbm, peer_ref), (near_hbm, near_ref), (bus_hbm, bus_ref), (cond_hbm, cond_ref),
                 (susc_hbm, susc_ref), (lim_hbm, lim_ref), (steps_hbm, steps_ref), (wm_hbm, wm_ref),
                 (wa_hbm, wa_ref))
        copies = [pltpu.make_async_copy(src, dst, sems.at[i]) for i, (src, dst) in enumerate(pairs)]
        for cp in copies:
            cp.start()
        copies[0].wait()
        peer = peer_ref[...]
        mine_t = (lax.broadcasted_iota(jnp.int32, (parts, cuts), 0) == peer).astype(F32)
        same = dot(mine_t.T.astype(BF), mine_t.astype(BF), NN)
        earlier = lax.broadcasted_iota(jnp.int32, (cuts, cuts), 0) < lax.broadcasted_iota(jnp.int32, (cuts, cuts), 1)
        rank = jnp.sum(jnp.where(earlier, same, 0.0), axis=0, keepdims=True)
        position = peer.astype(F32) * cap + rank
        slot_t = (lax.broadcasted_iota(jnp.int32, (slots, cuts), 0).astype(F32) == position).astype(F32).T
        slot_b = slot_t.astype(BF)
        slot_out[...] = slot_t
        copies[1].wait()
        inc_near = onehot(near_ref[...], buses)
        by_slot = dot(inc_near, slot_b, NN).astype(BF)
        for cp in copies[2:]:
            cp.wait()
        prm = rows(bus_ref[...].astype(F32) + 1.0, cond_ref[...], susc_ref[...], lim_ref[...],
                   steps_ref[...].astype(F32), jnp.zeros((3, cuts), F32))
        vals = rows(
            take(prm, slot_b),
            take(rows(wm_ref[...], wa_ref[...]), by_slot),
            jnp.zeros((nvals0 - 8 - 2 * nrow, slots), F32),
        )
        pay_out[...] = vals.T

    prep_args = (row(cut_peer), cut_rows[0], row(cut_bus), cut_rows[1], cut_rows[2], cut_rows[3], row(cut_steps),
                 wm, wa)
    slot_t, pay_setup = pl.pallas_call(
        prep_kernel,
        out_shape=(jax.ShapeDtypeStruct((cuts, slots), F32), jax.ShapeDtypeStruct((slots, nvals0), F32)),
        in_specs=[pl.BlockSpec(memory_space=pl.ANY)] * len(prep_args),
        out_specs=(pl.BlockSpec(memory_space=pltpu.VMEM), pl.BlockSpec(memory_space=pltpu.VMEM)),
        scratch_shapes=[pltpu.VMEM(a.shape, a.dtype) for a in prep_args] + [pltpu.SemaphoreType.DMA((len(prep_args),))],
    )(*prep_args)
    recv_setup = lax.all_to_all(pay_setup, "net", 0, 0, tiled=True)

    def mid_kernel(recv_ref, wm_ref, wa_ref, mirror_out, pay_out):
        mirror = recv_ref[...].T
        mirror_out[...] = mirror
        inc_recv = onehot(mirror[0:1].astype(jnp.int32) - 1, buses)
        vals = rows(take(rows(wm_ref[...], wa_ref[...]), inc_recv), jnp.zeros((nvals0 - 2 * nrow, slots), F32))
        pay_out[...] = vals.T

    mirror_t, pay_0 = vmem_call(
        mid_kernel,
        (jax.ShapeDtypeStruct((nvals0, slots), F32), jax.ShapeDtypeStruct((slots, nvals0), F32)),
        recv_setup, wm, wa,
    )
    recv_0 = lax.all_to_all(pay_0, "net", 0, 0, tiled=True)

    def spread(p):
        return (lax.broadcasted_iota(jnp.int32, (3 * slots, slots), 0)
                == 3 * lax.broadcasted_iota(jnp.int32, (3 * slots, slots), 1) + p).astype(BF)

    def local_part(first, refs):
        if first:
            (wm_ref, wa_ref, bf_ref, bt_ref, bc_ref, bs_ref, bl_ref, bn_ref,
             gb_ref, gl_ref, gq_ref, gr_ref, gcr_ref, gcq_ref, pe_ref,
             sr_lo_ref, sr_ref, sr_hi_ref, sq_ref,
             tot_out, sup_out, ci_out, g0_out, gq0_out) = refs
            zero_b = jnp.zeros((nrow, buses), F32)
            state = (wm_ref[...], wa_ref[...], zero_b, zero_b)
            carry_in = None
        else:
            (st_ref, bf_ref, bt_ref, bc_ref, bs_ref, bl_ref, bn_ref,
             gb_ref, gl_ref, gq_ref, gr_ref, gcr_ref, gcq_ref, pe_ref,
             ci_ref, g0_ref, gq0_ref, cp_ref, mir_ref,
             tot_out, sup_out, gr_out, gq_out, pn_out, prc_out) = refs
            state = tuple(st_ref[i] for i in range(4))
            carry_in = load_carry(ci_ref)
        inc_from = onehot(bf_ref[...], buses)
        inc_to = onehot(bt_ref[...], buses)
        inc_gen = onehot(gb_ref[...], buses)
        stack = split3(rows(*state))
        pick_from = split4(take_split(stack, inc_from), nrow)
        pick_to = split4(take_split(stack, inc_to), nrow)
        if not first:
            pn_out[...] = take_split(stack, onehot(cp_ref[0:1].astype(jnp.int32), buses))
            prc_out[...] = take_split(stack, onehot(mir_ref[0:1].astype(jnp.int32) - 1, buses))
        prm_in = (bc_ref[...], bs_ref[...], bl_ref[...], bn_ref[...])
        carry_i, fi, ti = advance(carry_in, pick_from, pick_to, prm_in)
        totals = give(fi, inc_from) + give(ti, inc_to)
        for i in range(4):
            tot_out[i] = totals[i * nrow:(i + 1) * nrow]
        lin, quad, ramp, capr, capq = gl_ref[...], gq_ref[...], gr_ref[...], gcr_ref[...], gcq_ref[...]
        per = pe_ref[...]
        nb = (per > 0).astype(F32) + (per < horizon - 1).astype(F32)
        denom = 2.0 * quad + 1.0 + ramp * nb
        if first:
            ext = rows(sr_lo_ref[...], sr_ref[...], sr_hi_ref[...])
            g0 = jnp.clip((ext[scen:scen + window] - lin + ramp * (ext[0:window] + ext[2 * scen:2 * scen + window]))
                          / denom, 0.0, capr)
            g0 = jnp.where((per >= 0) & (per < horizon), g0, 0.0)
            gen_real = g0[scen:scen + nrow]
            gen_react = jnp.clip(sq_ref[...], -capq, capq)
            supply = give(rows(gen_real, gen_react), inc_gen)
            store_carry(ci_out, carry_i)
            g0_out[...] = g0
            gq0_out[...] = gen_react
        else:
            g0 = g0_ref[...]
            gp = take(rows(state[2], state[3]), inc_gen)
            gp_r, gp_q = gp[0:nrow], gp[nrow:]
            gen_real = jnp.clip(
                (g0[scen:scen + nrow] - 2.0 * gp_r - lin + ramp * (g0[0:nrow] + g0[2 * scen:2 * scen + nrow]))
                / denom[scen:scen + nrow],
                0.0,
                capr,
            )
            gen_react = jnp.clip(gq0_ref[...] - 2.0 * gp_q, -capq, capq)
            supply = give(rows(gen_real + gp_r, gen_react + gp_q), inc_gen)
            gr_out[...] = gen_real
            gq_out[...] = gen_react
        sup_out[0] = supply[0:nrow]
        sup_out[1] = supply[nrow:]

    def mirror0_kernel(mirror_ref, wm_ref, wa_ref, bf_ref, bt_ref, cn_ref, gb_ref, tot_out, cm_out, dg_out):
        mirror = mirror_ref[...]
        inc_recv = onehot(mirror[0:1].astype(jnp.int32) - 1, buses)
        degree = (col_sum(onehot(bf_ref[...], buses)) + col_sum(onehot(bt_ref[...], buses))
                  + col_sum(onehot(cn_ref[...], buses)) + col_sum(inc_recv))
        dg_out[...] = rows(degree, col_sum(onehot(gb_ref[...], buses)), jnp.zeros((6, buses), F32))
        zm = jnp.zeros((nrow, slots), F32)
        zero_b = jnp.zeros((nrow, buses), F32)
        stack = rows(wm_ref[...], wa_ref[...], zero_b, zero_b)
        pick_recv = split4(take(stack, inc_recv), nrow)
        near_mirror = (mirror[8:8 + nrow], mirror[8 + nrow:8 + 2 * nrow], zm, zm)
        prm_mir = (mirror[1:2], mirror[2:3], mirror[3:4], mirror[4:5])
        carry_m, _, tmr = advance(None, near_mirror, pick_recv, prm_mir)
        totals = give(tmr, inc_recv)
        for i in range(4):
            tot_out[i] = totals[i * nrow:(i + 1) * nrow]
        store_carry(cm_out, carry_m)

    def cut_part(first, refs):
        (st_ref, wm_ref, wa_ref, lr_ref, lq_ref, recv_ref, mirror_ref, slot_ref,
         dg_ref, cp_ref, tin_ref, sup_ref, tm_ref) = refs[:13]
        rest = refs[13:]
        cprm_v = cp_ref[...]
        wmv, wav = wm_ref[...], wa_ref[...]
        slot_t = slot_ref[...].astype(BF)
        mirror = mirror_ref[...]
        inc_near = onehot(cprm_v[0:1].astype(jnp.int32), buses)
        inc_recv = onehot(mirror[0:1].astype(jnp.int32) - 1, buses)
        degree = dg_ref[0:1]
        gen_count = dg_ref[1:2]
        prm_cut = (cprm_v[1:2], cprm_v[2:3], cprm_v[3:4], cprm_v[4:5])
        if first:
            (cc_out, st_out, pay_out, plane_ref) = rest
            zero_b = jnp.zeros((nrow, buses), F32)
            state = (wmv, wav, zero_b, zero_b)
            far_slot = recv_ref[...].T
            zc = jnp.zeros((nrow, cuts), F32)
            far_c = give(rows(far_slot[0:nrow], far_slot[nrow:2 * nrow]), slot_t)
            far_cross = (far_c[0:nrow], far_c[nrow:], zc, zc)
            stack = rows(*state)
            pick_near = split4(take(stack, inc_near), nrow)
            carry_c, fc, _ = advance(None, pick_near, far_cross, prm_cut)
            totals = tin_ref[...] + tm_ref[...] + give(fc, inc_near).reshape(4, nrow, buses)
        else:
            (cc_in_ref, cm_ref, pn_ref, prc_ref, mag_out, ang_out, pr_out, plane_ref) = rest
            state = tuple(st_ref[i] for i in range(4))
            blocks = []
            for p in range(3):
                for k in range(cap):
                    plane_ref[pl.ds(k, parts, stride=cap), :] = recv_ref[pl.ds(p * cap + k, parts, stride=3 * cap), :]
                blocks.append(plane_ref[...].T)
            both = rows(*blocks)
            near_mirror = split4(both[0:4 * nrow], nrow)
            far_cross = split4(give(both[4 * nrow:], slot_t), nrow)
            pick_near = split4(pn_ref[...], nrow)
            pick_recv = split4(prc_ref[...], nrow)
            carry_c_in = load_carry(cc_in_ref)
            carry_m_in = load_carry(cm_ref)
            _, fc, _ = advance(carry_c_in, pick_near, far_cross, prm_cut)
            prm_mir = (mirror[1:2], mirror[2:3], mirror[3:4], mirror[4:5])
            _, _, tmr = advance(carry_m_in, near_mirror, pick_recv, prm_mir)
            totals = tin_ref[...] + (give(fc, inc_near) + give(tmr, inc_recv)).reshape(4, nrow, buses)
        mag = (totals[0] + wmv) / (degree + 1.0)
        ang = (totals[1] + wav) / (degree + 1.0)
        weight = 1.0 + BALANCE_WEIGHT * (gen_count + degree)
        pr = BALANCE_WEIGHT * (sup_ref[0] - totals[2] - lr_ref[...]) / weight
        pq = BALANCE_WEIGHT * (sup_ref[1] - totals[3] - lq_ref[...]) / weight
        if first:
            store_carry(cc_out, carry_c)
            st_out[0] = mag
            st_out[1] = ang
            st_out[2] = pr
            st_out[3] = pq
            new_stack = rows(mag, ang, pr, pq)
            near_slot = dot(inc_near, slot_t, NN).astype(BF)
            vals = rows(take(new_stack, near_slot), take(new_stack, inc_recv))
            for p in range(3):
                plane_ref[...] = vals[p * 128:(p + 1) * 128].T
                for k in range(cap):
                    pay_out[pl.ds(p * cap + k, parts, stride=3 * cap), :] = plane_ref[pl.ds(k, parts, stride=cap), :]
        else:
            mag_out[...] = mag
            ang_out[...] = ang
            pr_out[...] = pr

    sds = jax.ShapeDtypeStruct
    tot_shape = sds((4, nrow, buses), F32)
    br_all = br_rows
    gen_all = (*gen_rows, period_ext)
    tin0, sup0, ci1, g0, gq0 = vmem_call(
        lambda *refs: local_part(True, refs),
        (tot_shape, sds((2, nrow, buses), F32), sds((10, nrow, buses), F32), sds((window, gens), F32),
         sds((nrow, gens), F32)),
        wm, wa, *br_all, *gen_all, lo, sr, hi, sq,
    )
    tm0, cm1, dg = vmem_call(
        mirror0_kernel, (tot_shape, sds((10, nrow, slots), F32), sds((8, buses), F32)), mirror_t, wm, wa,
        br_rows[0], br_rows[1], cut_rows[0], gen_rows[0],
    )
    cprm = jnp.concatenate([cut_rows[0].astype(F32), *cut_rows[1:], jnp.zeros((3, cuts), F32)], axis=0)
    cc1, st1, pay_1 = vmem_call(
        lambda *refs: cut_part(True, refs),
        (sds((10, nrow, cuts), F32), tot_shape, sds((3 * slots, 128), F32)),
        wm, wm, wa, lr, lq, recv_0, mirror_t, slot_t, dg, cprm, tin0, sup0, tm0,
        scratch=[pltpu.VMEM((slots, 128), F32)],
    )
    recv_1 = lax.all_to_all(pay_1.reshape(3 * parts, 2, 128), "net", 0, 0, tiled=True).reshape(3 * slots, 128)
    tin1, sup1, gr, gq, pn1, prc1 = vmem_call(
        lambda *refs: local_part(False, refs),
        (tot_shape, sds((2, nrow, buses), F32), sds((nrow, gens), F32), sds((nrow, gens), F32),
         sds((4 * nrow, cuts), F32), sds((4 * nrow, slots), F32)),
        st1, *br_all, *gen_all, ci1, g0, gq0, cprm, mirror_t,
    )
    mag, ang, pr = vmem_call(
        lambda *refs: cut_part(False, refs),
        (sds((nrow, buses), F32), sds((nrow, buses), F32), sds((nrow, buses), F32)),
        st1, wm, wa, lr, lq, recv_1, mirror_t, slot_t, dg, cprm, tin1, sup1, tin1,
        cc1, cm1, pn1, prc1,
        scratch=[pltpu.VMEM((slots, 128), F32)],
    )
    shape_b = (periods, scen, buses)
    shape_g = (periods, scen, gens)
    return (mag.reshape(shape_b), ang.reshape(shape_b), pr.reshape(shape_b), gr.reshape(shape_g),
            gq.reshape(shape_g))


def solution(mesh):
    bus = P("tm", None, "net")
    one = P("net")
    return jax.shard_map(
        on_device,
        mesh=mesh,
        in_specs=(bus,) * 6 + (one,) * 12 + (one, P("net", None)) + (one,) * 5,
        out_specs=(bus,) * 5,
        check_vma=False,
    )
```

```python
import jax
import jax.numpy as jnp
from jax import lax
from jax.experimental import pallas as pl
from jax.experimental.pallas import tpu as pltpu
from jax.sharding import PartitionSpec as P

INNER = 4
STEP_SIZE = 0.0005
RADIUS = 0.05
BALANCE_WEIGHT = 2.0
HI = lax.Precision.HIGHEST
F32 = jnp.float32


NN = (((1,), (0,)), ((), ()))
NT = (((1,), (1,)), ((), ()))
BF = jnp.bfloat16


def split3(x):
    hi = x.astype(BF)
    r = x - hi.astype(F32)
    mid = r.astype(BF)
    lo = (r - mid.astype(F32)).astype(BF)
    return hi, mid, lo


def dot(a, b, dims):
    return lax.dot_general(a, b, dims, preferred_element_type=F32)


def take_split(parts, oh):
    hi, mid, lo = parts
    return (dot(hi, oh, NN) + dot(mid, oh, NN)) + dot(lo, oh, NN)


def take(vals, oh):
    hi, mid, lo = split3(vals)
    return (dot(hi, oh, NN) + dot(mid, oh, NN)) + dot(lo, oh, NN)


def give(vals, oh):
    hi, mid, lo = split3(vals)
    return (dot(hi, oh, NT) + dot(mid, oh, NT)) + dot(lo, oh, NT)


def take_left(oh, vals):
    hi, mid, lo = split3(vals)
    return (dot(oh, hi, NN) + dot(oh, mid, NN)) + dot(oh, lo, NN)


def give_left(oh, vals):
    hi, mid, lo = split3(vals)
    return (dot(oh, hi, NT) + dot(oh, mid, NT)) + dot(oh, lo, NT)


def onehot(ids_row, count):
    n = ids_row.shape[1]
    return (lax.broadcasted_iota(jnp.int32, (count, n), 0) == ids_row).astype(BF)


def col_sum(inc):
    return dot(jnp.ones((8, inc.shape[1]), BF), inc, NT)[0:1]


def rows(*parts):
    return jnp.concatenate(parts, axis=0)


def trig(x):
    d = x[1] - x[3]
    return (jnp.cos(d), jnp.sin(d))


def flows(x, cs, g, b):
    mf, _, mt, _ = x
    c, s = cs
    p = mf * mt
    return (
        g * mf * mf - p * (g * c + b * s),
        -b * mf * mf - p * (g * s - b * c),
        g * mt * mt - p * (g * c - b * s),
        -b * mt * mt + p * (g * s + b * c),
    )


def energy_grad(x, cs, f, t, ft, g, b, l2):
    mf, af, mt, at = x
    c, s = cs
    p = mf * mt
    ka = g * c + b * s
    kb = g * s - b * c
    kc = g * c - b * s
    kd = g * s + b * c
    if f is None:
        f = (g * mf * mf - p * ka, -b * mf * mf - p * kb, g * mt * mt - p * kc, -b * mt * mt + p * kd)
    f0, f1, f2, f3 = f
    ef = jnp.maximum(f0 * f0 + f1 * f1 - l2, 0.0)
    et = jnp.maximum(f2 * f2 + f3 * f3 - l2, 0.0)
    w0 = (f0 - ft[0]) + 2.0 * ef * f0
    w1 = (f1 - ft[1]) + 2.0 * ef * f1
    w2 = (f2 - ft[2]) + 2.0 * et * f2
    w3 = (f3 - ft[3]) + 2.0 * et * f3
    g_mf = (mf - t[0]) + w0 * (2.0 * g * mf - mt * ka) - w1 * (2.0 * b * mf + mt * kb) - w2 * mt * kc + w3 * mt * kd
    g_mt = (mt - t[2]) - w0 * mf * ka - w1 * mf * kb + w2 * (2.0 * g * mt - mf * kc) - w3 * (2.0 * b * mt - mf * kd)
    g_d = p * (w0 * kb - w1 * ka + w2 * kd + w3 * kc)
    return (g_mf, (af - t[1]) + g_d, g_mt, (at - t[3]) - g_d)


def solve(x, cs, f, t, ft, g, b, l2, steps):
    for attempt in range(INNER):
        if cs is None:
            cs = trig(x)
        grad = energy_grad(x, cs, f, t, ft, g, b, l2)
        x = tuple(
            jnp.where(attempt < steps, xi - jnp.clip(STEP_SIZE * gi, -RADIUS, RADIUS), xi)
            for xi, gi in zip(x, grad)
        )
        cs, f = None, None
    return x


def advance(carry, near, far, prm):
    g, b, lim, steps = prm
    ends = (near[0], near[1], far[0], far[1])
    prices = (near[2], near[3], far[2], far[3])
    if carry is None:
        copies = ends
        cs = trig(copies)
        flow_prev = flows(copies, cs, g, b)
        volt = tuple(jnp.zeros_like(e) for e in ends)
        target = ends
        flow_target = flow_prev
        dual_flow = volt
    else:
        copies, flow_prev, cs = carry
        volt = tuple(c - e for c, e in zip(copies, ends))
        target = tuple(e - v for e, v in zip(ends, volt))
        flow_target = tuple(f + 2.0 * q for f, q in zip(flow_prev, prices))
        dual_flow = tuple(-q for q in prices)
    copies = solve(copies, cs, flow_prev, target, flow_target, g, b, lim * lim, steps)
    cs = trig(copies)
    flow_prev = flows(copies, cs, g, b)
    side_from = rows(
        copies[0] + volt[0], copies[1] + volt[1], flow_prev[0] + dual_flow[0], flow_prev[1] + dual_flow[1]
    )
    side_to = rows(
        copies[2] + volt[2], copies[3] + volt[3], flow_prev[2] + dual_flow[2], flow_prev[3] + dual_flow[3]
    )
    return (copies, flow_prev, cs), side_from, side_to


def store_carry(ref, carry):
    for i in range(4):
        ref[i] = carry[0][i]
        ref[4 + i] = carry[1][i]
    ref[8] = carry[2][0]
    ref[9] = carry[2][1]


def load_carry(ref):
    return (tuple(ref[i] for i in range(4)), tuple(ref[4 + i] for i in range(4)), (ref[8], ref[9]))


def split4(a, n):
    return tuple(a[i * n:(i + 1) * n] for i in range(4))


def vmem_call(kernel, outs, *args, scratch=()):
    return pl.pallas_call(
        kernel,
        out_shape=outs,
        in_specs=[pl.BlockSpec(memory_space=pltpu.VMEM)] * len(args),
        out_specs=tuple(pl.BlockSpec(memory_space=pltpu.VMEM) for _ in outs),
        scratch_shapes=scratch,
        compiler_params=pltpu.CompilerParams(vmem_limit_bytes=48 * 1024 * 1024),
    )(*args)


def on_device(
    warm_mag, warm_angle, load_real, load_react, start_real, start_react,
    gen_bus, gen_linear, gen_quad, gen_ramp, gen_cap_real, gen_cap_react,
    branch_from, branch_to, branch_cond, branch_susc, branch_limit, branch_steps,
    cut_near, cut_peer, cut_bus, cut_cond, cut_susc, cut_limit, cut_steps,
):
    periods, scen, buses = warm_mag.shape
    nrow = periods * scen
    cuts = cut_near.shape[0]
    parts = lax.axis_size("net")
    cap = max(2, cuts // parts * 2)
    slots = parts * cap
    gens = gen_bus.shape[0]
    ntm = lax.axis_size("tm")
    horizon = periods * ntm

    def row(v):
        return v.reshape(1, -1)

    wm = warm_mag.reshape(nrow, buses)
    wa = warm_angle.reshape(nrow, buses)
    lr = load_real.reshape(nrow, buses)
    lq = load_react.reshape(nrow, buses)
    sr = start_real.reshape(nrow, gens)
    sq = start_react.reshape(nrow, gens)
    halo = 2 * scen
    lo = lax.ppermute(sr[nrow - halo:], "tm", [(i, i + 1) for i in range(ntm - 1)])
    hi = lax.ppermute(sr[:halo], "tm", [(i + 1, i) for i in range(ntm - 1)])
    window = nrow + 2 * scen
    period_ext = (
        lax.axis_index("tm") * periods - 1 + jnp.arange(window, dtype=jnp.int32) // scen
    ).reshape(window, 1)
    gen_rows = (row(gen_bus), row(gen_linear), row(gen_quad), row(gen_ramp), row(gen_cap_real), row(gen_cap_react))
    br_rows = (row(branch_from), row(branch_to), row(branch_cond), row(branch_susc), row(branch_limit),
               row(branch_steps.astype(F32)))
    cut_rows = (row(cut_near), row(cut_cond), row(cut_susc), row(cut_limit), row(cut_steps.astype(F32)))
    cut_bus_row = row(cut_bus.astype(F32))
    nvals0 = 128

    def prep_kernel(peer_hbm, near_hbm, bus_hbm, cond_hbm, susc_hbm, lim_hbm, steps_hbm, wm_hbm, wa_hbm,
                    slot_out, pay_out,
                    peer_ref, near_ref, bus_ref, cond_ref, susc_ref, lim_ref, steps_ref, wm_ref, wa_ref, sems):
        pairs = ((peer_hbm, peer_ref), (near_hbm, near_ref), (bus_hbm, bus_ref), (cond_hbm, cond_ref),
                 (susc_hbm, susc_ref), (lim_hbm, lim_ref), (steps_hbm, steps_ref), (wm_hbm, wm_ref),
                 (wa_hbm, wa_ref))
        copies = [pltpu.make_async_copy(src, dst, sems.at[i]) for i, (src, dst) in enumerate(pairs)]
        for cp in copies:
            cp.start()
        copies[0].wait()
        peer = peer_ref[...]
        mine_t = (lax.broadcasted_iota(jnp.int32, (parts, cuts), 0) == peer).astype(F32)
        same = dot(mine_t.T.astype(BF), mine_t.astype(BF), NN)
        earlier = lax.broadcasted_iota(jnp.int32, (cuts, cuts), 0) < lax.broadcasted_iota(jnp.int32, (cuts, cuts), 1)
        rank = jnp.sum(jnp.where(earlier, same, 0.0), axis=0, keepdims=True)
        position = peer.astype(F32) * cap + rank
        slot_t = (lax.broadcasted_iota(jnp.int32, (slots, cuts), 0).astype(F32) == position).astype(F32).T
        slot_b = slot_t.astype(BF)
        slot_out[...] = slot_t
        copies[1].wait()
        inc_near = onehot(near_ref[...], buses)
        by_slot = dot(inc_near, slot_b, NN).astype(BF)
        for cp in copies[2:]:
            cp.wait()
        prm = rows(bus_ref[...].astype(F32) + 1.0, cond_ref[...], susc_ref[...], lim_ref[...],
                   steps_ref[...].astype(F32), jnp.zeros((3, cuts), F32))
        vals = rows(
            take(prm, slot_b),
            take(rows(wm_ref[...], wa_ref[...]), by_slot),
            jnp.zeros((nvals0 - 8 - 2 * nrow, slots), F32),
        )
        pay_out[...] = vals.T

    prep_args = (row(cut_peer), cut_rows[0], row(cut_bus), cut_rows[1], cut_rows[2], cut_rows[3], row(cut_steps),
                 wm, wa)
    slot_t, pay_setup = pl.pallas_call(
        prep_kernel,
        out_shape=(jax.ShapeDtypeStruct((cuts, slots), F32), jax.ShapeDtypeStruct((slots, nvals0), F32)),
        in_specs=[pl.BlockSpec(memory_space=pl.ANY)] * len(prep_args),
        out_specs=(pl.BlockSpec(memory_space=pltpu.VMEM), pl.BlockSpec(memory_space=pltpu.VMEM)),
        scratch_shapes=[pltpu.VMEM(a.shape, a.dtype) for a in prep_args] + [pltpu.SemaphoreType.DMA((len(prep_args),))],
    )(*prep_args)
    recv_setup = lax.all_to_all(pay_setup, "net", 0, 0, tiled=True)

    def mid_kernel(recv_ref, wm_ref, wa_ref, mirror_out, pay_out):
        mirror = recv_ref[...].T
        mirror_out[...] = mirror
        inc_recv = onehot(mirror[0:1].astype(jnp.int32) - 1, buses)
        vals = rows(take(rows(wm_ref[...], wa_ref[...]), inc_recv), jnp.zeros((nvals0 - 2 * nrow, slots), F32))
        pay_out[...] = vals.T

    mirror_t, pay_0 = vmem_call(
        mid_kernel,
        (jax.ShapeDtypeStruct((nvals0, slots), F32), jax.ShapeDtypeStruct((slots, nvals0), F32)),
        recv_setup, wm, wa,
    )
    recv_0 = lax.all_to_all(pay_0, "net", 0, 0, tiled=True)

    def spread(p):
        return (lax.broadcasted_iota(jnp.int32, (3 * slots, slots), 0)
                == 3 * lax.broadcasted_iota(jnp.int32, (3 * slots, slots), 1) + p).astype(BF)

    def local_part(first, refs):
        if first:
            (wm_ref, wa_ref, bf_ref, bt_ref, bc_ref, bs_ref, bl_ref, bn_ref,
             gb_ref, gl_ref, gq_ref, gr_ref, gcr_ref, gcq_ref, pe_ref,
             sr_lo_ref, sr_ref, sr_hi_ref, sq_ref,
             tot_out, sup_out, ci_out, g0_out, gq0_out) = refs
            zero_b = jnp.zeros((nrow, buses), F32)
            state = (wm_ref[...], wa_ref[...], zero_b, zero_b)
            carry_in = None
        else:
            (st_ref, bf_ref, bt_ref, bc_ref, bs_ref, bl_ref, bn_ref,
             gb_ref, gl_ref, gq_ref, gr_ref, gcr_ref, gcq_ref, pe_ref,
             ci_ref, g0_ref, gq0_ref, cp_ref, mir_ref,
             tot_out, sup_out, gr_out, gq_out, pn_out, prc_out) = refs
            state = tuple(st_ref[i] for i in range(4))
            carry_in = load_carry(ci_ref)
        inc_from = onehot(bf_ref[...], buses)
        inc_to = onehot(bt_ref[...], buses)
        inc_gen = onehot(gb_ref[...], buses)
        stack = split3(rows(*state))
        pick_from = split4(take_split(stack, inc_from), nrow)
        pick_to = split4(take_split(stack, inc_to), nrow)
        if not first:
            pn_out[...] = take_split(stack, onehot(cp_ref[0:1].astype(jnp.int32), buses))
            prc_out[...] = take_split(stack, onehot(mir_ref[0:1].astype(jnp.int32) - 1, buses))
        prm_in = (bc_ref[...], bs_ref[...], bl_ref[...], bn_ref[...])
        carry_i, fi, ti = advance(carry_in, pick_from, pick_to, prm_in)
        totals = give(fi, inc_from) + give(ti, inc_to)
        for i in range(4):
            tot_out[i] = totals[i * nrow:(i + 1) * nrow]
        lin, quad, ramp, capr, capq = gl_ref[...], gq_ref[...], gr_ref[...], gcr_ref[...], gcq_ref[...]
        per = pe_ref[...]
        nb = (per > 0).astype(F32) + (per < horizon - 1).astype(F32)
        denom = 2.0 * quad + 1.0 + ramp * nb
        if first:
            ext = rows(sr_lo_ref[...], sr_ref[...], sr_hi_ref[...])
            g0 = jnp.clip((ext[scen:scen + window] - lin + ramp * (ext[0:window] + ext[2 * scen:2 * scen + window]))
                          / denom, 0.0, capr)
            g0 = jnp.where((per >= 0) & (per < horizon), g0, 0.0)
            gen_real = g0[scen:scen + nrow]
            gen_react = jnp.clip(sq_ref[...], -capq, capq)
            supply = give(rows(gen_real, gen_react), inc_gen)
            store_carry(ci_out, carry_i)
            g0_out[...] = g0
            gq0_out[...] = gen_react
        else:
            g0 = g0_ref[...]
            gp = take(rows(state[2], state[3]), inc_gen)
            gp_r, gp_q = gp[0:nrow], gp[nrow:]
            gen_real = jnp.clip(
                (g0[scen:scen + nrow] - 2.0 * gp_r - lin + ramp * (g0[0:nrow] + g0[2 * scen:2 * scen + nrow]))
                / denom[scen:scen + nrow],
                0.0,
                capr,
            )
            gen_react = jnp.clip(gq0_ref[...] - 2.0 * gp_q, -capq, capq)
            supply = give(rows(gen_real + gp_r, gen_react + gp_q), inc_gen)
            gr_out[...] = gen_real
            gq_out[...] = gen_react
        sup_out[0] = supply[0:nrow]
        sup_out[1] = supply[nrow:]

    def mirror0_kernel(mirror_ref, wm_ref, wa_ref, bf_ref, bt_ref, cn_ref, gb_ref, tot_out, cm_out, dg_out):
        mirror = mirror_ref[...]
        inc_recv = onehot(mirror[0:1].astype(jnp.int32) - 1, buses)
        degree = (col_sum(onehot(bf_ref[...], buses)) + col_sum(onehot(bt_ref[...], buses))
                  + col_sum(onehot(cn_ref[...], buses)) + col_sum(inc_recv))
        dg_out[...] = rows(degree, col_sum(onehot(gb_ref[...], buses)), jnp.zeros((6, buses), F32))
        zm = jnp.zeros((nrow, slots), F32)
        zero_b = jnp.zeros((nrow, buses), F32)
        stack = rows(wm_ref[...], wa_ref[...], zero_b, zero_b)
        pick_recv = split4(take(stack, inc_recv), nrow)
        near_mirror = (mirror[8:8 + nrow], mirror[8 + nrow:8 + 2 * nrow], zm, zm)
        prm_mir = (mirror[1:2], mirror[2:3], mirror[3:4], mirror[4:5])
        carry_m, _, tmr = advance(None, near_mirror, pick_recv, prm_mir)
        totals = give(tmr, inc_recv)
        for i in range(4):
            tot_out[i] = totals[i * nrow:(i + 1) * nrow]
        store_carry(cm_out, carry_m)

    def cut_part(first, refs):
        (st_ref, wm_ref, wa_ref, lr_ref, lq_ref, recv_ref, mirror_ref, slot_ref,
         dg_ref, cp_ref, tin_ref, sup_ref, tm_ref) = refs[:13]
        rest = refs[13:]
        cprm_v = cp_ref[...]
        wmv, wav = wm_ref[...], wa_ref[...]
        slot_t = slot_ref[...].astype(BF)
        mirror = mirror_ref[...]
        inc_near = onehot(cprm_v[0:1].astype(jnp.int32), buses)
        inc_recv = onehot(mirror[0:1].astype(jnp.int32) - 1, buses)
        degree = dg_ref[0:1]
        gen_count = dg_ref[1:2]
        prm_cut = (cprm_v[1:2], cprm_v[2:3], cprm_v[3:4], cprm_v[4:5])
        if first:
            (cc_out, st_out, pay_out, plane_ref) = rest
            zero_b = jnp.zeros((nrow, buses), F32)
            state = (wmv, wav, zero_b, zero_b)
            far_slot = recv_ref[...].T
            zc = jnp.zeros((nrow, cuts), F32)
            far_c = give(rows(far_slot[0:nrow], far_slot[nrow:2 * nrow]), slot_t)
            far_cross = (far_c[0:nrow], far_c[nrow:], zc, zc)
            warm_near = take(rows(wmv, wav), inc_near)
            pick_near = (warm_near[0:nrow], warm_near[nrow:], zc, zc)
            carry_c, fc, _ = advance(None, pick_near, far_cross, prm_cut)
            totals = tin_ref[...] + tm_ref[...] + give(fc, inc_near).reshape(4, nrow, buses)
        else:
            (cc_in_ref, cm_ref, pn_ref, prc_ref, mag_out, ang_out, pr_out, plane_ref) = rest
            state = tuple(st_ref[i] for i in range(4))
            blocks = []
            for p in range(3):
                for k in range(cap):
                    plane_ref[pl.ds(k, parts, stride=cap), :] = recv_ref[pl.ds(p * cap + k, parts, stride=3 * cap), :]
                blocks.append(plane_ref[...].T)
            both = rows(*blocks)
            near_mirror = split4(both[0:4 * nrow], nrow)
            far_cross = split4(give(both[4 * nrow:], slot_t), nrow)
            pick_near = split4(pn_ref[...], nrow)
            pick_recv = split4(prc_ref[...], nrow)
            carry_c_in = load_carry(cc_in_ref)
            carry_m_in = load_carry(cm_ref)
            _, fc, _ = advance(carry_c_in, pick_near, far_cross, prm_cut)
            prm_mir = (mirror[1:2], mirror[2:3], mirror[3:4], mirror[4:5])
            _, _, tmr = advance(carry_m_in, near_mirror, pick_recv, prm_mir)
            totals = tin_ref[...] + (give(fc, inc_near) + give(tmr, inc_recv)).reshape(4, nrow, buses)
        mag = (totals[0] + wmv) / (degree + 1.0)
        ang = (totals[1] + wav) / (degree + 1.0)
        weight = 1.0 + BALANCE_WEIGHT * (gen_count + degree)
        pr = BALANCE_WEIGHT * (sup_ref[0] - totals[2] - lr_ref[...]) / weight
        pq = BALANCE_WEIGHT * (sup_ref[1] - totals[3] - lq_ref[...]) / weight
        if first:
            store_carry(cc_out, carry_c)
            st_out[0] = mag
            st_out[1] = ang
            st_out[2] = pr
            st_out[3] = pq
            new_stack = split3(rows(mag, ang, pr, pq))
            near_slot = dot(inc_near, slot_t, NN).astype(BF)
            vals = rows(take_split(new_stack, near_slot), take_split(new_stack, inc_recv))
            for p in range(3):
                plane_ref[...] = vals[p * 128:(p + 1) * 128].T
                for k in range(cap):
                    pay_out[pl.ds(p * cap + k, parts, stride=3 * cap), :] = plane_ref[pl.ds(k, parts, stride=cap), :]
        else:
            mag_out[...] = mag
            ang_out[...] = ang
            pr_out[...] = pr

    sds = jax.ShapeDtypeStruct
    tot_shape = sds((4, nrow, buses), F32)
    br_all = br_rows
    gen_all = (*gen_rows, period_ext)
    tin0, sup0, ci1, g0, gq0 = vmem_call(
        lambda *refs: local_part(True, refs),
        (tot_shape, sds((2, nrow, buses), F32), sds((10, nrow, buses), F32), sds((window, gens), F32),
         sds((nrow, gens), F32)),
        wm, wa, *br_all, *gen_all, lo, sr, hi, sq,
    )
    tm0, cm1, dg = vmem_call(
        mirror0_kernel, (tot_shape, sds((10, nrow, slots), F32), sds((8, buses), F32)), mirror_t, wm, wa,
        br_rows[0], br_rows[1], cut_rows[0], gen_rows[0],
    )
    cprm = jnp.concatenate([cut_rows[0].astype(F32), *cut_rows[1:], jnp.zeros((3, cuts), F32)], axis=0)
    cc1, st1, pay_1 = vmem_call(
        lambda *refs: cut_part(True, refs),
        (sds((10, nrow, cuts), F32), tot_shape, sds((3 * slots, 128), F32)),
        wm, wm, wa, lr, lq, recv_0, mirror_t, slot_t, dg, cprm, tin0, sup0, tm0,
        scratch=[pltpu.VMEM((slots, 128), F32)],
    )
    recv_1 = lax.all_to_all(pay_1.reshape(3 * parts, 2, 128), "net", 0, 0, tiled=True).reshape(3 * slots, 128)
    tin1, sup1, gr, gq, pn1, prc1 = vmem_call(
        lambda *refs: local_part(False, refs),
        (tot_shape, sds((2, nrow, buses), F32), sds((nrow, gens), F32), sds((nrow, gens), F32),
         sds((4 * nrow, cuts), F32), sds((4 * nrow, slots), F32)),
        st1, *br_all, *gen_all, ci1, g0, gq0, cprm, mirror_t,
    )
    mag, ang, pr = vmem_call(
        lambda *refs: cut_part(False, refs),
        (sds((nrow, buses), F32), sds((nrow, buses), F32), sds((nrow, buses), F32)),
        st1, wm, wa, lr, lq, recv_1, mirror_t, slot_t, dg, cprm, tin1, sup1, tin1,
        cc1, cm1, pn1, prc1,
        scratch=[pltpu.VMEM((slots, 128), F32)],
    )
    shape_b = (periods, scen, buses)
    shape_g = (periods, scen, gens)
    return (mag.reshape(shape_b), ang.reshape(shape_b), pr.reshape(shape_b), gr.reshape(shape_g),
            gq.reshape(shape_g))


def solution(mesh):
    bus = P("tm", None, "net")
    one = P("net")
    return jax.shard_map(
        on_device,
        mesh=mesh,
        in_specs=(bus,) * 6 + (one,) * 12 + (one, P("net", None)) + (one,) * 5,
        out_specs=(bus,) * 5,
        check_vma=False,
    )
```

```python
import jax
import jax.numpy as jnp
from jax import lax
from jax.experimental import pallas as pl
from jax.experimental.pallas import tpu as pltpu
from jax.sharding import PartitionSpec as P

INNER = 4
STEP_SIZE = 0.0005
RADIUS = 0.05
BALANCE_WEIGHT = 2.0
HI = lax.Precision.HIGHEST
F32 = jnp.float32


NN = (((1,), (0,)), ((), ()))
NT = (((1,), (1,)), ((), ()))
BF = jnp.bfloat16


def split3(x):
    hi = x.astype(BF)
    r = x - hi.astype(F32)
    mid = r.astype(BF)
    lo = (r - mid.astype(F32)).astype(BF)
    return hi, mid, lo


def dot(a, b, dims):
    return lax.dot_general(a, b, dims, preferred_element_type=F32)


def take_split(parts, oh):
    hi, mid, lo = parts
    return (dot(hi, oh, NN) + dot(mid, oh, NN)) + dot(lo, oh, NN)


def take(vals, oh):
    hi, mid, lo = split3(vals)
    return (dot(hi, oh, NN) + dot(mid, oh, NN)) + dot(lo, oh, NN)


def give(vals, oh):
    hi, mid, lo = split3(vals)
    return (dot(hi, oh, NT) + dot(mid, oh, NT)) + dot(lo, oh, NT)


def take_left(oh, vals):
    hi, mid, lo = split3(vals)
    return (dot(oh, hi, NN) + dot(oh, mid, NN)) + dot(oh, lo, NN)


def give_left(oh, vals):
    hi, mid, lo = split3(vals)
    return (dot(oh, hi, NT) + dot(oh, mid, NT)) + dot(oh, lo, NT)


def onehot(ids_row, count):
    n = ids_row.shape[1]
    return (lax.broadcasted_iota(jnp.int32, (count, n), 0) == ids_row).astype(BF)


def col_sum(inc):
    return dot(jnp.ones((8, inc.shape[1]), BF), inc, NT)[0:1]


def rows(*parts):
    return jnp.concatenate(parts, axis=0)


def trig(x):
    d = x[1] - x[3]
    return (jnp.cos(d), jnp.sin(d))


def flows(x, cs, g, b):
    mf, _, mt, _ = x
    c, s = cs
    p = mf * mt
    return (
        g * mf * mf - p * (g * c + b * s),
        -b * mf * mf - p * (g * s - b * c),
        g * mt * mt - p * (g * c - b * s),
        -b * mt * mt + p * (g * s + b * c),
    )


def energy_grad(x, cs, f, t, ft, g, b, l2):
    mf, af, mt, at = x
    c, s = cs
    p = mf * mt
    ka = g * c + b * s
    kb = g * s - b * c
    kc = g * c - b * s
    kd = g * s + b * c
    if f is None:
        f = (g * mf * mf - p * ka, -b * mf * mf - p * kb, g * mt * mt - p * kc, -b * mt * mt + p * kd)
    f0, f1, f2, f3 = f
    ef = jnp.maximum(f0 * f0 + f1 * f1 - l2, 0.0)
    et = jnp.maximum(f2 * f2 + f3 * f3 - l2, 0.0)
    w0 = (f0 - ft[0]) + 2.0 * ef * f0
    w1 = (f1 - ft[1]) + 2.0 * ef * f1
    w2 = (f2 - ft[2]) + 2.0 * et * f2
    w3 = (f3 - ft[3]) + 2.0 * et * f3
    g_mf = (mf - t[0]) + w0 * (2.0 * g * mf - mt * ka) - w1 * (2.0 * b * mf + mt * kb) - w2 * mt * kc + w3 * mt * kd
    g_mt = (mt - t[2]) - w0 * mf * ka - w1 * mf * kb + w2 * (2.0 * g * mt - mf * kc) - w3 * (2.0 * b * mt - mf * kd)
    g_d = p * (w0 * kb - w1 * ka + w2 * kd + w3 * kc)
    return (g_mf, (af - t[1]) + g_d, g_mt, (at - t[3]) - g_d)


def solve(x, cs, f, t, ft, g, b, l2, steps):
    for attempt in range(INNER):
        if cs is None:
            cs = trig(x)
        grad = energy_grad(x, cs, f, t, ft, g, b, l2)
        x = tuple(
            jnp.where(attempt < steps, xi - jnp.clip(STEP_SIZE * gi, -RADIUS, RADIUS), xi)
            for xi, gi in zip(x, grad)
        )
        cs, f = None, None
    return x


def advance(carry, near, far, prm):
    g, b, lim, steps = prm
    ends = (near[0], near[1], far[0], far[1])
    prices = (near[2], near[3], far[2], far[3])
    if carry is None:
        copies = ends
        cs = trig(copies)
        flow_prev = flows(copies, cs, g, b)
        volt = tuple(jnp.zeros_like(e) for e in ends)
        target = ends
        flow_target = flow_prev
        dual_flow = volt
    else:
        copies, flow_prev, cs = carry
        volt = tuple(c - e for c, e in zip(copies, ends))
        target = tuple(e - v for e, v in zip(ends, volt))
        flow_target = tuple(f + 2.0 * q for f, q in zip(flow_prev, prices))
        dual_flow = tuple(-q for q in prices)
    copies = solve(copies, cs, flow_prev, target, flow_target, g, b, lim * lim, steps)
    cs = trig(copies)
    flow_prev = flows(copies, cs, g, b)
    side_from = rows(
        copies[0] + volt[0], copies[1] + volt[1], flow_prev[0] + dual_flow[0], flow_prev[1] + dual_flow[1]
    )
    side_to = rows(
        copies[2] + volt[2], copies[3] + volt[3], flow_prev[2] + dual_flow[2], flow_prev[3] + dual_flow[3]
    )
    return (copies, flow_prev, cs), side_from, side_to


def store_carry(ref, carry):
    for i in range(4):
        ref[i] = carry[0][i]
        ref[4 + i] = carry[1][i]
    ref[8] = carry[2][0]
    ref[9] = carry[2][1]


def load_carry(ref):
    return (tuple(ref[i] for i in range(4)), tuple(ref[4 + i] for i in range(4)), (ref[8], ref[9]))


def split4(a, n):
    return tuple(a[i * n:(i + 1) * n] for i in range(4))


def vmem_call(kernel, outs, *args, scratch=()):
    return pl.pallas_call(
        kernel,
        out_shape=outs,
        in_specs=[pl.BlockSpec(memory_space=pltpu.VMEM)] * len(args),
        out_specs=tuple(pl.BlockSpec(memory_space=pltpu.VMEM) for _ in outs),
        scratch_shapes=scratch,
        compiler_params=pltpu.CompilerParams(vmem_limit_bytes=48 * 1024 * 1024),
    )(*args)


def on_device(
    warm_mag, warm_angle, load_real, load_react, start_real, start_react,
    gen_bus, gen_linear, gen_quad, gen_ramp, gen_cap_real, gen_cap_react,
    branch_from, branch_to, branch_cond, branch_susc, branch_limit, branch_steps,
    cut_near, cut_peer, cut_bus, cut_cond, cut_susc, cut_limit, cut_steps,
):
    periods, scen, buses = warm_mag.shape
    nrow = periods * scen
    cuts = cut_near.shape[0]
    parts = lax.axis_size("net")
    cap = max(2, cuts // parts * 2)
    slots = parts * cap
    gens = gen_bus.shape[0]
    ntm = lax.axis_size("tm")
    horizon = periods * ntm

    def row(v):
        return v.reshape(1, -1)

    wm = warm_mag.reshape(nrow, buses)
    wa = warm_angle.reshape(nrow, buses)
    lr = load_real.reshape(nrow, buses)
    lq = load_react.reshape(nrow, buses)
    sr = start_real.reshape(nrow, gens)
    sq = start_react.reshape(nrow, gens)
    halo = 2 * scen
    lo = lax.ppermute(sr[nrow - halo:], "tm", [(i, i + 1) for i in range(ntm - 1)])
    hi = lax.ppermute(sr[:halo], "tm", [(i + 1, i) for i in range(ntm - 1)])
    window = nrow + 2 * scen
    period_ext = (
        lax.axis_index("tm") * periods - 1 + jnp.arange(window, dtype=jnp.int32) // scen
    ).reshape(window, 1)
    gen_rows = (row(gen_bus), row(gen_linear), row(gen_quad), row(gen_ramp), row(gen_cap_real), row(gen_cap_react))
    br_rows = (row(branch_from), row(branch_to), row(branch_cond), row(branch_susc), row(branch_limit),
               row(branch_steps.astype(F32)))
    cut_rows = (row(cut_near), row(cut_cond), row(cut_susc), row(cut_limit), row(cut_steps.astype(F32)))
    cut_bus_row = row(cut_bus.astype(F32))
    nvals0 = 128

    def prep_kernel(peer_hbm, near_hbm, bus_hbm, cond_hbm, susc_hbm, lim_hbm, steps_hbm, wm_hbm, wa_hbm,
                    slot_out, pay_out,
                    peer_ref, near_ref, bus_ref, cond_ref, susc_ref, lim_ref, steps_ref, wm_ref, wa_ref, sems):
        pairs = ((peer_hbm, peer_ref), (near_hbm, near_ref), (bus_hbm, bus_ref), (cond_hbm, cond_ref),
                 (susc_hbm, susc_ref), (lim_hbm, lim_ref), (steps_hbm, steps_ref), (wm_hbm, wm_ref),
                 (wa_hbm, wa_ref))
        copies = [pltpu.make_async_copy(src, dst, sems.at[i]) for i, (src, dst) in enumerate(pairs)]
        for cp in copies:
            cp.start()
        copies[0].wait()
        peer = peer_ref[...]
        mine_t = (lax.broadcasted_iota(jnp.int32, (parts, cuts), 0) == peer).astype(F32)
        same = dot(mine_t.T.astype(BF), mine_t.astype(BF), NN)
        earlier = lax.broadcasted_iota(jnp.int32, (cuts, cuts), 0) < lax.broadcasted_iota(jnp.int32, (cuts, cuts), 1)
        rank = jnp.sum(jnp.where(earlier, same, 0.0), axis=0, keepdims=True)
        position = peer.astype(F32) * cap + rank
        slot_t = (lax.broadcasted_iota(jnp.int32, (slots, cuts), 0).astype(F32) == position).astype(F32).T
        slot_b = slot_t.astype(BF)
        slot_out[...] = slot_t
        copies[1].wait()
        inc_near = onehot(near_ref[...], buses)
        by_slot = dot(inc_near, slot_b, NN).astype(BF)
        for cp in copies[2:]:
            cp.wait()
        prm = rows(bus_ref[...].astype(F32) + 1.0, cond_ref[...], susc_ref[...], lim_ref[...],
                   steps_ref[...].astype(F32), jnp.zeros((3, cuts), F32))
        vals = rows(
            take(prm, slot_b),
            take(rows(wm_ref[...], wa_ref[...]), by_slot),
            jnp.zeros((nvals0 - 8 - 2 * nrow, slots), F32),
        )
        pay_out[...] = vals.T

    prep_args = (row(cut_peer), cut_rows[0], row(cut_bus), cut_rows[1], cut_rows[2], cut_rows[3], row(cut_steps),
                 wm, wa)
    slot_t, pay_setup = pl.pallas_call(
        prep_kernel,
        out_shape=(jax.ShapeDtypeStruct((cuts, slots), F32), jax.ShapeDtypeStruct((slots, nvals0), F32)),
        in_specs=[pl.BlockSpec(memory_space=pl.ANY)] * len(prep_args),
        out_specs=(pl.BlockSpec(memory_space=pltpu.VMEM), pl.BlockSpec(memory_space=pltpu.VMEM)),
        scratch_shapes=[pltpu.VMEM(a.shape, a.dtype) for a in prep_args] + [pltpu.SemaphoreType.DMA((len(prep_args),))],
    )(*prep_args)
    recv_setup = lax.all_to_all(pay_setup, "net", 0, 0, tiled=True)

    def mid_kernel(recv_ref, wm_ref, wa_ref, pay_out):
        ids = recv_ref[:, 0:1].astype(jnp.int32) - 1
        inc_t = (ids == lax.broadcasted_iota(jnp.int32, (slots, buses), 1)).astype(BF)
        warm = rows(wm_ref[...], wa_ref[...], jnp.zeros((nvals0 - 2 * nrow, buses), F32))
        pay_out[...] = give_left(inc_t, warm)

    pay_0 = vmem_call(
        mid_kernel, (jax.ShapeDtypeStruct((slots, nvals0), F32),), recv_setup, wm, wa,
    )[0]
    recv_0 = lax.all_to_all(pay_0, "net", 0, 0, tiled=True)

    def spread(p):
        return (lax.broadcasted_iota(jnp.int32, (3 * slots, slots), 0)
                == 3 * lax.broadcasted_iota(jnp.int32, (3 * slots, slots), 1) + p).astype(BF)

    def local_part(first, refs):
        if first:
            (wm_ref, wa_ref, bf_ref, bt_ref, bc_ref, bs_ref, bl_ref, bn_ref,
             gb_ref, gl_ref, gq_ref, gr_ref, gcr_ref, gcq_ref, pe_ref,
             sr_lo_ref, sr_ref, sr_hi_ref, sq_ref,
             tot_out, sup_out, ci_out, g0_out, gq0_out) = refs
            zero_b = jnp.zeros((nrow, buses), F32)
            state = (wm_ref[...], wa_ref[...], zero_b, zero_b)
            carry_in = None
        else:
            (st_ref, bf_ref, bt_ref, bc_ref, bs_ref, bl_ref, bn_ref,
             gb_ref, gl_ref, gq_ref, gr_ref, gcr_ref, gcq_ref, pe_ref,
             ci_ref, g0_ref, gq0_ref, cp_ref, mir_ref,
             tot_out, sup_out, gr_out, gq_out, pn_out, prc_out) = refs
            state = tuple(st_ref[i] for i in range(4))
            carry_in = load_carry(ci_ref)
        inc_from = onehot(bf_ref[...], buses)
        inc_to = onehot(bt_ref[...], buses)
        inc_gen = onehot(gb_ref[...], buses)
        stack = split3(rows(*state))
        pick_from = split4(take_split(stack, inc_from), nrow)
        pick_to = split4(take_split(stack, inc_to), nrow)
        if not first:
            pn_out[...] = take_split(stack, onehot(cp_ref[0:1].astype(jnp.int32), buses))
            prc_out[...] = take_split(stack, onehot(mir_ref[0:1].astype(jnp.int32) - 1, buses))
        prm_in = (bc_ref[...], bs_ref[...], bl_ref[...], bn_ref[...])
        carry_i, fi, ti = advance(carry_in, pick_from, pick_to, prm_in)
        totals = give(fi, inc_from) + give(ti, inc_to)
        for i in range(4):
            tot_out[i] = totals[i * nrow:(i + 1) * nrow]
        lin, quad, ramp, capr, capq = gl_ref[...], gq_ref[...], gr_ref[...], gcr_ref[...], gcq_ref[...]
        per = pe_ref[...]
        nb = (per > 0).astype(F32) + (per < horizon - 1).astype(F32)
        denom = 2.0 * quad + 1.0 + ramp * nb
        if first:
            ext = rows(sr_lo_ref[...], sr_ref[...], sr_hi_ref[...])
            g0 = jnp.clip((ext[scen:scen + window] - lin + ramp * (ext[0:window] + ext[2 * scen:2 * scen + window]))
                          / denom, 0.0, capr)
            g0 = jnp.where((per >= 0) & (per < horizon), g0, 0.0)
            gen_real = g0[scen:scen + nrow]
            gen_react = jnp.clip(sq_ref[...], -capq, capq)
            supply = give(rows(gen_real, gen_react), inc_gen)
            store_carry(ci_out, carry_i)
            g0_out[...] = g0
            gq0_out[...] = gen_react
        else:
            g0 = g0_ref[...]
            gp = take(rows(state[2], state[3]), inc_gen)
            gp_r, gp_q = gp[0:nrow], gp[nrow:]
            gen_real = jnp.clip(
                (g0[scen:scen + nrow] - 2.0 * gp_r - lin + ramp * (g0[0:nrow] + g0[2 * scen:2 * scen + nrow]))
                / denom[scen:scen + nrow],
                0.0,
                capr,
            )
            gen_react = jnp.clip(gq0_ref[...] - 2.0 * gp_q, -capq, capq)
            supply = give(rows(gen_real + gp_r, gen_react + gp_q), inc_gen)
            gr_out[...] = gen_real
            gq_out[...] = gen_react
        sup_out[0] = supply[0:nrow]
        sup_out[1] = supply[nrow:]

    def mirror0_kernel(recv_ref, wm_ref, wa_ref, bf_ref, bt_ref, cn_ref, gb_ref, tot_out, cm_out, dg_out, mir_out):
        mirror = recv_ref[...].T
        mir_out[...] = mirror
        inc_recv = onehot(mirror[0:1].astype(jnp.int32) - 1, buses)
        degree = (col_sum(onehot(bf_ref[...], buses)) + col_sum(onehot(bt_ref[...], buses))
                  + col_sum(onehot(cn_ref[...], buses)) + col_sum(inc_recv))
        dg_out[...] = rows(degree, col_sum(onehot(gb_ref[...], buses)), jnp.zeros((6, buses), F32))
        zm = jnp.zeros((nrow, slots), F32)
        zero_b = jnp.zeros((nrow, buses), F32)
        stack = rows(wm_ref[...], wa_ref[...], zero_b, zero_b)
        pick_recv = split4(take(stack, inc_recv), nrow)
        near_mirror = (mirror[8:8 + nrow], mirror[8 + nrow:8 + 2 * nrow], zm, zm)
        prm_mir = (mirror[1:2], mirror[2:3], mirror[3:4], mirror[4:5])
        carry_m, _, tmr = advance(None, near_mirror, pick_recv, prm_mir)
        totals = give(tmr, inc_recv)
        for i in range(4):
            tot_out[i] = totals[i * nrow:(i + 1) * nrow]
        store_carry(cm_out, carry_m)

    def cut_part(first, refs):
        (st_ref, wm_ref, wa_ref, lr_ref, lq_ref, recv_ref, mirror_ref, slot_ref,
         dg_ref, cp_ref, tin_ref, sup_ref, tm_ref) = refs[:13]
        rest = refs[13:]
        cprm_v = cp_ref[...]
        wmv, wav = wm_ref[...], wa_ref[...]
        slot_t = slot_ref[...].astype(BF)
        mirror = mirror_ref[...]
        inc_near = onehot(cprm_v[0:1].astype(jnp.int32), buses)
        inc_recv = onehot(mirror[0:1].astype(jnp.int32) - 1, buses)
        degree = dg_ref[0:1]
        gen_count = dg_ref[1:2]
        prm_cut = (cprm_v[1:2], cprm_v[2:3], cprm_v[3:4], cprm_v[4:5])
        if first:
            (cc_out, st_out, pay_out, plane_ref) = rest
            zero_b = jnp.zeros((nrow, buses), F32)
            state = (wmv, wav, zero_b, zero_b)
            far_slot = recv_ref[...].T
            zc = jnp.zeros((nrow, cuts), F32)
            far_c = give(rows(far_slot[0:nrow], far_slot[nrow:2 * nrow]), slot_t)
            far_cross = (far_c[0:nrow], far_c[nrow:], zc, zc)
            warm_near = take(rows(wmv, wav), inc_near)
            pick_near = (warm_near[0:nrow], warm_near[nrow:], zc, zc)
            carry_c, fc, _ = advance(None, pick_near, far_cross, prm_cut)
            totals = tin_ref[...] + tm_ref[...] + give(fc, inc_near).reshape(4, nrow, buses)
        else:
            (cc_in_ref, cm_ref, pn_ref, prc_ref, mag_out, ang_out, pr_out, plane_ref) = rest
            state = tuple(st_ref[i] for i in range(4))
            blocks = []
            for p in range(3):
                for k in range(cap):
                    plane_ref[pl.ds(k, parts, stride=cap), :] = recv_ref[pl.ds(p * cap + k, parts, stride=3 * cap), :]
                blocks.append(plane_ref[...].T)
            both = rows(*blocks)
            near_mirror = split4(both[0:4 * nrow], nrow)
            far_cross = split4(give(both[4 * nrow:], slot_t), nrow)
            pick_near = split4(pn_ref[...], nrow)
            pick_recv = split4(prc_ref[...], nrow)
            carry_c_in = load_carry(cc_in_ref)
            carry_m_in = load_carry(cm_ref)
            _, fc, _ = advance(carry_c_in, pick_near, far_cross, prm_cut)
            prm_mir = (mirror[1:2], mirror[2:3], mirror[3:4], mirror[4:5])
            _, _, tmr = advance(carry_m_in, near_mirror, pick_recv, prm_mir)
            totals = tin_ref[...] + (give(fc, inc_near) + give(tmr, inc_recv)).reshape(4, nrow, buses)
        mag = (totals[0] + wmv) / (degree + 1.0)
        ang = (totals[1] + wav) / (degree + 1.0)
        weight = 1.0 + BALANCE_WEIGHT * (gen_count + degree)
        pr = BALANCE_WEIGHT * (sup_ref[0] - totals[2] - lr_ref[...]) / weight
        pq = BALANCE_WEIGHT * (sup_ref[1] - totals[3] - lq_ref[...]) / weight
        if first:
            store_carry(cc_out, carry_c)
            st_out[0] = mag
            st_out[1] = ang
            st_out[2] = pr
            st_out[3] = pq
            new_stack = split3(rows(mag, ang, pr, pq))
            near_slot = dot(inc_near, slot_t, NN).astype(BF)
            vals = rows(take_split(new_stack, near_slot), take_split(new_stack, inc_recv))
            for p in range(3):
                plane_ref[...] = vals[p * 128:(p + 1) * 128].T
                for k in range(cap):
                    pay_out[pl.ds(p * cap + k, parts, stride=3 * cap), :] = plane_ref[pl.ds(k, parts, stride=cap), :]
        else:
            mag_out[...] = mag
            ang_out[...] = ang
            pr_out[...] = pr

    sds = jax.ShapeDtypeStruct
    tot_shape = sds((4, nrow, buses), F32)
    br_all = br_rows
    gen_all = (*gen_rows, period_ext)
    tin0, sup0, ci1, g0, gq0 = vmem_call(
        lambda *refs: local_part(True, refs),
        (tot_shape, sds((2, nrow, buses), F32), sds((10, nrow, buses), F32), sds((window, gens), F32),
         sds((nrow, gens), F32)),
        wm, wa, *br_all, *gen_all, lo, sr, hi, sq,
    )
    tm0, cm1, dg, mirror_t = vmem_call(
        mirror0_kernel,
        (tot_shape, sds((10, nrow, slots), F32), sds((8, buses), F32), sds((nvals0, slots), F32)), recv_setup, wm, wa,
        br_rows[0], br_rows[1], cut_rows[0], gen_rows[0],
    )
    cprm = jnp.concatenate([cut_rows[0].astype(F32), *cut_rows[1:], jnp.zeros((3, cuts), F32)], axis=0)
    cc1, st1, pay_1 = vmem_call(
        lambda *refs: cut_part(True, refs),
        (sds((10, nrow, cuts), F32), tot_shape, sds((3 * slots, 128), F32)),
        wm, wm, wa, lr, lq, recv_0, mirror_t, slot_t, dg, cprm, tin0, sup0, tm0,
        scratch=[pltpu.VMEM((slots, 128), F32)],
    )
    recv_1 = lax.all_to_all(pay_1.reshape(3 * parts, 2, 128), "net", 0, 0, tiled=True).reshape(3 * slots, 128)
    tin1, sup1, gr, gq, pn1, prc1 = vmem_call(
        lambda *refs: local_part(False, refs),
        (tot_shape, sds((2, nrow, buses), F32), sds((nrow, gens), F32), sds((nrow, gens), F32),
         sds((4 * nrow, cuts), F32), sds((4 * nrow, slots), F32)),
        st1, *br_all, *gen_all, ci1, g0, gq0, cprm, mirror_t,
    )
    mag, ang, pr = vmem_call(
        lambda *refs: cut_part(False, refs),
        (sds((nrow, buses), F32), sds((nrow, buses), F32), sds((nrow, buses), F32)),
        st1, wm, wa, lr, lq, recv_1, mirror_t, slot_t, dg, cprm, tin1, sup1, tin1,
        cc1, cm1, pn1, prc1,
        scratch=[pltpu.VMEM((slots, 128), F32)],
    )
    shape_b = (periods, scen, buses)
    shape_g = (periods, scen, gens)
    return (mag.reshape(shape_b), ang.reshape(shape_b), pr.reshape(shape_b), gr.reshape(shape_g),
            gq.reshape(shape_g))


def solution(mesh):
    bus = P("tm", None, "net")
    one = P("net")
    return jax.shard_map(
        on_device,
        mesh=mesh,
        in_specs=(bus,) * 6 + (one,) * 12 + (one, P("net", None)) + (one,) * 5,
        out_specs=(bus,) * 5,
        check_vma=False,
    )
```

```python
import jax
import jax.numpy as jnp
from jax import lax
from jax.experimental import pallas as pl
from jax.experimental.pallas import tpu as pltpu
from jax.sharding import PartitionSpec as P

INNER = 4
STEP_SIZE = 0.0005
RADIUS = 0.05
BALANCE_WEIGHT = 2.0
HI = lax.Precision.HIGHEST
F32 = jnp.float32


NN = (((1,), (0,)), ((), ()))
NT = (((1,), (1,)), ((), ()))
BF = jnp.bfloat16


def split3(x):
    hi = x.astype(BF)
    r = x - hi.astype(F32)
    mid = r.astype(BF)
    lo = (r - mid.astype(F32)).astype(BF)
    return hi, mid, lo


def dot(a, b, dims):
    return lax.dot_general(a, b, dims, preferred_element_type=F32)


def take_split(parts, oh):
    hi, mid, lo = parts
    return (dot(hi, oh, NN) + dot(mid, oh, NN)) + dot(lo, oh, NN)


def take(vals, oh):
    hi, mid, lo = split3(vals)
    return (dot(hi, oh, NN) + dot(mid, oh, NN)) + dot(lo, oh, NN)


def give(vals, oh):
    hi, mid, lo = split3(vals)
    return (dot(hi, oh, NT) + dot(mid, oh, NT)) + dot(lo, oh, NT)


def take_left(oh, vals):
    hi, mid, lo = split3(vals)
    return (dot(oh, hi, NN) + dot(oh, mid, NN)) + dot(oh, lo, NN)


def give_left(oh, vals):
    hi, mid, lo = split3(vals)
    return (dot(oh, hi, NT) + dot(oh, mid, NT)) + dot(oh, lo, NT)


def onehot(ids_row, count):
    n = ids_row.shape[1]
    return (lax.broadcasted_iota(jnp.int32, (count, n), 0) == ids_row).astype(BF)


def col_sum(inc):
    return dot(jnp.ones((8, inc.shape[1]), BF), inc, NT)[0:1]


def rows(*parts):
    return jnp.concatenate(parts, axis=0)


def trig(x):
    d = x[1] - x[3]
    return (jnp.cos(d), jnp.sin(d))


def flows(x, cs, g, b):
    mf, _, mt, _ = x
    c, s = cs
    p = mf * mt
    return (
        g * mf * mf - p * (g * c + b * s),
        -b * mf * mf - p * (g * s - b * c),
        g * mt * mt - p * (g * c - b * s),
        -b * mt * mt + p * (g * s + b * c),
    )


def energy_grad(x, cs, f, t, ft, g, b, l2):
    mf, af, mt, at = x
    c, s = cs
    p = mf * mt
    ka = g * c + b * s
    kb = g * s - b * c
    kc = g * c - b * s
    kd = g * s + b * c
    if f is None:
        f = (g * mf * mf - p * ka, -b * mf * mf - p * kb, g * mt * mt - p * kc, -b * mt * mt + p * kd)
    f0, f1, f2, f3 = f
    ef = jnp.maximum(f0 * f0 + f1 * f1 - l2, 0.0)
    et = jnp.maximum(f2 * f2 + f3 * f3 - l2, 0.0)
    w0 = (f0 - ft[0]) + 2.0 * ef * f0
    w1 = (f1 - ft[1]) + 2.0 * ef * f1
    w2 = (f2 - ft[2]) + 2.0 * et * f2
    w3 = (f3 - ft[3]) + 2.0 * et * f3
    g_mf = (mf - t[0]) + w0 * (2.0 * g * mf - mt * ka) - w1 * (2.0 * b * mf + mt * kb) - w2 * mt * kc + w3 * mt * kd
    g_mt = (mt - t[2]) - w0 * mf * ka - w1 * mf * kb + w2 * (2.0 * g * mt - mf * kc) - w3 * (2.0 * b * mt - mf * kd)
    g_d = p * (w0 * kb - w1 * ka + w2 * kd + w3 * kc)
    return (g_mf, (af - t[1]) + g_d, g_mt, (at - t[3]) - g_d)


def solve(x, cs, f, t, ft, g, b, l2, steps):
    for attempt in range(INNER):
        if cs is None:
            cs = trig(x)
        grad = energy_grad(x, cs, f, t, ft, g, b, l2)
        x = tuple(
            jnp.where(attempt < steps, xi - jnp.clip(STEP_SIZE * gi, -RADIUS, RADIUS), xi)
            for xi, gi in zip(x, grad)
        )
        cs, f = None, None
    return x


def advance(carry, near, far, prm):
    g, b, lim, steps = prm
    ends = (near[0], near[1], far[0], far[1])
    prices = (near[2], near[3], far[2], far[3])
    if carry is None:
        copies = ends
        cs = trig(copies)
        flow_prev = flows(copies, cs, g, b)
        volt = tuple(jnp.zeros_like(e) for e in ends)
        target = ends
        flow_target = flow_prev
        dual_flow = volt
    else:
        copies, flow_prev, cs = carry
        volt = tuple(c - e for c, e in zip(copies, ends))
        target = tuple(e - v for e, v in zip(ends, volt))
        flow_target = tuple(f + 2.0 * q for f, q in zip(flow_prev, prices))
        dual_flow = tuple(-q for q in prices)
    copies = solve(copies, cs, flow_prev, target, flow_target, g, b, lim * lim, steps)
    cs = trig(copies)
    flow_prev = flows(copies, cs, g, b)
    side_from = rows(
        copies[0] + volt[0], copies[1] + volt[1], flow_prev[0] + dual_flow[0], flow_prev[1] + dual_flow[1]
    )
    side_to = rows(
        copies[2] + volt[2], copies[3] + volt[3], flow_prev[2] + dual_flow[2], flow_prev[3] + dual_flow[3]
    )
    return (copies, flow_prev, cs), side_from, side_to


def store_carry(ref, carry):
    for i in range(4):
        ref[i] = carry[0][i]
        ref[4 + i] = carry[1][i]
    ref[8] = carry[2][0]
    ref[9] = carry[2][1]


def load_carry(ref):
    return (tuple(ref[i] for i in range(4)), tuple(ref[4 + i] for i in range(4)), (ref[8], ref[9]))


def split4(a, n):
    return tuple(a[i * n:(i + 1) * n] for i in range(4))


def vmem_call(kernel, outs, *args, scratch=()):
    return pl.pallas_call(
        kernel,
        out_shape=outs,
        in_specs=[pl.BlockSpec(memory_space=pltpu.VMEM)] * len(args),
        out_specs=tuple(pl.BlockSpec(memory_space=pltpu.VMEM) for _ in outs),
        scratch_shapes=scratch,
        compiler_params=pltpu.CompilerParams(vmem_limit_bytes=48 * 1024 * 1024),
    )(*args)


def on_device(
    warm_mag, warm_angle, load_real, load_react, start_real, start_react,
    gen_bus, gen_linear, gen_quad, gen_ramp, gen_cap_real, gen_cap_react,
    branch_from, branch_to, branch_cond, branch_susc, branch_limit, branch_steps,
    cut_near, cut_peer, cut_bus, cut_cond, cut_susc, cut_limit, cut_steps,
):
    periods, scen, buses = warm_mag.shape
    nrow = periods * scen
    cuts = cut_near.shape[0]
    parts = lax.axis_size("net")
    cap = max(2, cuts // parts * 2)
    slots = parts * cap
    gens = gen_bus.shape[0]
    ntm = lax.axis_size("tm")
    horizon = periods * ntm

    def row(v):
        return v.reshape(1, -1)

    wm = warm_mag.reshape(nrow, buses)
    wa = warm_angle.reshape(nrow, buses)
    lr = load_real.reshape(nrow, buses)
    lq = load_react.reshape(nrow, buses)
    sr = start_real.reshape(nrow, gens)
    sq = start_react.reshape(nrow, gens)
    halo = 2 * scen
    lo = lax.ppermute(sr[nrow - halo:], "tm", [(i, i + 1) for i in range(ntm - 1)])
    hi = lax.ppermute(sr[:halo], "tm", [(i + 1, i) for i in range(ntm - 1)])
    window = nrow + 2 * scen
    period_ext = (
        lax.axis_index("tm") * periods - 1 + jnp.arange(window, dtype=jnp.int32) // scen
    ).reshape(window, 1)
    gen_rows = (row(gen_bus), row(gen_linear), row(gen_quad), row(gen_ramp), row(gen_cap_real), row(gen_cap_react))
    br_rows = (row(branch_from), row(branch_to), row(branch_cond), row(branch_susc), row(branch_limit),
               row(branch_steps.astype(F32)))
    cut_rows = (row(cut_near), row(cut_cond), row(cut_susc), row(cut_limit), row(cut_steps.astype(F32)))
    cut_bus_row = row(cut_bus.astype(F32))
    nvals0 = 128

    def prep_kernel(peer_hbm, near_hbm, bus_hbm, cond_hbm, susc_hbm, lim_hbm, steps_hbm, wm_hbm, wa_hbm,
                    slot_out, pay_out,
                    peer_ref, near_ref, bus_ref, cond_ref, susc_ref, lim_ref, steps_ref, wm_ref, wa_ref, sems):
        pairs = ((peer_hbm, peer_ref), (near_hbm, near_ref), (bus_hbm, bus_ref), (cond_hbm, cond_ref),
                 (susc_hbm, susc_ref), (lim_hbm, lim_ref), (steps_hbm, steps_ref), (wm_hbm, wm_ref),
                 (wa_hbm, wa_ref))
        copies = [pltpu.make_async_copy(src, dst, sems.at[i]) for i, (src, dst) in enumerate(pairs)]
        for cp in copies:
            cp.start()
        copies[0].wait()
        peer = peer_ref[...]
        mine_t = (lax.broadcasted_iota(jnp.int32, (parts, cuts), 0) == peer).astype(F32)
        same = dot(mine_t.T.astype(BF), mine_t.astype(BF), NN)
        earlier = lax.broadcasted_iota(jnp.int32, (cuts, cuts), 0) < lax.broadcasted_iota(jnp.int32, (cuts, cuts), 1)
        rank = jnp.sum(jnp.where(earlier, same, 0.0), axis=0, keepdims=True)
        position = peer.astype(F32) * cap + rank
        slot_t = (lax.broadcasted_iota(jnp.int32, (slots, cuts), 0).astype(F32) == position).astype(F32).T
        slot_b = slot_t.astype(BF)
        slot_out[...] = slot_t
        copies[1].wait()
        inc_near = onehot(near_ref[...], buses)
        by_slot = dot(inc_near, slot_b, NN).astype(BF)
        for cp in copies[2:]:
            cp.wait()
        prm = rows(bus_ref[...].astype(F32) + 1.0, cond_ref[...], susc_ref[...], lim_ref[...],
                   steps_ref[...].astype(F32), jnp.zeros((3, cuts), F32))
        vals = rows(
            take(prm, slot_b),
            take(rows(wm_ref[...], wa_ref[...]), by_slot),
            jnp.zeros((nvals0 - 8 - 2 * nrow, slots), F32),
        )
        pay_out[...] = vals.T

    prep_args = (row(cut_peer), cut_rows[0], row(cut_bus), cut_rows[1], cut_rows[2], cut_rows[3], row(cut_steps),
                 wm, wa)
    slot_t, pay_setup = pl.pallas_call(
        prep_kernel,
        out_shape=(jax.ShapeDtypeStruct((cuts, slots), F32), jax.ShapeDtypeStruct((slots, nvals0), F32)),
        in_specs=[pl.BlockSpec(memory_space=pl.ANY)] * len(prep_args),
        out_specs=(pl.BlockSpec(memory_space=pltpu.VMEM), pl.BlockSpec(memory_space=pltpu.VMEM)),
        scratch_shapes=[pltpu.VMEM(a.shape, a.dtype) for a in prep_args] + [pltpu.SemaphoreType.DMA((len(prep_args),))],
    )(*prep_args)
    recv_setup = lax.all_to_all(pay_setup, "net", 0, 0, tiled=True)

    def mid_kernel(recv_ref, wm_ref, wa_ref, mirror_out, pay_out):
        mirror = recv_ref[...].T
        mirror_out[...] = mirror
        inc_recv = onehot(mirror[0:1].astype(jnp.int32) - 1, buses)
        vals = rows(take(rows(wm_ref[...], wa_ref[...]), inc_recv), jnp.zeros((nvals0 - 2 * nrow, slots), F32))
        pay_out[...] = vals.T

    mirror_t, pay_0 = vmem_call(
        mid_kernel,
        (jax.ShapeDtypeStruct((nvals0, slots), F32), jax.ShapeDtypeStruct((slots, nvals0), F32)),
        recv_setup, wm, wa,
    )
    recv_0 = lax.all_to_all(pay_0, "net", 0, 0, tiled=True)

    def spread(p):
        return (lax.broadcasted_iota(jnp.int32, (3 * slots, slots), 0)
                == 3 * lax.broadcasted_iota(jnp.int32, (3 * slots, slots), 1) + p).astype(BF)

    def local_part(first, refs):
        if first:
            (wm_ref, wa_ref, bf_ref, bt_ref, bc_ref, bs_ref, bl_ref, bn_ref,
             gb_ref, gl_ref, gq_ref, gr_ref, gcr_ref, gcq_ref, pe_ref,
             sr_lo_ref, sr_ref, sr_hi_ref, sq_ref,
             tot_out, sup_out, ci_out, g0_out, gq0_out) = refs
            zero_b = jnp.zeros((nrow, buses), F32)
            state = (wm_ref[...], wa_ref[...], zero_b, zero_b)
            carry_in = None
        else:
            (st_ref, bf_ref, bt_ref, bc_ref, bs_ref, bl_ref, bn_ref,
             gb_ref, gl_ref, gq_ref, gr_ref, gcr_ref, gcq_ref, pe_ref,
             ci_ref, g0_ref, gq0_ref, cp_ref, mir_ref,
             tot_out, sup_out, gr_out, gq_out, pn_out, prc_out) = refs
            state = tuple(st_ref[i] for i in range(4))
            carry_in = load_carry(ci_ref)
        inc_from = onehot(bf_ref[...], buses)
        inc_to = onehot(bt_ref[...], buses)
        inc_gen = onehot(gb_ref[...], buses)
        stack = split3(rows(*state))
        pick_from = split4(take_split(stack, inc_from), nrow)
        pick_to = split4(take_split(stack, inc_to), nrow)
        if not first:
            pn_out[...] = take_split(stack, onehot(cp_ref[0:1].astype(jnp.int32), buses))
            prc_out[...] = take_split(stack, onehot(mir_ref[0:1].astype(jnp.int32) - 1, buses))
        prm_in = (bc_ref[...], bs_ref[...], bl_ref[...], bn_ref[...])
        carry_i, fi, ti = advance(carry_in, pick_from, pick_to, prm_in)
        totals = give(fi, inc_from) + give(ti, inc_to)
        for i in range(4):
            tot_out[i] = totals[i * nrow:(i + 1) * nrow]
        lin, quad, ramp, capr, capq = gl_ref[...], gq_ref[...], gr_ref[...], gcr_ref[...], gcq_ref[...]
        per = pe_ref[...]
        nb = (per > 0).astype(F32) + (per < horizon - 1).astype(F32)
        denom = 2.0 * quad + 1.0 + ramp * nb
        if first:
            ext = rows(sr_lo_ref[...], sr_ref[...], sr_hi_ref[...])
            g0 = jnp.clip((ext[scen:scen + window] - lin + ramp * (ext[0:window] + ext[2 * scen:2 * scen + window]))
                          / denom, 0.0, capr)
            g0 = jnp.where((per >= 0) & (per < horizon), g0, 0.0)
            gen_real = g0[scen:scen + nrow]
            gen_react = jnp.clip(sq_ref[...], -capq, capq)
            supply = give(rows(gen_real, gen_react), inc_gen)
            store_carry(ci_out, carry_i)
            g0_out[...] = g0
            gq0_out[...] = gen_react
        else:
            g0 = g0_ref[...]
            gp = take(rows(state[2], state[3]), inc_gen)
            gp_r, gp_q = gp[0:nrow], gp[nrow:]
            gen_real = jnp.clip(
                (g0[scen:scen + nrow] - 2.0 * gp_r - lin + ramp * (g0[0:nrow] + g0[2 * scen:2 * scen + nrow]))
                / denom[scen:scen + nrow],
                0.0,
                capr,
            )
            gen_react = jnp.clip(gq0_ref[...] - 2.0 * gp_q, -capq, capq)
            supply = give(rows(gen_real + gp_r, gen_react + gp_q), inc_gen)
            gr_out[...] = gen_real
            gq_out[...] = gen_react
        sup_out[0] = supply[0:nrow]
        sup_out[1] = supply[nrow:]

    def mirror0_kernel(mirror_ref, wm_ref, wa_ref, bf_ref, bt_ref, cn_ref, gb_ref, tot_out, cm_out, dg_out):
        mirror = mirror_ref[...]
        inc_recv = onehot(mirror[0:1].astype(jnp.int32) - 1, buses)
        degree = (col_sum(onehot(bf_ref[...], buses)) + col_sum(onehot(bt_ref[...], buses))
                  + col_sum(onehot(cn_ref[...], buses)) + col_sum(inc_recv))
        dg_out[...] = rows(degree, col_sum(onehot(gb_ref[...], buses)), jnp.zeros((6, buses), F32))
        zm = jnp.zeros((nrow, slots), F32)
        zero_b = jnp.zeros((nrow, buses), F32)
        stack = rows(wm_ref[...], wa_ref[...], zero_b, zero_b)
        pick_recv = split4(take(stack, inc_recv), nrow)
        near_mirror = (mirror[8:8 + nrow], mirror[8 + nrow:8 + 2 * nrow], zm, zm)
        prm_mir = (mirror[1:2], mirror[2:3], mirror[3:4], mirror[4:5])
        carry_m, _, tmr = advance(None, near_mirror, pick_recv, prm_mir)
        totals = give(tmr, inc_recv)
        for i in range(4):
            tot_out[i] = totals[i * nrow:(i + 1) * nrow]
        store_carry(cm_out, carry_m)

    def cut_part(first, refs):
        (st_ref, wm_ref, wa_ref, lr_ref, lq_ref, recv_ref, mirror_ref, slot_ref,
         dg_ref, cp_ref, tin_ref, sup_ref, tm_ref) = refs[:13]
        rest = refs[13:]
        cprm_v = cp_ref[...]
        wmv, wav = wm_ref[...], wa_ref[...]
        slot_t = slot_ref[...].astype(BF)
        mirror = mirror_ref[...]
        inc_near = onehot(cprm_v[0:1].astype(jnp.int32), buses)
        inc_recv = onehot(mirror[0:1].astype(jnp.int32) - 1, buses)
        degree = dg_ref[0:1]
        gen_count = dg_ref[1:2]
        prm_cut = (cprm_v[1:2], cprm_v[2:3], cprm_v[3:4], cprm_v[4:5])
        if first:
            (cc_out, st_out, pay_out, plane_ref) = rest
            zero_b = jnp.zeros((nrow, buses), F32)
            state = (wmv, wav, zero_b, zero_b)
            far_slot = recv_ref[...].T
            zc = jnp.zeros((nrow, cuts), F32)
            hr = nrow // 2
            low = lax.broadcasted_iota(jnp.int32, (hr, 2 * cuts), 1) < cuts
            wide = lambda v: jnp.concatenate([v, v], axis=1)
            inc2 = onehot(wide(cprm_v[0:1]).astype(jnp.int32), buses)

            def pack(v):
                return jnp.where(low, v[:hr], v[hr:])

            far_c = give(rows(far_slot[0:nrow], far_slot[nrow:2 * nrow]), rows(slot_t, slot_t))
            zp = jnp.zeros((hr, 2 * cuts), F32)
            far_cross = (pack(far_c[0:nrow]), pack(far_c[nrow:]), zp, zp)
            warm_near = take(rows(wmv, wav), inc2)
            pick_near = (pack(warm_near[0:nrow]), pack(warm_near[nrow:]), zp, zp)
            carry_p, fc, _ = advance(None, pick_near, far_cross, tuple(wide(v) for v in prm_cut))
            t_low = give(jnp.where(rows(*(low,) * 4), fc, 0.0), inc2)
            t_high = give(jnp.where(rows(*(low,) * 4), 0.0, fc), inc2)
            cross_t = rows(*(x for i in range(4) for x in (t_low[i * hr:(i + 1) * hr], t_high[i * hr:(i + 1) * hr])))
            totals = tin_ref[...] + tm_ref[...] + cross_t.reshape(4, nrow, buses)
            flat = rows(*carry_p[0], *carry_p[1], *carry_p[2])
            lanes = lax.broadcasted_iota(jnp.int32, (2 * cuts, cuts), 0)
            cols = lax.broadcasted_iota(jnp.int32, (2 * cuts, cuts), 1)
            u_low = take(flat, (lanes == cols).astype(BF))
            u_high = take(flat, (lanes == cols + cuts).astype(BF))
            unp = [rows(u_low[a * hr:(a + 1) * hr], u_high[a * hr:(a + 1) * hr]) for a in range(10)]
            carry_c = (tuple(unp[0:4]), tuple(unp[4:8]), (unp[8], unp[9]))
        else:
            (cc_in_ref, cm_ref, pn_ref, prc_ref, mag_out, ang_out, pr_out, plane_ref) = rest
            state = tuple(st_ref[i] for i in range(4))
            blocks = []
            for p in range(3):
                for k in range(cap):
                    plane_ref[pl.ds(k, parts, stride=cap), :] = recv_ref[pl.ds(p * cap + k, parts, stride=3 * cap), :]
                blocks.append(plane_ref[...].T)
            both = rows(*blocks)
            near_mirror = split4(both[0:4 * nrow], nrow)
            far_cross = split4(give(both[4 * nrow:], slot_t), nrow)
            pick_near = split4(pn_ref[...], nrow)
            pick_recv = split4(prc_ref[...], nrow)
            carry_c_in = load_carry(cc_in_ref)
            carry_m_in = load_carry(cm_ref)
            _, fc, _ = advance(carry_c_in, pick_near, far_cross, prm_cut)
            prm_mir = (mirror[1:2], mirror[2:3], mirror[3:4], mirror[4:5])
            _, _, tmr = advance(carry_m_in, near_mirror, pick_recv, prm_mir)
            totals = tin_ref[...] + (give(fc, inc_near) + give(tmr, inc_recv)).reshape(4, nrow, buses)
        mag = (totals[0] + wmv) / (degree + 1.0)
        ang = (totals[1] + wav) / (degree + 1.0)
        weight = 1.0 + BALANCE_WEIGHT * (gen_count + degree)
        pr = BALANCE_WEIGHT * (sup_ref[0] - totals[2] - lr_ref[...]) / weight
        pq = BALANCE_WEIGHT * (sup_ref[1] - totals[3] - lq_ref[...]) / weight
        if first:
            store_carry(cc_out, carry_c)
            st_out[0] = mag
            st_out[1] = ang
            st_out[2] = pr
            st_out[3] = pq
            new_stack = split3(rows(mag, ang, pr, pq))
            near_slot = dot(inc_near, slot_t, NN).astype(BF)
            vals = rows(take_split(new_stack, near_slot), take_split(new_stack, inc_recv))
            for p in range(3):
                plane_ref[...] = vals[p * 128:(p + 1) * 128].T
                for k in range(cap):
                    pay_out[pl.ds(p * cap + k, parts, stride=3 * cap), :] = plane_ref[pl.ds(k, parts, stride=cap), :]
        else:
            mag_out[...] = mag
            ang_out[...] = ang
            pr_out[...] = pr

    sds = jax.ShapeDtypeStruct
    tot_shape = sds((4, nrow, buses), F32)
    br_all = br_rows
    gen_all = (*gen_rows, period_ext)
    tin0, sup0, ci1, g0, gq0 = vmem_call(
        lambda *refs: local_part(True, refs),
        (tot_shape, sds((2, nrow, buses), F32), sds((10, nrow, buses), F32), sds((window, gens), F32),
         sds((nrow, gens), F32)),
        wm, wa, *br_all, *gen_all, lo, sr, hi, sq,
    )
    tm0, cm1, dg = vmem_call(
        mirror0_kernel, (tot_shape, sds((10, nrow, slots), F32), sds((8, buses), F32)), mirror_t, wm, wa,
        br_rows[0], br_rows[1], cut_rows[0], gen_rows[0],
    )
    cprm = jnp.concatenate([cut_rows[0].astype(F32), *cut_rows[1:], jnp.zeros((3, cuts), F32)], axis=0)
    cc1, st1, pay_1 = vmem_call(
        lambda *refs: cut_part(True, refs),
        (sds((10, nrow, cuts), F32), tot_shape, sds((3 * slots, 128), F32)),
        wm, wm, wa, lr, lq, recv_0, mirror_t, slot_t, dg, cprm, tin0, sup0, tm0,
        scratch=[pltpu.VMEM((slots, 128), F32)],
    )
    recv_1 = lax.all_to_all(pay_1.reshape(3 * parts, 2, 128), "net", 0, 0, tiled=True).reshape(3 * slots, 128)
    tin1, sup1, gr, gq, pn1, prc1 = vmem_call(
        lambda *refs: local_part(False, refs),
        (tot_shape, sds((2, nrow, buses), F32), sds((nrow, gens), F32), sds((nrow, gens), F32),
         sds((4 * nrow, cuts), F32), sds((4 * nrow, slots), F32)),
        st1, *br_all, *gen_all, ci1, g0, gq0, cprm, mirror_t,
    )
    mag, ang, pr = vmem_call(
        lambda *refs: cut_part(False, refs),
        (sds((nrow, buses), F32), sds((nrow, buses), F32), sds((nrow, buses), F32)),
        st1, wm, wa, lr, lq, recv_1, mirror_t, slot_t, dg, cprm, tin1, sup1, tin1,
        cc1, cm1, pn1, prc1,
        scratch=[pltpu.VMEM((slots, 128), F32)],
    )
    shape_b = (periods, scen, buses)
    shape_g = (periods, scen, gens)
    return (mag.reshape(shape_b), ang.reshape(shape_b), pr.reshape(shape_b), gr.reshape(shape_g),
            gq.reshape(shape_g))


def solution(mesh):
    bus = P("tm", None, "net")
    one = P("net")
    return jax.shard_map(
        on_device,
        mesh=mesh,
        in_specs=(bus,) * 6 + (one,) * 12 + (one, P("net", None)) + (one,) * 5,
        out_specs=(bus,) * 5,
        check_vma=False,
    )
```

```python
import jax
import jax.numpy as jnp
from jax import lax
from jax.experimental import pallas as pl
from jax.experimental.pallas import tpu as pltpu
from jax.sharding import PartitionSpec as P

INNER = 4
STEP_SIZE = 0.0005
RADIUS = 0.05
BALANCE_WEIGHT = 2.0
HI = lax.Precision.HIGHEST
F32 = jnp.float32


NN = (((1,), (0,)), ((), ()))
NT = (((1,), (1,)), ((), ()))
BF = jnp.bfloat16


def split3(x):
    hi = x.astype(BF)
    r = x - hi.astype(F32)
    mid = r.astype(BF)
    lo = (r - mid.astype(F32)).astype(BF)
    return hi, mid, lo


def dot(a, b, dims):
    return lax.dot_general(a, b, dims, preferred_element_type=F32)


def take_split(parts, oh):
    hi, mid, lo = parts
    return (dot(hi, oh, NN) + dot(mid, oh, NN)) + dot(lo, oh, NN)


def take(vals, oh):
    hi, mid, lo = split3(vals)
    return (dot(hi, oh, NN) + dot(mid, oh, NN)) + dot(lo, oh, NN)


def give(vals, oh):
    hi, mid, lo = split3(vals)
    return (dot(hi, oh, NT) + dot(mid, oh, NT)) + dot(lo, oh, NT)


def take_left(oh, vals):
    hi, mid, lo = split3(vals)
    return (dot(oh, hi, NN) + dot(oh, mid, NN)) + dot(oh, lo, NN)


def give_left(oh, vals):
    hi, mid, lo = split3(vals)
    return (dot(oh, hi, NT) + dot(oh, mid, NT)) + dot(oh, lo, NT)


def onehot(ids_row, count):
    n = ids_row.shape[1]
    return (lax.broadcasted_iota(jnp.int32, (count, n), 0) == ids_row).astype(BF)


def col_sum(inc):
    return dot(jnp.ones((8, inc.shape[1]), BF), inc, NT)[0:1]


def rows(*parts):
    return jnp.concatenate(parts, axis=0)


def trig(x):
    d = x[1] - x[3]
    return (jnp.cos(d), jnp.sin(d))


def flows(x, cs, g, b):
    mf, _, mt, _ = x
    c, s = cs
    p = mf * mt
    return (
        g * mf * mf - p * (g * c + b * s),
        -b * mf * mf - p * (g * s - b * c),
        g * mt * mt - p * (g * c - b * s),
        -b * mt * mt + p * (g * s + b * c),
    )


def energy_grad(x, cs, f, t, ft, g, b, l2):
    mf, af, mt, at = x
    c, s = cs
    p = mf * mt
    ka = g * c + b * s
    kb = g * s - b * c
    kc = g * c - b * s
    kd = g * s + b * c
    if f is None:
        f = (g * mf * mf - p * ka, -b * mf * mf - p * kb, g * mt * mt - p * kc, -b * mt * mt + p * kd)
    f0, f1, f2, f3 = f
    ef = jnp.maximum(f0 * f0 + f1 * f1 - l2, 0.0)
    et = jnp.maximum(f2 * f2 + f3 * f3 - l2, 0.0)
    w0 = (f0 - ft[0]) + 2.0 * ef * f0
    w1 = (f1 - ft[1]) + 2.0 * ef * f1
    w2 = (f2 - ft[2]) + 2.0 * et * f2
    w3 = (f3 - ft[3]) + 2.0 * et * f3
    g_mf = (mf - t[0]) + w0 * (2.0 * g * mf - mt * ka) - w1 * (2.0 * b * mf + mt * kb) - w2 * mt * kc + w3 * mt * kd
    g_mt = (mt - t[2]) - w0 * mf * ka - w1 * mf * kb + w2 * (2.0 * g * mt - mf * kc) - w3 * (2.0 * b * mt - mf * kd)
    g_d = p * (w0 * kb - w1 * ka + w2 * kd + w3 * kc)
    return (g_mf, (af - t[1]) + g_d, g_mt, (at - t[3]) - g_d)


def solve(x, cs, f, t, ft, g, b, l2, steps):
    for attempt in range(INNER):
        if cs is None:
            cs = trig(x)
        grad = energy_grad(x, cs, f, t, ft, g, b, l2)
        x = tuple(
            jnp.where(attempt < steps, xi - jnp.clip(STEP_SIZE * gi, -RADIUS, RADIUS), xi)
            for xi, gi in zip(x, grad)
        )
        cs, f = None, None
    return x


def advance(carry, near, far, prm):
    g, b, lim, steps = prm
    ends = (near[0], near[1], far[0], far[1])
    prices = (near[2], near[3], far[2], far[3])
    if carry is None:
        copies = ends
        cs = trig(copies)
        flow_prev = flows(copies, cs, g, b)
        volt = tuple(jnp.zeros_like(e) for e in ends)
        target = ends
        flow_target = flow_prev
        dual_flow = volt
    else:
        copies, flow_prev, cs = carry
        volt = tuple(c - e for c, e in zip(copies, ends))
        target = tuple(e - v for e, v in zip(ends, volt))
        flow_target = tuple(f + 2.0 * q for f, q in zip(flow_prev, prices))
        dual_flow = tuple(-q for q in prices)
    copies = solve(copies, cs, flow_prev, target, flow_target, g, b, lim * lim, steps)
    cs = trig(copies)
    flow_prev = flows(copies, cs, g, b)
    side_from = rows(
        copies[0] + volt[0], copies[1] + volt[1], flow_prev[0] + dual_flow[0], flow_prev[1] + dual_flow[1]
    )
    side_to = rows(
        copies[2] + volt[2], copies[3] + volt[3], flow_prev[2] + dual_flow[2], flow_prev[3] + dual_flow[3]
    )
    return (copies, flow_prev, cs), side_from, side_to


def store_carry(ref, carry):
    for i in range(4):
        ref[i] = carry[0][i]
        ref[4 + i] = carry[1][i]
    ref[8] = carry[2][0]
    ref[9] = carry[2][1]


def load_carry(ref):
    return (tuple(ref[i] for i in range(4)), tuple(ref[4 + i] for i in range(4)), (ref[8], ref[9]))


def split4(a, n):
    return tuple(a[i * n:(i + 1) * n] for i in range(4))


def vmem_call(kernel, outs, *args, scratch=()):
    return pl.pallas_call(
        kernel,
        out_shape=outs,
        in_specs=[pl.BlockSpec(memory_space=pltpu.VMEM)] * len(args),
        out_specs=tuple(pl.BlockSpec(memory_space=pltpu.VMEM) for _ in outs),
        scratch_shapes=scratch,
        compiler_params=pltpu.CompilerParams(vmem_limit_bytes=48 * 1024 * 1024),
    )(*args)


def on_device(
    warm_mag, warm_angle, load_real, load_react, start_real, start_react,
    gen_bus, gen_linear, gen_quad, gen_ramp, gen_cap_real, gen_cap_react,
    branch_from, branch_to, branch_cond, branch_susc, branch_limit, branch_steps,
    cut_near, cut_peer, cut_bus, cut_cond, cut_susc, cut_limit, cut_steps,
):
    periods, scen, buses = warm_mag.shape
    nrow = periods * scen
    cuts = cut_near.shape[0]
    parts = lax.axis_size("net")
    cap = max(2, cuts // parts * 2)
    slots = parts * cap
    gens = gen_bus.shape[0]
    ntm = lax.axis_size("tm")
    horizon = periods * ntm

    def row(v):
        return v.reshape(1, -1)

    wm = warm_mag.reshape(nrow, buses)
    wa = warm_angle.reshape(nrow, buses)
    lr = load_real.reshape(nrow, buses)
    lq = load_react.reshape(nrow, buses)
    sr = start_real.reshape(nrow, gens)
    sq = start_react.reshape(nrow, gens)
    halo = 2 * scen
    lo = lax.ppermute(sr[nrow - halo:], "tm", [(i, i + 1) for i in range(ntm - 1)])
    hi = lax.ppermute(sr[:halo], "tm", [(i + 1, i) for i in range(ntm - 1)])
    window = nrow + 2 * scen
    period_ext = (
        lax.axis_index("tm") * periods - 1 + jnp.arange(window, dtype=jnp.int32) // scen
    ).reshape(window, 1)
    gen_rows = (row(gen_bus), row(gen_linear), row(gen_quad), row(gen_ramp), row(gen_cap_real), row(gen_cap_react))
    br_rows = (row(branch_from), row(branch_to), row(branch_cond), row(branch_susc), row(branch_limit),
               row(branch_steps.astype(F32)))
    cut_rows = (row(cut_near), row(cut_cond), row(cut_susc), row(cut_limit), row(cut_steps.astype(F32)))
    cut_bus_row = row(cut_bus.astype(F32))
    nvals0 = 128

    def prep_kernel(peer_hbm, near_hbm, bus_hbm, cond_hbm, susc_hbm, lim_hbm, steps_hbm, wm_hbm, wa_hbm,
                    slot_out, pay_out,
                    peer_ref, near_ref, bus_ref, cond_ref, susc_ref, lim_ref, steps_ref, wm_ref, wa_ref, sems):
        pairs = ((peer_hbm, peer_ref), (near_hbm, near_ref), (bus_hbm, bus_ref), (cond_hbm, cond_ref),
                 (susc_hbm, susc_ref), (lim_hbm, lim_ref), (steps_hbm, steps_ref), (wm_hbm, wm_ref),
                 (wa_hbm, wa_ref))
        copies = [pltpu.make_async_copy(src, dst, sems.at[i]) for i, (src, dst) in enumerate(pairs)]
        for cp in copies:
            cp.start()
        copies[0].wait()
        peer = peer_ref[...]
        mine_t = (lax.broadcasted_iota(jnp.int32, (parts, cuts), 0) == peer).astype(F32)
        same = dot(mine_t.T.astype(BF), mine_t.astype(BF), NN)
        earlier = lax.broadcasted_iota(jnp.int32, (cuts, cuts), 0) < lax.broadcasted_iota(jnp.int32, (cuts, cuts), 1)
        rank = jnp.sum(jnp.where(earlier, same, 0.0), axis=0, keepdims=True)
        position = peer.astype(F32) * cap + rank
        slot_t = (lax.broadcasted_iota(jnp.int32, (slots, cuts), 0).astype(F32) == position).astype(F32).T
        slot_b = slot_t.astype(BF)
        slot_out[...] = slot_t
        copies[1].wait()
        inc_near = onehot(near_ref[...], buses)
        by_slot = dot(inc_near, slot_b, NN).astype(BF)
        for cp in copies[2:]:
            cp.wait()
        prm = rows(bus_ref[...].astype(F32) + 1.0, cond_ref[...], susc_ref[...], lim_ref[...],
                   steps_ref[...].astype(F32), jnp.zeros((3, cuts), F32))
        vals = rows(
            take(prm, slot_b),
            take(rows(wm_ref[...], wa_ref[...]), by_slot),
            jnp.zeros((nvals0 - 8 - 2 * nrow, slots), F32),
        )
        pay_out[...] = vals.T

    prep_args = (row(cut_peer), cut_rows[0], row(cut_bus), cut_rows[1], cut_rows[2], cut_rows[3], row(cut_steps),
                 wm, wa)
    slot_t, pay_setup = pl.pallas_call(
        prep_kernel,
        out_shape=(jax.ShapeDtypeStruct((cuts, slots), F32), jax.ShapeDtypeStruct((slots, nvals0), F32)),
        in_specs=[pl.BlockSpec(memory_space=pl.ANY)] * len(prep_args),
        out_specs=(pl.BlockSpec(memory_space=pltpu.VMEM), pl.BlockSpec(memory_space=pltpu.VMEM)),
        scratch_shapes=[pltpu.VMEM(a.shape, a.dtype) for a in prep_args] + [pltpu.SemaphoreType.DMA((len(prep_args),))],
    )(*prep_args)
    recv_setup = lax.all_to_all(pay_setup, "net", 0, 0, tiled=True)

    def mid_kernel(recv_ref, wm_ref, wa_ref, mirror_out, pay_out):
        mirror = recv_ref[...].T
        mirror_out[...] = mirror
        inc_recv = onehot(mirror[0:1].astype(jnp.int32) - 1, buses)
        vals = rows(take(rows(wm_ref[...], wa_ref[...]), inc_recv), jnp.zeros((nvals0 - 2 * nrow, slots), F32))
        pay_out[...] = vals.T

    mirror_t, pay_0 = vmem_call(
        mid_kernel,
        (jax.ShapeDtypeStruct((nvals0, slots), F32), jax.ShapeDtypeStruct((slots, nvals0), F32)),
        recv_setup, wm, wa,
    )
    recv_0 = lax.all_to_all(pay_0, "net", 0, 0, tiled=True)

    def spread(p):
        return (lax.broadcasted_iota(jnp.int32, (3 * slots, slots), 0)
                == 3 * lax.broadcasted_iota(jnp.int32, (3 * slots, slots), 1) + p).astype(BF)

    def local_part(first, refs):
        if first:
            (wm_ref, wa_ref, bf_ref, bt_ref, bc_ref, bs_ref, bl_ref, bn_ref,
             gb_ref, gl_ref, gq_ref, gr_ref, gcr_ref, gcq_ref, pe_ref,
             sr_lo_ref, sr_ref, sr_hi_ref, sq_ref,
             tot_out, sup_out, ci_out, g0_out, gq0_out) = refs
            zero_b = jnp.zeros((nrow, buses), F32)
            state = (wm_ref[...], wa_ref[...], zero_b, zero_b)
            carry_in = None
        else:
            (st_ref, bf_ref, bt_ref, bc_ref, bs_ref, bl_ref, bn_ref,
             gb_ref, gl_ref, gq_ref, gr_ref, gcr_ref, gcq_ref, pe_ref,
             ci_ref, g0_ref, gq0_ref, cp_ref, mir_ref,
             tot_out, sup_out, gr_out, gq_out, pn_out, prc_out) = refs
            state = tuple(st_ref[i] for i in range(4))
            carry_in = load_carry(ci_ref)
        inc_from = onehot(bf_ref[...], buses)
        inc_to = onehot(bt_ref[...], buses)
        inc_gen = onehot(gb_ref[...], buses)
        stack = split3(rows(*state))
        pick_from = split4(take_split(stack, inc_from), nrow)
        pick_to = split4(take_split(stack, inc_to), nrow)
        if not first:
            pn_out[...] = take_split(stack, onehot(cp_ref[0:1].astype(jnp.int32), buses))
            prc_out[...] = take_split(stack, onehot(mir_ref[0:1].astype(jnp.int32) - 1, buses))
        prm_in = (bc_ref[...], bs_ref[...], bl_ref[...], bn_ref[...])
        carry_i, fi, ti = advance(carry_in, pick_from, pick_to, prm_in)
        totals = give(fi, inc_from) + give(ti, inc_to)
        for i in range(4):
            tot_out[i] = totals[i * nrow:(i + 1) * nrow]
        lin, quad, ramp, capr, capq = gl_ref[...], gq_ref[...], gr_ref[...], gcr_ref[...], gcq_ref[...]
        per = pe_ref[...]
        nb = (per > 0).astype(F32) + (per < horizon - 1).astype(F32)
        denom = 2.0 * quad + 1.0 + ramp * nb
        if first:
            ext = rows(sr_lo_ref[...], sr_ref[...], sr_hi_ref[...])
            g0 = jnp.clip((ext[scen:scen + window] - lin + ramp * (ext[0:window] + ext[2 * scen:2 * scen + window]))
                          / denom, 0.0, capr)
            g0 = jnp.where((per >= 0) & (per < horizon), g0, 0.0)
            gen_real = g0[scen:scen + nrow]
            gen_react = jnp.clip(sq_ref[...], -capq, capq)
            supply = give(rows(gen_real, gen_react), inc_gen)
            store_carry(ci_out, carry_i)
            g0_out[...] = g0
            gq0_out[...] = gen_react
        else:
            g0 = g0_ref[...]
            gp = take(rows(state[2], state[3]), inc_gen)
            gp_r, gp_q = gp[0:nrow], gp[nrow:]
            gen_real = jnp.clip(
                (g0[scen:scen + nrow] - 2.0 * gp_r - lin + ramp * (g0[0:nrow] + g0[2 * scen:2 * scen + nrow]))
                / denom[scen:scen + nrow],
                0.0,
                capr,
            )
            gen_react = jnp.clip(gq0_ref[...] - 2.0 * gp_q, -capq, capq)
            supply = give(rows(gen_real + gp_r, gen_react + gp_q), inc_gen)
            gr_out[...] = gen_real
            gq_out[...] = gen_react
        sup_out[0] = supply[0:nrow]
        sup_out[1] = supply[nrow:]

    def mirror0_kernel(mirror_ref, wm_ref, wa_ref, bf_ref, bt_ref, cn_ref, gb_ref, tot_out, cm_out, dg_out):
        mirror = mirror_ref[...]
        inc_recv = onehot(mirror[0:1].astype(jnp.int32) - 1, buses)
        degree = (col_sum(onehot(bf_ref[...], buses)) + col_sum(onehot(bt_ref[...], buses))
                  + col_sum(onehot(cn_ref[...], buses)) + col_sum(inc_recv))
        dg_out[...] = rows(degree, col_sum(onehot(gb_ref[...], buses)), jnp.zeros((6, buses), F32))
        zm = jnp.zeros((nrow, slots), F32)
        zero_b = jnp.zeros((nrow, buses), F32)
        stack = rows(wm_ref[...], wa_ref[...], zero_b, zero_b)
        pick_recv = split4(take(stack, inc_recv), nrow)
        near_mirror = (mirror[8:8 + nrow], mirror[8 + nrow:8 + 2 * nrow], zm, zm)
        prm_mir = (mirror[1:2], mirror[2:3], mirror[3:4], mirror[4:5])
        carry_m, _, tmr = advance(None, near_mirror, pick_recv, prm_mir)
        totals = give(tmr, inc_recv)
        for i in range(4):
            tot_out[i] = totals[i * nrow:(i + 1) * nrow]
        store_carry(cm_out, carry_m)

    def cut_part(first, refs):
        (st_ref, wm_ref, wa_ref, lr_ref, lq_ref, recv_ref, mirror_ref, slot_ref,
         dg_ref, cp_ref, tin_ref, sup_ref, tm_ref) = refs[:13]
        rest = refs[13:]
        cprm_v = cp_ref[...]
        wmv, wav = wm_ref[...], wa_ref[...]
        slot_t = slot_ref[...].astype(BF)
        mirror = mirror_ref[...]
        inc_near = onehot(cprm_v[0:1].astype(jnp.int32), buses)
        inc_recv = onehot(mirror[0:1].astype(jnp.int32) - 1, buses)
        degree = dg_ref[0:1]
        gen_count = dg_ref[1:2]
        prm_cut = (cprm_v[1:2], cprm_v[2:3], cprm_v[3:4], cprm_v[4:5])
        if first:
            (cc_out, st_out, pay_out, plane_ref) = rest
            zero_b = jnp.zeros((nrow, buses), F32)
            state = (wmv, wav, zero_b, zero_b)
            far_slot = recv_ref[...].T
            zc = jnp.zeros((nrow, cuts), F32)
            hr = nrow // 2
            low = lax.broadcasted_iota(jnp.int32, (hr, 2 * cuts), 1) < cuts
            wide = lambda v: jnp.concatenate([v, v], axis=1)
            inc2 = onehot(wide(cprm_v[0:1]).astype(jnp.int32), buses)

            def pack(v):
                return jnp.where(low, v[:hr], v[hr:])

            far_c = give(rows(far_slot[0:nrow], far_slot[nrow:2 * nrow]), rows(slot_t, slot_t))
            zp = jnp.zeros((hr, 2 * cuts), F32)
            far_cross = (pack(far_c[0:nrow]), pack(far_c[nrow:]), zp, zp)
            warm_near = take(rows(wmv, wav), inc2)
            pick_near = (pack(warm_near[0:nrow]), pack(warm_near[nrow:]), zp, zp)
            carry_p, fc, _ = advance(None, pick_near, far_cross, tuple(wide(v) for v in prm_cut))
            t_low = give(jnp.where(rows(*(low,) * 4), fc, 0.0), inc2)
            t_high = give(jnp.where(rows(*(low,) * 4), 0.0, fc), inc2)
            cross_t = rows(*(x for i in range(4) for x in (t_low[i * hr:(i + 1) * hr], t_high[i * hr:(i + 1) * hr])))
            totals = tin_ref[...] + tm_ref[...] + cross_t.reshape(4, nrow, buses)
            flat = rows(*carry_p[0], *carry_p[1], *carry_p[2])
            lanes = lax.broadcasted_iota(jnp.int32, (2 * cuts, cuts), 0)
            cols = lax.broadcasted_iota(jnp.int32, (2 * cuts, cuts), 1)
            u_low = take(flat, (lanes == cols).astype(BF))
            u_high = take(flat, (lanes == cols + cuts).astype(BF))
            unp = [rows(u_low[a * hr:(a + 1) * hr], u_high[a * hr:(a + 1) * hr]) for a in range(10)]
            carry_c = (tuple(unp[0:4]), tuple(unp[4:8]), (unp[8], unp[9]))
        else:
            (cc_in_ref, cm_ref, pn_ref, prc_ref, mag_out, ang_out, pr_out, plane_ref) = rest
            state = tuple(st_ref[i] for i in range(4))
            blocks = []
            for p in range(3):
                for k in range(cap):
                    plane_ref[pl.ds(k, parts, stride=cap), :] = recv_ref[pl.ds(p * cap + k, parts, stride=3 * cap), :]
                blocks.append(plane_ref[...].T)
            both = rows(*blocks)
            near_mirror = split4(both[0:4 * nrow], nrow)
            hr = nrow // 2
            low = lax.broadcasted_iota(jnp.int32, (hr, 2 * cuts), 1) < cuts
            wide = lambda v: jnp.concatenate([v, v], axis=1)
            inc2 = onehot(wide(cprm_v[0:1]).astype(jnp.int32), buses)

            def pack(v):
                return jnp.where(low, v[:hr], v[hr:])

            def pack_narrow(v):
                return jnp.where(low, wide(v[:hr]), wide(v[hr:]))

            far_w = give(both[4 * nrow:], rows(slot_t, slot_t))
            far_cross = tuple(pack(x) for x in split4(far_w, nrow))
            pick_near = tuple(pack_narrow(x) for x in split4(pn_ref[...], nrow))
            pick_recv = split4(prc_ref[...], nrow)
            cc_in = load_carry(cc_in_ref)
            carry_c_in = (tuple(pack_narrow(x) for x in cc_in[0]), tuple(pack_narrow(x) for x in cc_in[1]),
                          tuple(pack_narrow(x) for x in cc_in[2]))
            carry_m_in = load_carry(cm_ref)
            _, fc, _ = advance(carry_c_in, pick_near, far_cross, tuple(wide(v) for v in prm_cut))
            t_low = give(jnp.where(rows(*(low,) * 4), fc, 0.0), inc2)
            t_high = give(jnp.where(rows(*(low,) * 4), 0.0, fc), inc2)
            cross_t = rows(*(x for i in range(4) for x in (t_low[i * hr:(i + 1) * hr], t_high[i * hr:(i + 1) * hr])))
            prm_mir = (mirror[1:2], mirror[2:3], mirror[3:4], mirror[4:5])
            _, _, tmr = advance(carry_m_in, near_mirror, pick_recv, prm_mir)
            totals = tin_ref[...] + (cross_t + give(tmr, inc_recv)).reshape(4, nrow, buses)
        mag = (totals[0] + wmv) / (degree + 1.0)
        ang = (totals[1] + wav) / (degree + 1.0)
        weight = 1.0 + BALANCE_WEIGHT * (gen_count + degree)
        pr = BALANCE_WEIGHT * (sup_ref[0] - totals[2] - lr_ref[...]) / weight
        pq = BALANCE_WEIGHT * (sup_ref[1] - totals[3] - lq_ref[...]) / weight
        if first:
            store_carry(cc_out, carry_c)
            st_out[0] = mag
            st_out[1] = ang
            st_out[2] = pr
            st_out[3] = pq
            new_stack = split3(rows(mag, ang, pr, pq))
            near_slot = dot(inc_near, slot_t, NN).astype(BF)
            vals = rows(take_split(new_stack, near_slot), take_split(new_stack, inc_recv))
            for p in range(3):
                plane_ref[...] = vals[p * 128:(p + 1) * 128].T
                for k in range(cap):
                    pay_out[pl.ds(p * cap + k, parts, stride=3 * cap), :] = plane_ref[pl.ds(k, parts, stride=cap), :]
        else:
            mag_out[...] = mag
            ang_out[...] = ang
            pr_out[...] = pr

    sds = jax.ShapeDtypeStruct
    tot_shape = sds((4, nrow, buses), F32)
    br_all = br_rows
    gen_all = (*gen_rows, period_ext)
    tin0, sup0, ci1, g0, gq0 = vmem_call(
        lambda *refs: local_part(True, refs),
        (tot_shape, sds((2, nrow, buses), F32), sds((10, nrow, buses), F32), sds((window, gens), F32),
         sds((nrow, gens), F32)),
        wm, wa, *br_all, *gen_all, lo, sr, hi, sq,
    )
    tm0, cm1, dg = vmem_call(
        mirror0_kernel, (tot_shape, sds((10, nrow, slots), F32), sds((8, buses), F32)), mirror_t, wm, wa,
        br_rows[0], br_rows[1], cut_rows[0], gen_rows[0],
    )
    cprm = jnp.concatenate([cut_rows[0].astype(F32), *cut_rows[1:], jnp.zeros((3, cuts), F32)], axis=0)
    cc1, st1, pay_1 = vmem_call(
        lambda *refs: cut_part(True, refs),
        (sds((10, nrow, cuts), F32), tot_shape, sds((3 * slots, 128), F32)),
        wm, wm, wa, lr, lq, recv_0, mirror_t, slot_t, dg, cprm, tin0, sup0, tm0,
        scratch=[pltpu.VMEM((slots, 128), F32)],
    )
    recv_1 = lax.all_to_all(pay_1.reshape(3 * parts, 2, 128), "net", 0, 0, tiled=True).reshape(3 * slots, 128)
    tin1, sup1, gr, gq, pn1, prc1 = vmem_call(
        lambda *refs: local_part(False, refs),
        (tot_shape, sds((2, nrow, buses), F32), sds((nrow, gens), F32), sds((nrow, gens), F32),
         sds((4 * nrow, cuts), F32), sds((4 * nrow, slots), F32)),
        st1, *br_all, *gen_all, ci1, g0, gq0, cprm, mirror_t,
    )
    mag, ang, pr = vmem_call(
        lambda *refs: cut_part(False, refs),
        (sds((nrow, buses), F32), sds((nrow, buses), F32), sds((nrow, buses), F32)),
        st1, wm, wa, lr, lq, recv_1, mirror_t, slot_t, dg, cprm, tin1, sup1, tin1,
        cc1, cm1, pn1, prc1,
        scratch=[pltpu.VMEM((slots, 128), F32)],
    )
    shape_b = (periods, scen, buses)
    shape_g = (periods, scen, gens)
    return (mag.reshape(shape_b), ang.reshape(shape_b), pr.reshape(shape_b), gr.reshape(shape_g),
            gq.reshape(shape_g))


def solution(mesh):
    bus = P("tm", None, "net")
    one = P("net")
    return jax.shard_map(
        on_device,
        mesh=mesh,
        in_specs=(bus,) * 6 + (one,) * 12 + (one, P("net", None)) + (one,) * 5,
        out_specs=(bus,) * 5,
        check_vma=False,
    )
```

```python
import jax
import jax.numpy as jnp
from jax import lax
from jax.experimental import pallas as pl
from jax.experimental.pallas import tpu as pltpu
from jax.sharding import PartitionSpec as P

INNER = 4
STEP_SIZE = 0.0005
RADIUS = 0.05
BALANCE_WEIGHT = 2.0
HI = lax.Precision.HIGHEST
F32 = jnp.float32


NN = (((1,), (0,)), ((), ()))
NT = (((1,), (1,)), ((), ()))
BF = jnp.bfloat16


def split3(x):
    hi = x.astype(BF)
    r = x - hi.astype(F32)
    mid = r.astype(BF)
    lo = (r - mid.astype(F32)).astype(BF)
    return hi, mid, lo


def dot(a, b, dims):
    return lax.dot_general(a, b, dims, preferred_element_type=F32)


def take_split(parts, oh):
    hi, mid, lo = parts
    return (dot(hi, oh, NN) + dot(mid, oh, NN)) + dot(lo, oh, NN)


def take(vals, oh):
    hi, mid, lo = split3(vals)
    return (dot(hi, oh, NN) + dot(mid, oh, NN)) + dot(lo, oh, NN)


def give(vals, oh):
    hi, mid, lo = split3(vals)
    return (dot(hi, oh, NT) + dot(mid, oh, NT)) + dot(lo, oh, NT)


def take_left(oh, vals):
    hi, mid, lo = split3(vals)
    return (dot(oh, hi, NN) + dot(oh, mid, NN)) + dot(oh, lo, NN)


def give_left(oh, vals):
    hi, mid, lo = split3(vals)
    return (dot(oh, hi, NT) + dot(oh, mid, NT)) + dot(oh, lo, NT)


def onehot(ids_row, count):
    n = ids_row.shape[1]
    return (lax.broadcasted_iota(jnp.int32, (count, n), 0) == ids_row).astype(BF)


def col_sum(inc):
    return dot(jnp.ones((8, inc.shape[1]), BF), inc, NT)[0:1]


def rows(*parts):
    return jnp.concatenate(parts, axis=0)


def trig(x):
    d = x[1] - x[3]
    return (jnp.cos(d), jnp.sin(d))


def flows(x, cs, g, b):
    mf, _, mt, _ = x
    c, s = cs
    p = mf * mt
    return (
        g * mf * mf - p * (g * c + b * s),
        -b * mf * mf - p * (g * s - b * c),
        g * mt * mt - p * (g * c - b * s),
        -b * mt * mt + p * (g * s + b * c),
    )


def energy_grad(x, cs, f, t, ft, g, b, l2):
    mf, af, mt, at = x
    c, s = cs
    p = mf * mt
    ka = g * c + b * s
    kb = g * s - b * c
    kc = g * c - b * s
    kd = g * s + b * c
    if f is None:
        f = (g * mf * mf - p * ka, -b * mf * mf - p * kb, g * mt * mt - p * kc, -b * mt * mt + p * kd)
    f0, f1, f2, f3 = f
    ef = jnp.maximum(f0 * f0 + f1 * f1 - l2, 0.0)
    et = jnp.maximum(f2 * f2 + f3 * f3 - l2, 0.0)
    w0 = (f0 - ft[0]) + 2.0 * ef * f0
    w1 = (f1 - ft[1]) + 2.0 * ef * f1
    w2 = (f2 - ft[2]) + 2.0 * et * f2
    w3 = (f3 - ft[3]) + 2.0 * et * f3
    g_mf = (mf - t[0]) + w0 * (2.0 * g * mf - mt * ka) - w1 * (2.0 * b * mf + mt * kb) - w2 * mt * kc + w3 * mt * kd
    g_mt = (mt - t[2]) - w0 * mf * ka - w1 * mf * kb + w2 * (2.0 * g * mt - mf * kc) - w3 * (2.0 * b * mt - mf * kd)
    g_d = p * (w0 * kb - w1 * ka + w2 * kd + w3 * kc)
    return (g_mf, (af - t[1]) + g_d, g_mt, (at - t[3]) - g_d)


def solve(x, cs, f, t, ft, g, b, l2, steps):
    for attempt in range(INNER):
        if cs is None:
            cs = trig(x)
        grad = energy_grad(x, cs, f, t, ft, g, b, l2)
        x = tuple(
            jnp.where(attempt < steps, xi - jnp.clip(STEP_SIZE * gi, -RADIUS, RADIUS), xi)
            for xi, gi in zip(x, grad)
        )
        cs, f = None, None
    return x


def advance(carry, near, far, prm):
    g, b, lim, steps = prm
    ends = (near[0], near[1], far[0], far[1])
    prices = (near[2], near[3], far[2], far[3])
    if carry is None:
        copies = ends
        cs = trig(copies)
        flow_prev = flows(copies, cs, g, b)
        volt = tuple(jnp.zeros_like(e) for e in ends)
        target = ends
        flow_target = flow_prev
        dual_flow = volt
    else:
        copies, flow_prev, cs = carry
        volt = tuple(c - e for c, e in zip(copies, ends))
        target = tuple(e - v for e, v in zip(ends, volt))
        flow_target = tuple(f + 2.0 * q for f, q in zip(flow_prev, prices))
        dual_flow = tuple(-q for q in prices)
    copies = solve(copies, cs, flow_prev, target, flow_target, g, b, lim * lim, steps)
    cs = trig(copies)
    flow_prev = flows(copies, cs, g, b)
    side_from = rows(
        copies[0] + volt[0], copies[1] + volt[1], flow_prev[0] + dual_flow[0], flow_prev[1] + dual_flow[1]
    )
    side_to = rows(
        copies[2] + volt[2], copies[3] + volt[3], flow_prev[2] + dual_flow[2], flow_prev[3] + dual_flow[3]
    )
    return (copies, flow_prev, cs), side_from, side_to


def store_carry(ref, carry):
    for i in range(4):
        ref[i] = carry[0][i]
        ref[4 + i] = carry[1][i]
    ref[8] = carry[2][0]
    ref[9] = carry[2][1]


def load_carry(ref):
    return (tuple(ref[i] for i in range(4)), tuple(ref[4 + i] for i in range(4)), (ref[8], ref[9]))


def split4(a, n):
    return tuple(a[i * n:(i + 1) * n] for i in range(4))


def vmem_call(kernel, outs, *args, scratch=()):
    return pl.pallas_call(
        kernel,
        out_shape=outs,
        in_specs=[pl.BlockSpec(memory_space=pltpu.VMEM)] * len(args),
        out_specs=tuple(pl.BlockSpec(memory_space=pltpu.VMEM) for _ in outs),
        scratch_shapes=scratch,
        compiler_params=pltpu.CompilerParams(vmem_limit_bytes=48 * 1024 * 1024),
    )(*args)


def on_device(
    warm_mag, warm_angle, load_real, load_react, start_real, start_react,
    gen_bus, gen_linear, gen_quad, gen_ramp, gen_cap_real, gen_cap_react,
    branch_from, branch_to, branch_cond, branch_susc, branch_limit, branch_steps,
    cut_near, cut_peer, cut_bus, cut_cond, cut_susc, cut_limit, cut_steps,
):
    periods, scen, buses = warm_mag.shape
    nrow = periods * scen
    cuts = cut_near.shape[0]
    parts = lax.axis_size("net")
    cap = max(2, cuts // parts * 2)
    slots = parts * cap
    gens = gen_bus.shape[0]
    ntm = lax.axis_size("tm")
    horizon = periods * ntm

    def row(v):
        return v.reshape(1, -1)

    wm = warm_mag.reshape(nrow, buses)
    wa = warm_angle.reshape(nrow, buses)
    lr = load_real.reshape(nrow, buses)
    lq = load_react.reshape(nrow, buses)
    sr = start_real.reshape(nrow, gens)
    sq = start_react.reshape(nrow, gens)
    halo = 2 * scen
    lo = lax.ppermute(sr[nrow - halo:], "tm", [(i, i + 1) for i in range(ntm - 1)])
    hi = lax.ppermute(sr[:halo], "tm", [(i + 1, i) for i in range(ntm - 1)])
    window = nrow + 2 * scen
    period_ext = (
        lax.axis_index("tm") * periods - 1 + jnp.arange(window, dtype=jnp.int32) // scen
    ).reshape(window, 1)
    gen_rows = (row(gen_bus), row(gen_linear), row(gen_quad), row(gen_ramp), row(gen_cap_real), row(gen_cap_react))
    br_rows = (row(branch_from), row(branch_to), row(branch_cond), row(branch_susc), row(branch_limit),
               row(branch_steps.astype(F32)))
    cut_rows = (row(cut_near), row(cut_cond), row(cut_susc), row(cut_limit), row(cut_steps.astype(F32)))
    cut_bus_row = row(cut_bus.astype(F32))
    nvals0 = 128

    def prep_kernel(peer_hbm, near_hbm, bus_hbm, cond_hbm, susc_hbm, lim_hbm, steps_hbm, wm_hbm, wa_hbm,
                    slot_out, pay_out,
                    peer_ref, near_ref, bus_ref, cond_ref, susc_ref, lim_ref, steps_ref, wm_ref, wa_ref, sems):
        pairs = ((peer_hbm, peer_ref), (near_hbm, near_ref), (bus_hbm, bus_ref), (cond_hbm, cond_ref),
                 (susc_hbm, susc_ref), (lim_hbm, lim_ref), (steps_hbm, steps_ref), (wm_hbm, wm_ref),
                 (wa_hbm, wa_ref))
        copies = [pltpu.make_async_copy(src, dst, sems.at[i]) for i, (src, dst) in enumerate(pairs)]
        for cp in copies:
            cp.start()
        copies[0].wait()
        peer = peer_ref[...]
        mine_t = (lax.broadcasted_iota(jnp.int32, (parts, cuts), 0) == peer).astype(F32)
        same = dot(mine_t.T.astype(BF), mine_t.astype(BF), NN)
        earlier = lax.broadcasted_iota(jnp.int32, (cuts, cuts), 0) < lax.broadcasted_iota(jnp.int32, (cuts, cuts), 1)
        rank = jnp.sum(jnp.where(earlier, same, 0.0), axis=0, keepdims=True)
        position = peer.astype(F32) * cap + rank
        slot_t = (lax.broadcasted_iota(jnp.int32, (slots, cuts), 0).astype(F32) == position).astype(F32).T
        slot_b = slot_t.astype(BF)
        slot_out[...] = slot_t
        copies[1].wait()
        inc_near = onehot(near_ref[...], buses)
        by_slot = dot(inc_near, slot_b, NN).astype(BF)
        for cp in copies[2:]:
            cp.wait()
        prm = rows(bus_ref[...].astype(F32) + 1.0, cond_ref[...], susc_ref[...], lim_ref[...],
                   steps_ref[...].astype(F32), jnp.zeros((3, cuts), F32))
        vals = rows(
            take(prm, slot_b),
            take(rows(wm_ref[...], wa_ref[...]), by_slot),
            jnp.zeros((nvals0 - 8 - 2 * nrow, slots), F32),
        )
        pay_out[...] = vals.T

    prep_args = (row(cut_peer), cut_rows[0], row(cut_bus), cut_rows[1], cut_rows[2], cut_rows[3], row(cut_steps),
                 wm, wa)
    slot_t, pay_setup = pl.pallas_call(
        prep_kernel,
        out_shape=(jax.ShapeDtypeStruct((cuts, slots), F32), jax.ShapeDtypeStruct((slots, nvals0), F32)),
        in_specs=[pl.BlockSpec(memory_space=pl.ANY)] * len(prep_args),
        out_specs=(pl.BlockSpec(memory_space=pltpu.VMEM), pl.BlockSpec(memory_space=pltpu.VMEM)),
        scratch_shapes=[pltpu.VMEM(a.shape, a.dtype) for a in prep_args] + [pltpu.SemaphoreType.DMA((len(prep_args),))],
    )(*prep_args)
    recv_setup = lax.all_to_all(pay_setup, "net", 0, 0, tiled=True)

    def mid_kernel(recv_ref, wm_ref, wa_ref, pay_out):
        ids = recv_ref[:, 0:1].astype(jnp.int32) - 1
        inc_t = (ids == lax.broadcasted_iota(jnp.int32, (slots, buses), 1)).astype(BF)
        warm = rows(wm_ref[...], wa_ref[...], jnp.zeros((nvals0 - 2 * nrow, buses), F32))
        pay_out[...] = give_left(inc_t, warm)

    pay_0 = vmem_call(
        mid_kernel, (jax.ShapeDtypeStruct((slots, nvals0), F32),), recv_setup, wm, wa,
    )[0]
    recv_0 = lax.all_to_all(pay_0, "net", 0, 0, tiled=True)

    def spread(p):
        return (lax.broadcasted_iota(jnp.int32, (3 * slots, slots), 0)
                == 3 * lax.broadcasted_iota(jnp.int32, (3 * slots, slots), 1) + p).astype(BF)

    def local_part(first, refs):
        if first:
            (wm_ref, wa_ref, bf_ref, bt_ref, bc_ref, bs_ref, bl_ref, bn_ref,
             gb_ref, gl_ref, gq_ref, gr_ref, gcr_ref, gcq_ref, pe_ref,
             sr_lo_ref, sr_ref, sr_hi_ref, sq_ref,
             tot_out, sup_out, ci_out, g0_out, gq0_out) = refs
            zero_b = jnp.zeros((nrow, buses), F32)
            state = (wm_ref[...], wa_ref[...], zero_b, zero_b)
            carry_in = None
        else:
            (st_ref, bf_ref, bt_ref, bc_ref, bs_ref, bl_ref, bn_ref,
             gb_ref, gl_ref, gq_ref, gr_ref, gcr_ref, gcq_ref, pe_ref,
             ci_ref, g0_ref, gq0_ref, cp_ref, mir_ref,
             tot_out, sup_out, gr_out, gq_out, pn_out, prc_out) = refs
            state = tuple(st_ref[i] for i in range(4))
            carry_in = load_carry(ci_ref)
        inc_from = onehot(bf_ref[...], buses)
        inc_to = onehot(bt_ref[...], buses)
        inc_gen = onehot(gb_ref[...], buses)
        stack = split3(rows(*state))
        pick_from = split4(take_split(stack, inc_from), nrow)
        pick_to = split4(take_split(stack, inc_to), nrow)
        if not first:
            pn_out[...] = take_split(stack, onehot(cp_ref[0:1].astype(jnp.int32), buses))
            prc_out[...] = take_split(stack, onehot(mir_ref[0:1].astype(jnp.int32) - 1, buses))
        prm_in = (bc_ref[...], bs_ref[...], bl_ref[...], bn_ref[...])
        carry_i, fi, ti = advance(carry_in, pick_from, pick_to, prm_in)
        totals = give(fi, inc_from) + give(ti, inc_to)
        for i in range(4):
            tot_out[i] = totals[i * nrow:(i + 1) * nrow]
        lin, quad, ramp, capr, capq = gl_ref[...], gq_ref[...], gr_ref[...], gcr_ref[...], gcq_ref[...]
        per = pe_ref[...]
        nb = (per > 0).astype(F32) + (per < horizon - 1).astype(F32)
        denom = 2.0 * quad + 1.0 + ramp * nb
        if first:
            ext = rows(sr_lo_ref[...], sr_ref[...], sr_hi_ref[...])
            g0 = jnp.clip((ext[scen:scen + window] - lin + ramp * (ext[0:window] + ext[2 * scen:2 * scen + window]))
                          / denom, 0.0, capr)
            g0 = jnp.where((per >= 0) & (per < horizon), g0, 0.0)
            gen_real = g0[scen:scen + nrow]
            gen_react = jnp.clip(sq_ref[...], -capq, capq)
            supply = give(rows(gen_real, gen_react), inc_gen)
            store_carry(ci_out, carry_i)
            g0_out[...] = g0
            gq0_out[...] = gen_react
        else:
            g0 = g0_ref[...]
            gp = take(rows(state[2], state[3]), inc_gen)
            gp_r, gp_q = gp[0:nrow], gp[nrow:]
            gen_real = jnp.clip(
                (g0[scen:scen + nrow] - 2.0 * gp_r - lin + ramp * (g0[0:nrow] + g0[2 * scen:2 * scen + nrow]))
                / denom[scen:scen + nrow],
                0.0,
                capr,
            )
            gen_react = jnp.clip(gq0_ref[...] - 2.0 * gp_q, -capq, capq)
            supply = give(rows(gen_real + gp_r, gen_react + gp_q), inc_gen)
            gr_out[...] = gen_real
            gq_out[...] = gen_react
        sup_out[0] = supply[0:nrow]
        sup_out[1] = supply[nrow:]

    def mirror0_kernel(recv_ref, wm_ref, wa_ref, bf_ref, bt_ref, cn_ref, gb_ref, tot_out, cm_out, dg_out, mir_out):
        mirror = recv_ref[...].T
        mir_out[...] = mirror
        inc_recv = onehot(mirror[0:1].astype(jnp.int32) - 1, buses)
        degree = (col_sum(onehot(bf_ref[...], buses)) + col_sum(onehot(bt_ref[...], buses))
                  + col_sum(onehot(cn_ref[...], buses)) + col_sum(inc_recv))
        dg_out[...] = rows(degree, col_sum(onehot(gb_ref[...], buses)), jnp.zeros((6, buses), F32))
        zm = jnp.zeros((nrow, slots), F32)
        zero_b = jnp.zeros((nrow, buses), F32)
        stack = rows(wm_ref[...], wa_ref[...], zero_b, zero_b)
        pick_recv = split4(take(stack, inc_recv), nrow)
        near_mirror = (mirror[8:8 + nrow], mirror[8 + nrow:8 + 2 * nrow], zm, zm)
        prm_mir = (mirror[1:2], mirror[2:3], mirror[3:4], mirror[4:5])
        carry_m, _, tmr = advance(None, near_mirror, pick_recv, prm_mir)
        totals = give(tmr, inc_recv)
        for i in range(4):
            tot_out[i] = totals[i * nrow:(i + 1) * nrow]
        store_carry(cm_out, carry_m)

    def cut_part(first, refs):
        (st_ref, wm_ref, wa_ref, lr_ref, lq_ref, recv_ref, mirror_ref, slot_ref,
         dg_ref, cp_ref, tin_ref, sup_ref, tm_ref) = refs[:13]
        rest = refs[13:]
        cprm_v = cp_ref[...]
        wmv, wav = wm_ref[...], wa_ref[...]
        slot_t = slot_ref[...].astype(BF)
        mirror = mirror_ref[...]
        inc_near = onehot(cprm_v[0:1].astype(jnp.int32), buses)
        inc_recv = onehot(mirror[0:1].astype(jnp.int32) - 1, buses)
        degree = dg_ref[0:1]
        gen_count = dg_ref[1:2]
        prm_cut = (cprm_v[1:2], cprm_v[2:3], cprm_v[3:4], cprm_v[4:5])
        if first:
            (cc_out, st_out, pay_out, plane_ref) = rest
            zero_b = jnp.zeros((nrow, buses), F32)
            state = (wmv, wav, zero_b, zero_b)
            far_slot = recv_ref[...].T
            zc = jnp.zeros((nrow, cuts), F32)
            hr = nrow // 2
            low = lax.broadcasted_iota(jnp.int32, (hr, 2 * cuts), 1) < cuts
            wide = lambda v: jnp.concatenate([v, v], axis=1)
            inc2 = onehot(wide(cprm_v[0:1]).astype(jnp.int32), buses)

            def pack(v):
                return jnp.where(low, v[:hr], v[hr:])

            far_c = give(rows(far_slot[0:nrow], far_slot[nrow:2 * nrow]), rows(slot_t, slot_t))
            zp = jnp.zeros((hr, 2 * cuts), F32)
            far_cross = (pack(far_c[0:nrow]), pack(far_c[nrow:]), zp, zp)
            warm_near = take(rows(wmv, wav), inc2)
            pick_near = (pack(warm_near[0:nrow]), pack(warm_near[nrow:]), zp, zp)
            carry_p, fc, _ = advance(None, pick_near, far_cross, tuple(wide(v) for v in prm_cut))
            t_low = give(jnp.where(rows(*(low,) * 4), fc, 0.0), inc2)
            t_high = give(jnp.where(rows(*(low,) * 4), 0.0, fc), inc2)
            cross_t = rows(*(x for i in range(4) for x in (t_low[i * hr:(i + 1) * hr], t_high[i * hr:(i + 1) * hr])))
            totals = tin_ref[...] + tm_ref[...] + cross_t.reshape(4, nrow, buses)
            flat = rows(*carry_p[0], *carry_p[1], *carry_p[2])
            lanes = lax.broadcasted_iota(jnp.int32, (2 * cuts, cuts), 0)
            cols = lax.broadcasted_iota(jnp.int32, (2 * cuts, cuts), 1)
            u_low = take(flat, (lanes == cols).astype(BF))
            u_high = take(flat, (lanes == cols + cuts).astype(BF))
            unp = [rows(u_low[a * hr:(a + 1) * hr], u_high[a * hr:(a + 1) * hr]) for a in range(10)]
            carry_c = (tuple(unp[0:4]), tuple(unp[4:8]), (unp[8], unp[9]))
        else:
            (cc_in_ref, cm_ref, pn_ref, prc_ref, mag_out, ang_out, pr_out, plane_ref) = rest
            state = tuple(st_ref[i] for i in range(4))
            blocks = []
            for p in range(3):
                for k in range(cap):
                    plane_ref[pl.ds(k, parts, stride=cap), :] = recv_ref[pl.ds(p * cap + k, parts, stride=3 * cap), :]
                blocks.append(plane_ref[...].T)
            both = rows(*blocks)
            near_mirror = split4(both[0:4 * nrow], nrow)
            far_cross = split4(give(both[4 * nrow:], slot_t), nrow)
            pick_near = split4(pn_ref[...], nrow)
            pick_recv = split4(prc_ref[...], nrow)
            carry_c_in = load_carry(cc_in_ref)
            carry_m_in = load_carry(cm_ref)
            _, fc, _ = advance(carry_c_in, pick_near, far_cross, prm_cut)
            prm_mir = (mirror[1:2], mirror[2:3], mirror[3:4], mirror[4:5])
            _, _, tmr = advance(carry_m_in, near_mirror, pick_recv, prm_mir)
            totals = tin_ref[...] + (give(fc, inc_near) + give(tmr, inc_recv)).reshape(4, nrow, buses)
        mag = (totals[0] + wmv) / (degree + 1.0)
        ang = (totals[1] + wav) / (degree + 1.0)
        weight = 1.0 + BALANCE_WEIGHT * (gen_count + degree)
        pr = BALANCE_WEIGHT * (sup_ref[0] - totals[2] - lr_ref[...]) / weight
        pq = BALANCE_WEIGHT * (sup_ref[1] - totals[3] - lq_ref[...]) / weight
        if first:
            store_carry(cc_out, carry_c)
            st_out[0] = mag
            st_out[1] = ang
            st_out[2] = pr
            st_out[3] = pq
            new_stack = split3(rows(mag, ang, pr, pq))
            near_slot = dot(inc_near, slot_t, NN).astype(BF)
            vals = rows(take_split(new_stack, near_slot), take_split(new_stack, inc_recv))
            for p in range(3):
                plane_ref[...] = vals[p * 128:(p + 1) * 128].T
                for k in range(cap):
                    pay_out[pl.ds(p * cap + k, parts, stride=3 * cap), :] = plane_ref[pl.ds(k, parts, stride=cap), :]
        else:
            mag_out[...] = mag
            ang_out[...] = ang
            pr_out[...] = pr

    sds = jax.ShapeDtypeStruct
    tot_shape = sds((4, nrow, buses), F32)
    br_all = br_rows
    gen_all = (*gen_rows, period_ext)
    tin0, sup0, ci1, g0, gq0 = vmem_call(
        lambda *refs: local_part(True, refs),
        (tot_shape, sds((2, nrow, buses), F32), sds((10, nrow, buses), F32), sds((window, gens), F32),
         sds((nrow, gens), F32)),
        wm, wa, *br_all, *gen_all, lo, sr, hi, sq,
    )
    tm0, cm1, dg, mirror_t = vmem_call(
        mirror0_kernel,
        (tot_shape, sds((10, nrow, slots), F32), sds((8, buses), F32), sds((nvals0, slots), F32)), recv_setup, wm, wa,
        br_rows[0], br_rows[1], cut_rows[0], gen_rows[0],
    )
    cprm = jnp.concatenate([cut_rows[0].astype(F32), *cut_rows[1:], jnp.zeros((3, cuts), F32)], axis=0)
    cc1, st1, pay_1 = vmem_call(
        lambda *refs: cut_part(True, refs),
        (sds((10, nrow, cuts), F32), tot_shape, sds((3 * slots, 128), F32)),
        wm, wm, wa, lr, lq, recv_0, mirror_t, slot_t, dg, cprm, tin0, sup0, tm0,
        scratch=[pltpu.VMEM((slots, 128), F32)],
    )
    recv_1 = lax.all_to_all(pay_1.reshape(3 * parts, 2, 128), "net", 0, 0, tiled=True).reshape(3 * slots, 128)
    tin1, sup1, gr, gq, pn1, prc1 = vmem_call(
        lambda *refs: local_part(False, refs),
        (tot_shape, sds((2, nrow, buses), F32), sds((nrow, gens), F32), sds((nrow, gens), F32),
         sds((4 * nrow, cuts), F32), sds((4 * nrow, slots), F32)),
        st1, *br_all, *gen_all, ci1, g0, gq0, cprm, mirror_t,
    )
    mag, ang, pr = vmem_call(
        lambda *refs: cut_part(False, refs),
        (sds((nrow, buses), F32), sds((nrow, buses), F32), sds((nrow, buses), F32)),
        st1, wm, wa, lr, lq, recv_1, mirror_t, slot_t, dg, cprm, tin1, sup1, tin1,
        cc1, cm1, pn1, prc1,
        scratch=[pltpu.VMEM((slots, 128), F32)],
    )
    shape_b = (periods, scen, buses)
    shape_g = (periods, scen, gens)
    return (mag.reshape(shape_b), ang.reshape(shape_b), pr.reshape(shape_b), gr.reshape(shape_g),
            gq.reshape(shape_g))


def solution(mesh):
    bus = P("tm", None, "net")
    one = P("net")
    return jax.shard_map(
        on_device,
        mesh=mesh,
        in_specs=(bus,) * 6 + (one,) * 12 + (one, P("net", None)) + (one,) * 5,
        out_specs=(bus,) * 5,
        check_vma=False,
    )
```
